32 devices in a mesh: gx: 4 (over y, x), gy: 8 (over z, core).
Axes of the slice: x: 2, y: 2, z: 4, core: 2. Of those that a mesh axis runs over, the one named last changes fastest.
Arguments:
- populations: float32 [64, 128, 19, 128], P('gx', 'gy'), may hold values from 0.001 to 0.9, as said below
Outputs:
- relaxed_populations: float32 [64, 128, 19, 128], P('gx', 'gy')
- picture: float32 [4, 128, 128], P(None, 'gy', 'gx')
The draws below stay inside these ranges and needn't reach their ends.
Inputs may be any that keep to these rules, and one draw needn't show every extreme that they name: `populations`: positive; near a local equilibrium of densities between 0.15 and 2.2 with drift of at most 0.08 a component.
All inputs are finite; a program needn't handle non-finite values.
Results may differ from the reference program's by a relative error of at most 0.0003.
Values sent between devices are 32-bit elements; how exact they have to be, the bound alone decides.
No kernel may reach another device: no remote copies, remote signals or barrier semaphores. Data moves between devices by JAX's collectives and lax.ppermute only.
A program may use at most 64 MiB of HBM per device.

```python
import math
import jax
import jax.numpy as jnp
import numpy as np
from jax import lax

NX = 64
NY = 128
NZ = 128


def draw_populations(key, part):
    subkeys = jax.random.split(key, 3)
    extent = (NX, NY, NZ)
    density = jnp.exp(jax.random.uniform(subkeys[0], extent, jnp.float32, math.log(0.15), math.log(2.2)))
    drift = jnp.clip(0.04 * jax.random.normal(subkeys[1], (3,) + extent, jnp.float32), -0.08, 0.08)
    jitter = jax.random.uniform(subkeys[2], (NX, NY, 19, NZ), jnp.float32, 0.85, 1.15)
    velocities = [[0, 0, 0], [1, 0, 0], [-1, 0, 0], [0, 1, 0], [0, -1, 0], [0, 0, 1], [0, 0, -1], [1, 1, 0], [-1, -1, 0], [1, -1, 0], [-1, 1, 0], [1, 0, 1], [-1, 0, -1], [1, 0, -1], [-1, 0, 1], [0, 1, 1], [0, -1, -1], [0, 1, -1], [0, -1, 1]]
    weights = [1.0 / 3.0] + [1.0 / 18.0] * 6 + [1.0 / 36.0] * 12
    speed_squared = drift[0] * drift[0] + drift[1] * drift[1] + drift[2] * drift[2]
    columns = []
    for q in range(19):
        along = velocities[q][0] * drift[0] + velocities[q][1] * drift[1] + velocities[q][2] * drift[2]
        columns.append(weights[q] * density * (1.0 + 3.0 * along + 4.5 * along * along - 1.5 * speed_squared))
    return jnp.stack(columns, axis=2) * jitter


def setup_inputs(seed: int = 0) -> dict:
    keys = jax.random.split(jax.random.key(seed), 2)
    populations = draw_populations(jax.random.fold_in(keys[1], 71), 0)
    return dict(populations=populations)


cohesion = -6.0
optical = 2.0


def lattice_tables():
    velocities = np.array([[0, 0, 0], [1, 0, 0], [-1, 0, 0], [0, 1, 0], [0, -1, 0], [0, 0, 1], [0, 0, -1],
                           [1, 1, 0], [-1, -1, 0], [1, -1, 0], [-1, 1, 0],
                           [1, 0, 1], [-1, 0, -1], [1, 0, -1], [-1, 0, 1],
                           [0, 1, 1], [0, -1, -1], [0, 1, -1], [0, -1, 1]])
    weights = np.array([1.0 / 3.0] + [1.0 / 18.0] * 6 + [1.0 / 36.0] * 12)
    along_x = velocities[:, 0] * 1.0
    along_y = velocities[:, 1] * 1.0
    along_z = velocities[:, 2] * 1.0
    squared = along_x * along_x + along_y * along_y + along_z * along_z
    moment_rows = [np.ones(19), 19.0 * squared - 30.0, (21.0 * squared * squared - 53.0 * squared + 24.0) / 2.0,
                   along_x, (5.0 * squared - 9.0) * along_x, along_y, (5.0 * squared - 9.0) * along_y,
                   along_z, (5.0 * squared - 9.0) * along_z,
                   3.0 * along_x * along_x - squared, (3.0 * squared - 5.0) * (3.0 * along_x * along_x - squared),
                   along_y * along_y - along_z * along_z,
                   (3.0 * squared - 5.0) * (along_y * along_y - along_z * along_z),
                   along_x * along_y, along_y * along_z, along_x * along_z,
                   (along_y * along_y - along_z * along_z) * along_x,
                   (along_z * along_z - along_x * along_x) * along_y,
                   (along_x * along_x - along_y * along_y) * along_z]
    moments = np.stack(moment_rows)
    inverse = moments.T / np.sum(moments * moments, axis=1)
    relax_rates = np.array([0.0, 1.19, 1.4, 0.0, 1.2, 0.0, 1.2, 0.0, 1.2, 1.0, 1.4, 1.0, 1.4, 1.0, 1.0, 1.0, 1.98, 1.98, 1.98])
    relaxing = inverse @ (relax_rates[:, None] * moments)
    forcing_map = inverse @ ((1.0 - 0.5 * relax_rates)[:, None] * moments)
    return velocities, weights, relaxing, forcing_map


def collide(populations, density, forcing, velocities, weights, relaxing, forcing_map):
    lattice = jnp.asarray(velocities, dtype=jnp.float32)
    spread = jnp.asarray(weights, dtype=jnp.float32)[None, None, :, None]
    relax_table = jnp.asarray(relaxing, dtype=jnp.float32)
    source_table = jnp.asarray(forcing_map, dtype=jnp.float32)
    momentum = jnp.einsum("qd,xyqz->dxyz", lattice, populations, precision=lax.Precision.HIGHEST)
    drift = (momentum + 0.5 * forcing) / density[None]
    along = jnp.einsum("qd,dxyz->xyqz", lattice, drift, precision=lax.Precision.HIGHEST)
    pushed = jnp.einsum("qd,dxyz->xyqz", lattice, forcing, precision=lax.Precision.HIGHEST)
    speed_squared = jnp.sum(drift * drift, axis=0)[:, :, None, :]
    work_done = jnp.sum(drift * forcing, axis=0)[:, :, None, :]
    balance = spread * density[:, :, None, :] * (1.0 + 3.0 * along + 4.5 * along * along - 1.5 * speed_squared)
    guo_term = spread * (3.0 * (pushed - work_done) + 9.0 * along * pushed)
    relaxed = jnp.einsum("pq,xyqz->xypz", relax_table, populations - balance, precision=lax.Precision.HIGHEST)
    sourced = jnp.einsum("pq,xyqz->xypz", source_table, guo_term, precision=lax.Precision.HIGHEST)
    return populations - relaxed + sourced


def palette(density):
    reds = density / (1.0 + density)
    greens = jnp.exp(-density)
    blues = 0.5 * (1.0 + jnp.tanh(2.0 * (density - 1.0)))
    return reds, greens, blues


def reference(populations):
    velocities, weights, relaxing, forcing_map = lattice_tables()
    length_x = populations.shape[0]
    density = jnp.sum(populations, axis=2)
    potential = 1.0 - jnp.exp(-density)
    totals = [jnp.zeros_like(potential), jnp.zeros_like(potential), jnp.zeros_like(potential)]
    for q in range(1, 19):
        steps = [int(v) for v in velocities[q]]
        neighbour = jnp.roll(potential, (-steps[0], -steps[1], -steps[2]), axis=(0, 1, 2))
        for d in range(3):
            if steps[d] != 0:
                totals[d] = totals[d] + (weights[q] * steps[d]) * neighbour
    forcing = jnp.stack([-cohesion * potential * totals[d] for d in range(3)])

    def collide_layer(position):
        layer_pops = lax.dynamic_index_in_dim(populations, position, 0, keepdims=True)
        layer_density = lax.dynamic_index_in_dim(density, position, 0, keepdims=True)
        layer_forcing = lax.dynamic_index_in_dim(forcing, position, 1, keepdims=True)
        return collide(layer_pops, layer_density, layer_forcing, velocities, weights, relaxing, forcing_map)[0]

    positions = jnp.arange(length_x, dtype=jnp.int32)
    collided = lax.map(collide_layer, positions)

    def pull_layer(position):
        columns = []
        for q in range(19):
            steps = [int(v) for v in velocities[q]]
            anchor = (position - steps[0]) % length_x
            taken = lax.dynamic_index_in_dim(collided, anchor, 0, keepdims=False)[:, q, :]
            columns.append(jnp.roll(taken, (steps[1], steps[2]), axis=(0, 1)))
        return jnp.stack(columns, axis=1)

    fresh = lax.map(pull_layer, positions)
    new_density = jnp.sum(fresh, axis=2)
    extinction = optical * new_density / length_x
    optical_depth = jnp.cumsum(extinction, axis=0) - extinction
    weight_map = jnp.exp(-optical_depth) * (1.0 - jnp.exp(-extinction))
    reds, greens, blues = palette(new_density)
    picture = jnp.stack([jnp.sum(weight_map * reds, axis=0), jnp.sum(weight_map * greens, axis=0),
                         jnp.sum(weight_map * blues, axis=0), 1.0 - jnp.exp(-jnp.sum(extinction, axis=0))])
    return fresh, picture
```

```python
import jax
import jax.numpy as jnp
import numpy as np
from jax import lax
from jax.sharding import PartitionSpec as P

cohesion = -6.0
optical = 2.0


def extended(cells, sides, width):
    for axis, dim in sides:
        count = lax.axis_size(axis)
        head = lax.slice_in_dim(cells, 0, width, axis=dim)
        tail = lax.slice_in_dim(cells, cells.shape[dim] - width, cells.shape[dim], axis=dim)
        cells = jnp.concatenate(
            [
                lax.ppermute(tail, axis, [(i, (i + 1) % count) for i in range(count)]),
                cells,
                lax.ppermute(head, axis, [((i + 1) % count, i) for i in range(count)]),
            ],
            axis=dim,
        )
    return cells


def from_partner(x, axis, distance):
    return lax.ppermute(x, axis, [(i, i ^ 1 << distance) for i in range(lax.axis_size(axis))])


def lattice_tables():
    velocities = np.array(
        [
            [0, 0, 0],
            [1, 0, 0],
            [-1, 0, 0],
            [0, 1, 0],
            [0, -1, 0],
            [0, 0, 1],
            [0, 0, -1],
            [1, 1, 0],
            [-1, -1, 0],
            [1, -1, 0],
            [-1, 1, 0],
            [1, 0, 1],
            [-1, 0, -1],
            [1, 0, -1],
            [-1, 0, 1],
            [0, 1, 1],
            [0, -1, -1],
            [0, 1, -1],
            [0, -1, 1],
        ]
    )
    weights = np.array([1.0 / 3.0] + [1.0 / 18.0] * 6 + [1.0 / 36.0] * 12)
    along_x = velocities[:, 0] * 1.0
    along_y = velocities[:, 1] * 1.0
    along_z = velocities[:, 2] * 1.0
    squared = along_x * along_x + along_y * along_y + along_z * along_z
    moment_rows = [
        np.ones(19),
        19.0 * squared - 30.0,
        (21.0 * squared * squared - 53.0 * squared + 24.0) / 2.0,
        along_x,
        (5.0 * squared - 9.0) * along_x,
        along_y,
        (5.0 * squared - 9.0) * along_y,
        along_z,
        (5.0 * squared - 9.0) * along_z,
        3.0 * along_x * along_x - squared,
        (3.0 * squared - 5.0) * (3.0 * along_x * along_x - squared),
        along_y * along_y - along_z * along_z,
        (3.0 * squared - 5.0) * (along_y * along_y - along_z * along_z),
        along_x * along_y,
        along_y * along_z,
        along_x * along_z,
        (along_y * along_y - along_z * along_z) * along_x,
        (along_z * along_z - along_x * along_x) * along_y,
        (along_x * along_x - along_y * along_y) * along_z,
    ]
    moments = np.stack(moment_rows)
    inverse = moments.T / np.sum(moments * moments, axis=1)
    relax_rates = np.array(
        [
            0.0,
            1.19,
            1.4,
            0.0,
            1.2,
            0.0,
            1.2,
            0.0,
            1.2,
            1.0,
            1.4,
            1.0,
            1.4,
            1.0,
            1.0,
            1.0,
            1.98,
            1.98,
            1.98,
        ]
    )
    relaxing = inverse @ (relax_rates[:, None] * moments)
    forcing_map = inverse @ ((1.0 - 0.5 * relax_rates)[:, None] * moments)
    return (velocities, weights, relaxing, forcing_map)


def collide(populations, density, forcing, velocities, weights, relaxing, forcing_map):
    lattice = jnp.asarray(velocities, dtype=jnp.float32)
    spread = jnp.asarray(weights, dtype=jnp.float32)[None, None, :, None]
    relax_table = jnp.asarray(relaxing, dtype=jnp.float32)
    source_table = jnp.asarray(forcing_map, dtype=jnp.float32)
    momentum = jnp.einsum("qd,xyqz->dxyz", lattice, populations, precision=lax.Precision.HIGHEST)
    drift = (momentum + 0.5 * forcing) / density[None]
    along = jnp.einsum("qd,dxyz->xyqz", lattice, drift, precision=lax.Precision.HIGHEST)
    pushed = jnp.einsum("qd,dxyz->xyqz", lattice, forcing, precision=lax.Precision.HIGHEST)
    speed_squared = jnp.sum(drift * drift, axis=0)[:, :, None, :]
    work_done = jnp.sum(drift * forcing, axis=0)[:, :, None, :]
    balance = (
        spread
        * density[:, :, None, :]
        * (1.0 + 3.0 * along + 4.5 * along * along - 1.5 * speed_squared)
    )
    guo_term = spread * (3.0 * (pushed - work_done) + 9.0 * along * pushed)
    relaxed = jnp.einsum(
        "pq,xyqz->xypz", relax_table, populations - balance, precision=lax.Precision.HIGHEST
    )
    sourced = jnp.einsum("pq,xyqz->xypz", source_table, guo_term, precision=lax.Precision.HIGHEST)
    return populations - relaxed + sourced


def attraction(padded, offset, extent_x, extent_y, velocities, weights):
    centre = padded[offset : offset + extent_x, offset : offset + extent_y]
    totals = [jnp.zeros_like(centre), jnp.zeros_like(centre), jnp.zeros_like(centre)]
    for q in range(1, 19):
        steps = [int(v) for v in velocities[q]]
        start_x = offset + steps[0]
        start_y = offset + steps[1]
        neighbour = padded[start_x : start_x + extent_x, start_y : start_y + extent_y]
        neighbour = jnp.roll(neighbour, -steps[2], axis=2)
        for d in range(3):
            if steps[d] != 0:
                totals[d] = totals[d] + weights[q] * steps[d] * neighbour
    return jnp.stack([-cohesion * centre * totals[d] for d in range(3)])


def palette(density):
    reds = density / (1.0 + density)
    greens = jnp.exp(-density)
    blues = 0.5 * (1.0 + jnp.tanh(2.0 * (density - 1.0)))
    return (reds, greens, blues)


SIDES = [(-1, -1), (-1, 0), (-1, 1), (0, -1), (0, 1), (1, -1), (1, 0), (1, 1)]


def from_side(slab, side):
    sx, sy = side
    nx = lax.axis_size("gx")
    ny = lax.axis_size("gy")
    if sx == 0:
        return lax.ppermute(slab, "gy", [(j, (j - sy) % ny) for j in range(ny)])
    if sy == 0:
        return lax.ppermute(slab, "gx", [(i, (i - sx) % nx) for i in range(nx)])
    pairs = []
    for i in range(nx):
        for j in range(ny):
            pairs.append((i * ny + j, ((i - sx) % nx) * ny + (j - sy) % ny))
    return lax.ppermute(slab, ("gx", "gy"), pairs)


def side_range(s, n):
    if s == -1:
        return slice(n - 1, n)
    if s == 1:
        return slice(0, 1)
    return slice(0, n)


def exchange(cells, extent_x, extent_y):
    got = {}
    for side in SIDES:
        slab = cells[side_range(side[0], extent_x), side_range(side[1], extent_y)]
        got[side] = from_side(slab, side)
    return got


def padded_from(centre, got):
    rows = []
    for sx in (-1, 0, 1):
        parts = []
        for sy in (-1, 0, 1):
            parts.append(centre if (sx, sy) == (0, 0) else got[(sx, sy)])
        rows.append(jnp.concatenate(parts, axis=1))
    return jnp.concatenate(rows, axis=0)


def body(populations):
    velocities, weights, relaxing, forcing_map = lattice_tables()
    extent_x = populations.shape[0]
    extent_y = populations.shape[1]
    density = jnp.sum(populations, axis=2)
    potential = 1.0 - jnp.exp(-density)
    padded = padded_from(potential, exchange(potential, extent_x, extent_y))
    forcing = attraction(padded, 1, extent_x, extent_y, velocities, weights)
    collided = collide(populations, density, forcing, velocities, weights, relaxing, forcing_map)
    wanted = {}
    got = {}
    for side in SIDES:
        sx, sy = side
        qs = [
            q
            for q in range(19)
            if (sx == 0 or velocities[q][0] == -sx) and (sy == 0 or velocities[q][1] == -sy)
        ]
        wanted[side] = qs
        slab = collided[side_range(sx, extent_x), side_range(sy, extent_y)][:, :, np.array(qs)]
        got[side] = from_side(slab, side)
    read = []
    for q in range(19):
        cx, cy, cz = [int(v) for v in velocities[q]]
        column = collided[:, :, q]
        if (cx, cy) != (0, 0):
            pieces = {}
            for side in SIDES:
                if q in wanted[side]:
                    pieces[side] = got[side][:, :, wanted[side].index(q)]
                else:
                    shape = (
                        1 if side[0] else extent_x,
                        1 if side[1] else extent_y,
                        column.shape[2],
                    )
                    pieces[side] = jnp.zeros(shape, column.dtype)
            whole = padded_from(column, pieces)
            column = whole[1 - cx : 1 - cx + extent_x, 1 - cy : 1 - cy + extent_y]
        read.append(jnp.roll(column, cz, axis=2))
    fresh = jnp.stack(read, axis=2)
    groups = lax.axis_size("gx")
    length_x = extent_x * groups
    new_density = jnp.sum(fresh, axis=2)
    extinction = optical * new_density / length_x
    optical_depth = jnp.cumsum(extinction, axis=0) - extinction
    weight_map = jnp.exp(-optical_depth) * (1.0 - jnp.exp(-extinction))
    reds, greens, blues = palette(new_density)
    layered = jnp.stack(
        [
            jnp.sum(weight_map * reds, axis=0),
            jnp.sum(weight_map * greens, axis=0),
            jnp.sum(weight_map * blues, axis=0),
            1.0 - jnp.exp(-jnp.sum(extinction, axis=0)),
        ]
    )
    depth_z = layered.shape[2]
    block_len = depth_z // groups
    blocked = layered.reshape(4, extent_y, groups, block_len)
    position = lax.axis_index("gx")
    own = lax.dynamic_index_in_dim(blocked, position, 2, keepdims=False)
    parts = [None] * groups
    for shift in range(groups):
        if shift == 0:
            continue
        target = (position + shift) % groups
        outgoing = lax.dynamic_index_in_dim(blocked, target, 2, keepdims=False)
        incoming = lax.ppermute(outgoing, "gx", [(i, (i + shift) % groups) for i in range(groups)])
        parts[shift] = incoming
    total = None
    for source in range(groups):
        shift = (position - source) % groups
        piece = own
        for s in range(1, groups):
            piece = jnp.where(shift == s, parts[s], piece)
        total = piece if total is None else total + (1.0 - total[3:4]) * piece
    picture = total
    return (fresh, picture)


def solution(mesh):
    placed = (P("gx", "gy", None, None),)
    return jax.shard_map(
        body,
        mesh=mesh,
        in_specs=placed,
        out_specs=(P("gx", "gy", None, None), P(None, "gy", "gx")),
        check_vma=False,
    )
```

```python
import jax
import jax.numpy as jnp
import numpy as np
from jax import lax
from jax.sharding import PartitionSpec as P

cohesion = -6.0
optical = 2.0


def extended(cells, sides, width):
    for axis, dim in sides:
        count = lax.axis_size(axis)
        head = lax.slice_in_dim(cells, 0, width, axis=dim)
        tail = lax.slice_in_dim(cells, cells.shape[dim] - width, cells.shape[dim], axis=dim)
        cells = jnp.concatenate(
            [
                lax.ppermute(tail, axis, [(i, (i + 1) % count) for i in range(count)]),
                cells,
                lax.ppermute(head, axis, [((i + 1) % count, i) for i in range(count)]),
            ],
            axis=dim,
        )
    return cells


def from_partner(x, axis, distance):
    return lax.ppermute(x, axis, [(i, i ^ 1 << distance) for i in range(lax.axis_size(axis))])


def lattice_tables():
    velocities = np.array(
        [
            [0, 0, 0],
            [1, 0, 0],
            [-1, 0, 0],
            [0, 1, 0],
            [0, -1, 0],
            [0, 0, 1],
            [0, 0, -1],
            [1, 1, 0],
            [-1, -1, 0],
            [1, -1, 0],
            [-1, 1, 0],
            [1, 0, 1],
            [-1, 0, -1],
            [1, 0, -1],
            [-1, 0, 1],
            [0, 1, 1],
            [0, -1, -1],
            [0, 1, -1],
            [0, -1, 1],
        ]
    )
    weights = np.array([1.0 / 3.0] + [1.0 / 18.0] * 6 + [1.0 / 36.0] * 12)
    along_x = velocities[:, 0] * 1.0
    along_y = velocities[:, 1] * 1.0
    along_z = velocities[:, 2] * 1.0
    squared = along_x * along_x + along_y * along_y + along_z * along_z
    moment_rows = [
        np.ones(19),
        19.0 * squared - 30.0,
        (21.0 * squared * squared - 53.0 * squared + 24.0) / 2.0,
        along_x,
        (5.0 * squared - 9.0) * along_x,
        along_y,
        (5.0 * squared - 9.0) * along_y,
        along_z,
        (5.0 * squared - 9.0) * along_z,
        3.0 * along_x * along_x - squared,
        (3.0 * squared - 5.0) * (3.0 * along_x * along_x - squared),
        along_y * along_y - along_z * along_z,
        (3.0 * squared - 5.0) * (along_y * along_y - along_z * along_z),
        along_x * along_y,
        along_y * along_z,
        along_x * along_z,
        (along_y * along_y - along_z * along_z) * along_x,
        (along_z * along_z - along_x * along_x) * along_y,
        (along_x * along_x - along_y * along_y) * along_z,
    ]
    moments = np.stack(moment_rows)
    inverse = moments.T / np.sum(moments * moments, axis=1)
    relax_rates = np.array(
        [
            0.0,
            1.19,
            1.4,
            0.0,
            1.2,
            0.0,
            1.2,
            0.0,
            1.2,
            1.0,
            1.4,
            1.0,
            1.4,
            1.0,
            1.0,
            1.0,
            1.98,
            1.98,
            1.98,
        ]
    )
    relaxing = inverse @ (relax_rates[:, None] * moments)
    forcing_map = inverse @ ((1.0 - 0.5 * relax_rates)[:, None] * moments)
    return (velocities, weights, relaxing, forcing_map)


def collide(populations, density, forcing, velocities, weights, relaxing, forcing_map):
    lattice = jnp.asarray(velocities, dtype=jnp.float32)
    spread = jnp.asarray(weights, dtype=jnp.float32)[None, None, :, None]
    relax_table = jnp.asarray(relaxing, dtype=jnp.float32)
    source_table = jnp.asarray(forcing_map, dtype=jnp.float32)
    momentum = jnp.einsum("qd,xyqz->dxyz", lattice, populations, precision=lax.Precision.HIGHEST)
    drift = (momentum + 0.5 * forcing) / density[None]
    along = jnp.einsum("qd,dxyz->xyqz", lattice, drift, precision=lax.Precision.HIGHEST)
    pushed = jnp.einsum("qd,dxyz->xyqz", lattice, forcing, precision=lax.Precision.HIGHEST)
    speed_squared = jnp.sum(drift * drift, axis=0)[:, :, None, :]
    work_done = jnp.sum(drift * forcing, axis=0)[:, :, None, :]
    balance = (
        spread
        * density[:, :, None, :]
        * (1.0 + 3.0 * along + 4.5 * along * along - 1.5 * speed_squared)
    )
    guo_term = spread * (3.0 * (pushed - work_done) + 9.0 * along * pushed)
    relaxed = jnp.einsum(
        "pq,xyqz->xypz", relax_table, populations - balance, precision=lax.Precision.HIGHEST
    )
    sourced = jnp.einsum("pq,xyqz->xypz", source_table, guo_term, precision=lax.Precision.HIGHEST)
    return populations - relaxed + sourced


def attraction(padded, offset, extent_x, extent_y, velocities, weights):
    centre = padded[offset : offset + extent_x, offset : offset + extent_y]
    totals = [jnp.zeros_like(centre), jnp.zeros_like(centre), jnp.zeros_like(centre)]
    for q in range(1, 19):
        steps = [int(v) for v in velocities[q]]
        start_x = offset + steps[0]
        start_y = offset + steps[1]
        neighbour = padded[start_x : start_x + extent_x, start_y : start_y + extent_y]
        neighbour = jnp.roll(neighbour, -steps[2], axis=2)
        for d in range(3):
            if steps[d] != 0:
                totals[d] = totals[d] + weights[q] * steps[d] * neighbour
    return jnp.stack([-cohesion * centre * totals[d] for d in range(3)])


def palette(density):
    reds = density / (1.0 + density)
    greens = jnp.exp(-density)
    blues = 0.5 * (1.0 + jnp.tanh(2.0 * (density - 1.0)))
    return (reds, greens, blues)


def shift_ring(x, axis, step):
    count = lax.axis_size(axis)
    return lax.ppermute(x, axis, [(i, (i - step) % count) for i in range(count)])


def collide_major(f, rho, force, velocities, weights, relaxing, forcing_map):
    lattice = velocities.astype(np.float32)
    extra = (1,) * rho.ndim
    cx = jnp.asarray(lattice[:, 0]).reshape((19,) + extra)
    cy = jnp.asarray(lattice[:, 1]).reshape((19,) + extra)
    cz = jnp.asarray(lattice[:, 2]).reshape((19,) + extra)
    spread = jnp.asarray(weights.astype(np.float32)).reshape((19,) + extra)
    momentum = [
        sum(f[q] * float(velocities[q][d]) for q in range(19) if velocities[q][d] != 0)
        for d in range(3)
    ]
    drift = [(momentum[d] + 0.5 * force[d]) / rho for d in range(3)]
    along = cx * drift[0] + cy * drift[1] + cz * drift[2]
    pushed = cx * force[0] + cy * force[1] + cz * force[2]
    speed_squared = drift[0] * drift[0] + drift[1] * drift[1] + drift[2] * drift[2]
    work_done = drift[0] * force[0] + drift[1] * force[1] + drift[2] * force[2]
    balance = spread * rho * (1.0 + 3.0 * along + 4.5 * along * along - 1.5 * speed_squared)
    guo_term = spread * (3.0 * (pushed - work_done) + 9.0 * along * pushed)
    relax_table = jnp.asarray(relaxing, dtype=jnp.float32)
    source_table = jnp.asarray(forcing_map, dtype=jnp.float32)
    relaxed = jnp.einsum("pq,q...->p...", relax_table, f - balance, precision=lax.Precision.HIGHEST)
    sourced = jnp.einsum("pq,q...->p...", source_table, guo_term, precision=lax.Precision.HIGHEST)
    return f - relaxed + sourced


def body(populations):
    velocities, weights, relaxing, forcing_map = lattice_tables()
    extent_x = populations.shape[0]
    extent_y = populations.shape[1]
    f = jnp.transpose(populations, (2, 0, 1, 3))
    potential = 1.0 - jnp.exp(-jnp.sum(f, axis=0))
    to_next = jnp.concatenate([f[:, extent_x - 1], potential[extent_x - 1 : extent_x], potential[extent_x - 2 : extent_x - 1]])
    to_prev = jnp.concatenate([f[:, 0], potential[0:1], potential[1:2]])
    from_prev = shift_ring(to_next, "gx", -1)
    from_next = shift_ring(to_prev, "gx", 1)
    fx = jnp.concatenate([from_prev[None, :19].transpose(1, 0, 2, 3), f, from_next[None, :19].transpose(1, 0, 2, 3)], axis=1)
    px = jnp.concatenate([from_prev[20:21], from_prev[19:20], potential, from_next[19:20], from_next[20:21]], axis=0)
    zero_x = jnp.zeros((19, 1, fx.shape[3]), f.dtype)

    def y_message(row_pop, row_near, row_far):
        pops = jnp.concatenate([zero_x, fx[:, :, row_pop], zero_x], axis=1)
        return jnp.concatenate([pops, px[None, :, row_near], px[None, :, row_far]], axis=0)

    from_below = shift_ring(y_message(extent_y - 1, extent_y - 1, extent_y - 2), "gy", -1)
    from_above = shift_ring(y_message(0, 0, 1), "gy", 1)
    fxy = jnp.concatenate(
        [from_below[:19, 1:-1, None], fx, from_above[:19, 1:-1, None]], axis=2
    )
    pxy = jnp.concatenate(
        [from_below[20][:, None], from_below[19][:, None], px, from_above[19][:, None], from_above[20][:, None]],
        axis=1,
    )
    ext_x = extent_x + 2
    ext_y = extent_y + 2
    centre = pxy[1 : 1 + ext_x, 1 : 1 + ext_y]
    totals = [jnp.zeros_like(centre), jnp.zeros_like(centre), jnp.zeros_like(centre)]
    for q in range(1, 19):
        steps = [int(v) for v in velocities[q]]
        neighbour = pxy[1 + steps[0] : 1 + steps[0] + ext_x, 1 + steps[1] : 1 + steps[1] + ext_y]
        neighbour = jnp.roll(neighbour, -steps[2], axis=2)
        for d in range(3):
            if steps[d] != 0:
                totals[d] = totals[d] + weights[q] * steps[d] * neighbour
    force = [-cohesion * centre * totals[d] for d in range(3)]
    rho = jnp.sum(fxy, axis=0)
    collided = collide_major(fxy, rho, force, velocities, weights, relaxing, forcing_map)
    read = []
    for q in range(19):
        cx, cy, cz = [int(v) for v in velocities[q]]
        column = collided[q, 1 - cx : 1 - cx + extent_x, 1 - cy : 1 - cy + extent_y]
        read.append(jnp.roll(column, cz, axis=2))
    fresh_major = jnp.stack(read, axis=0)
    fresh = jnp.transpose(fresh_major, (1, 2, 0, 3))
    groups = lax.axis_size("gx")
    length_x = extent_x * groups
    new_density = jnp.sum(fresh_major, axis=0)
    extinction = optical * new_density / length_x
    optical_depth = jnp.cumsum(extinction, axis=0) - extinction
    weight_map = jnp.exp(-optical_depth) * (1.0 - jnp.exp(-extinction))
    reds, greens, blues = palette(new_density)
    layered = jnp.stack(
        [
            jnp.sum(weight_map * reds, axis=0),
            jnp.sum(weight_map * greens, axis=0),
            jnp.sum(weight_map * blues, axis=0),
            1.0 - jnp.exp(-jnp.sum(extinction, axis=0)),
        ]
    )
    depth_z = layered.shape[2]
    block_len = depth_z // groups
    blocked = layered.reshape(4, extent_y, groups, block_len)
    position = lax.axis_index("gx")
    current = blocked
    for level in range(groups.bit_length() - 1):
        parity = position // (1 << level) % 2
        halves = current.shape[2] // 2
        paired = current.reshape(4, extent_y, halves, 2, block_len)
        lower = paired[:, :, :, 0]
        upper = paired[:, :, :, 1]
        kept = jnp.where(parity == 1, upper, lower)
        handed = jnp.where(parity == 1, lower, upper)
        partner = from_partner(handed, "gx", level)
        nearer = jnp.where(parity == 0, kept, partner)
        farther = jnp.where(parity == 0, partner, kept)
        current = nearer + (1.0 - nearer[3:4]) * farther
    picture = current.reshape(4, extent_y, block_len)
    return (fresh, picture)


def solution(mesh):
    placed = (P("gx", "gy", None, None),)
    return jax.shard_map(
        body,
        mesh=mesh,
        in_specs=placed,
        out_specs=(P("gx", "gy", None, None), P(None, "gy", "gx")),
        check_vma=False,
    )
```

```python
import jax
import jax.numpy as jnp
import numpy as np
from jax import lax
from jax.sharding import PartitionSpec as P
from jax.experimental import pallas as pl
from jax.experimental.pallas import tpu as pltpu

cohesion = -6.0
optical = 2.0


def extended(cells, sides, width):
    for axis, dim in sides:
        count = lax.axis_size(axis)
        head = lax.slice_in_dim(cells, 0, width, axis=dim)
        tail = lax.slice_in_dim(cells, cells.shape[dim] - width, cells.shape[dim], axis=dim)
        cells = jnp.concatenate(
            [
                lax.ppermute(tail, axis, [(i, (i + 1) % count) for i in range(count)]),
                cells,
                lax.ppermute(head, axis, [((i + 1) % count, i) for i in range(count)]),
            ],
            axis=dim,
        )
    return cells


def from_partner(x, axis, distance):
    return lax.ppermute(x, axis, [(i, i ^ 1 << distance) for i in range(lax.axis_size(axis))])


def lattice_tables():
    velocities = np.array(
        [
            [0, 0, 0],
            [1, 0, 0],
            [-1, 0, 0],
            [0, 1, 0],
            [0, -1, 0],
            [0, 0, 1],
            [0, 0, -1],
            [1, 1, 0],
            [-1, -1, 0],
            [1, -1, 0],
            [-1, 1, 0],
            [1, 0, 1],
            [-1, 0, -1],
            [1, 0, -1],
            [-1, 0, 1],
            [0, 1, 1],
            [0, -1, -1],
            [0, 1, -1],
            [0, -1, 1],
        ]
    )
    weights = np.array([1.0 / 3.0] + [1.0 / 18.0] * 6 + [1.0 / 36.0] * 12)
    along_x = velocities[:, 0] * 1.0
    along_y = velocities[:, 1] * 1.0
    along_z = velocities[:, 2] * 1.0
    squared = along_x * along_x + along_y * along_y + along_z * along_z
    moment_rows = [
        np.ones(19),
        19.0 * squared - 30.0,
        (21.0 * squared * squared - 53.0 * squared + 24.0) / 2.0,
        along_x,
        (5.0 * squared - 9.0) * along_x,
        along_y,
        (5.0 * squared - 9.0) * along_y,
        along_z,
        (5.0 * squared - 9.0) * along_z,
        3.0 * along_x * along_x - squared,
        (3.0 * squared - 5.0) * (3.0 * along_x * along_x - squared),
        along_y * along_y - along_z * along_z,
        (3.0 * squared - 5.0) * (along_y * along_y - along_z * along_z),
        along_x * along_y,
        along_y * along_z,
        along_x * along_z,
        (along_y * along_y - along_z * along_z) * along_x,
        (along_z * along_z - along_x * along_x) * along_y,
        (along_x * along_x - along_y * along_y) * along_z,
    ]
    moments = np.stack(moment_rows)
    inverse = moments.T / np.sum(moments * moments, axis=1)
    relax_rates = np.array(
        [
            0.0,
            1.19,
            1.4,
            0.0,
            1.2,
            0.0,
            1.2,
            0.0,
            1.2,
            1.0,
            1.4,
            1.0,
            1.4,
            1.0,
            1.0,
            1.0,
            1.98,
            1.98,
            1.98,
        ]
    )
    relaxing = inverse @ (relax_rates[:, None] * moments)
    forcing_map = inverse @ ((1.0 - 0.5 * relax_rates)[:, None] * moments)
    return (velocities, weights, relaxing, forcing_map)


def collide(populations, density, forcing, velocities, weights, relaxing, forcing_map):
    lattice = jnp.asarray(velocities, dtype=jnp.float32)
    spread = jnp.asarray(weights, dtype=jnp.float32)[None, None, :, None]
    relax_table = jnp.asarray(relaxing, dtype=jnp.float32)
    source_table = jnp.asarray(forcing_map, dtype=jnp.float32)
    momentum = jnp.einsum("qd,xyqz->dxyz", lattice, populations, precision=lax.Precision.HIGHEST)
    drift = (momentum + 0.5 * forcing) / density[None]
    along = jnp.einsum("qd,dxyz->xyqz", lattice, drift, precision=lax.Precision.HIGHEST)
    pushed = jnp.einsum("qd,dxyz->xyqz", lattice, forcing, precision=lax.Precision.HIGHEST)
    speed_squared = jnp.sum(drift * drift, axis=0)[:, :, None, :]
    work_done = jnp.sum(drift * forcing, axis=0)[:, :, None, :]
    balance = (
        spread
        * density[:, :, None, :]
        * (1.0 + 3.0 * along + 4.5 * along * along - 1.5 * speed_squared)
    )
    guo_term = spread * (3.0 * (pushed - work_done) + 9.0 * along * pushed)
    relaxed = jnp.einsum(
        "pq,xyqz->xypz", relax_table, populations - balance, precision=lax.Precision.HIGHEST
    )
    sourced = jnp.einsum("pq,xyqz->xypz", source_table, guo_term, precision=lax.Precision.HIGHEST)
    return populations - relaxed + sourced


def attraction(padded, offset, extent_x, extent_y, velocities, weights):
    centre = padded[offset : offset + extent_x, offset : offset + extent_y]
    totals = [jnp.zeros_like(centre), jnp.zeros_like(centre), jnp.zeros_like(centre)]
    for q in range(1, 19):
        steps = [int(v) for v in velocities[q]]
        start_x = offset + steps[0]
        start_y = offset + steps[1]
        neighbour = padded[start_x : start_x + extent_x, start_y : start_y + extent_y]
        neighbour = jnp.roll(neighbour, -steps[2], axis=2)
        for d in range(3):
            if steps[d] != 0:
                totals[d] = totals[d] + weights[q] * steps[d] * neighbour
    return jnp.stack([-cohesion * centre * totals[d] for d in range(3)])


def palette(density):
    reds = density / (1.0 + density)
    greens = jnp.exp(-density)
    blues = 0.5 * (1.0 + jnp.tanh(2.0 * (density - 1.0)))
    return (reds, greens, blues)


def shift_ring(x, axis, step):
    count = lax.axis_size(axis)
    return lax.ppermute(x, axis, [(i, (i - step) % count) for i in range(count)])


def collide_major(f, rho, force, velocities, weights, relaxing, forcing_map):
    lattice = velocities.astype(np.float32)
    extra = (1,) * rho.ndim
    cx = jnp.asarray(lattice[:, 0]).reshape((19,) + extra)
    cy = jnp.asarray(lattice[:, 1]).reshape((19,) + extra)
    cz = jnp.asarray(lattice[:, 2]).reshape((19,) + extra)
    spread = jnp.asarray(weights.astype(np.float32)).reshape((19,) + extra)
    momentum = [
        sum(f[q] * float(velocities[q][d]) for q in range(19) if velocities[q][d] != 0)
        for d in range(3)
    ]
    drift = [(momentum[d] + 0.5 * force[d]) / rho for d in range(3)]
    along = cx * drift[0] + cy * drift[1] + cz * drift[2]
    pushed = cx * force[0] + cy * force[1] + cz * force[2]
    speed_squared = drift[0] * drift[0] + drift[1] * drift[1] + drift[2] * drift[2]
    work_done = drift[0] * force[0] + drift[1] * force[1] + drift[2] * force[2]
    balance = spread * rho * (1.0 + 3.0 * along + 4.5 * along * along - 1.5 * speed_squared)
    guo_term = spread * (3.0 * (pushed - work_done) + 9.0 * along * pushed)
    relax_table = jnp.asarray(relaxing, dtype=jnp.float32)
    source_table = jnp.asarray(forcing_map, dtype=jnp.float32)
    relaxed = jnp.einsum("pq,q...->p...", relax_table, f - balance, precision=lax.Precision.HIGHEST)
    sourced = jnp.einsum("pq,q...->p...", source_table, guo_term, precision=lax.Precision.HIGHEST)
    return f - relaxed + sourced


def stream_and_render(collided, velocities, extent_x, extent_y, length_x):
    depth_z = collided.shape[3]
    steps = [[int(v) for v in velocities[q]] for q in range(19)]

    def kernel(c_ref, o_ref, pic_ref):
        for q in range(19):
            cx, cy, cz = steps[q]

            def move(x, carry):
                v = c_ref[q, x + 1 - cx, pl.ds(1 - cy, extent_y), :]
                if cz != 0:
                    v = pltpu.roll(v, shift=cz % depth_z, axis=1)
                o_ref[q, x] = v
                return carry

            lax.fori_loop(0, extent_x, move, 0)

        def render(x, carry):
            depth, red, green, blue = carry
            fresh_density = o_ref[0, x]
            for q in range(1, 19):
                fresh_density = fresh_density + o_ref[q, x]
            extinction = optical * fresh_density / length_x
            weight = jnp.exp(-depth) * (1.0 - jnp.exp(-extinction))
            red = red + weight * (fresh_density / (1.0 + fresh_density))
            green = green + weight * jnp.exp(-fresh_density)
            blue = blue + weight * (0.5 * (1.0 + jnp.tanh(2.0 * (fresh_density - 1.0))))
            return (depth + extinction, red, green, blue)

        zero = jnp.zeros((extent_y, depth_z), jnp.float32)
        depth, red, green, blue = lax.fori_loop(0, extent_x, render, (zero, zero, zero, zero))
        pic_ref[0] = red
        pic_ref[1] = green
        pic_ref[2] = blue
        pic_ref[3] = 1.0 - jnp.exp(-depth)

    return pl.pallas_call(
        kernel,
        out_shape=(
            jax.ShapeDtypeStruct((19, extent_x, extent_y, depth_z), jnp.float32),
            jax.ShapeDtypeStruct((4, extent_y, depth_z), jnp.float32),
        ),
        in_specs=[pl.BlockSpec(memory_space=pltpu.VMEM)],
        out_specs=(pl.BlockSpec(memory_space=pltpu.VMEM), pl.BlockSpec(memory_space=pltpu.VMEM)),
    )(collided)


def body(populations):
    velocities, weights, relaxing, forcing_map = lattice_tables()
    extent_x = populations.shape[0]
    extent_y = populations.shape[1]
    f = jnp.transpose(populations, (2, 0, 1, 3))
    potential = 1.0 - jnp.exp(-jnp.sum(f, axis=0))
    to_next = jnp.concatenate([f[:, extent_x - 1], potential[extent_x - 1 : extent_x], potential[extent_x - 2 : extent_x - 1]])
    to_prev = jnp.concatenate([f[:, 0], potential[0:1], potential[1:2]])
    from_prev = shift_ring(to_next, "gx", -1)
    from_next = shift_ring(to_prev, "gx", 1)
    fx = jnp.concatenate([from_prev[None, :19].transpose(1, 0, 2, 3), f, from_next[None, :19].transpose(1, 0, 2, 3)], axis=1)
    px = jnp.concatenate([from_prev[20:21], from_prev[19:20], potential, from_next[19:20], from_next[20:21]], axis=0)
    zero_x = jnp.zeros((19, 1, fx.shape[3]), f.dtype)

    def y_message(row_pop, row_near, row_far):
        pops = jnp.concatenate([zero_x, fx[:, :, row_pop], zero_x], axis=1)
        return jnp.concatenate([pops, px[None, :, row_near], px[None, :, row_far]], axis=0)

    from_below = shift_ring(y_message(extent_y - 1, extent_y - 1, extent_y - 2), "gy", -1)
    from_above = shift_ring(y_message(0, 0, 1), "gy", 1)
    fxy = jnp.concatenate(
        [from_below[:19, 1:-1, None], fx, from_above[:19, 1:-1, None]], axis=2
    )
    pxy = jnp.concatenate(
        [from_below[20][:, None], from_below[19][:, None], px, from_above[19][:, None], from_above[20][:, None]],
        axis=1,
    )
    ext_x = extent_x + 2
    ext_y = extent_y + 2
    centre = pxy[1 : 1 + ext_x, 1 : 1 + ext_y]
    totals = [jnp.zeros_like(centre), jnp.zeros_like(centre), jnp.zeros_like(centre)]
    for q in range(1, 19):
        steps = [int(v) for v in velocities[q]]
        neighbour = pxy[1 + steps[0] : 1 + steps[0] + ext_x, 1 + steps[1] : 1 + steps[1] + ext_y]
        neighbour = jnp.roll(neighbour, -steps[2], axis=2)
        for d in range(3):
            if steps[d] != 0:
                totals[d] = totals[d] + weights[q] * steps[d] * neighbour
    force = [-cohesion * centre * totals[d] for d in range(3)]
    rho = jnp.sum(fxy, axis=0)
    collided = collide_major(fxy, rho, force, velocities, weights, relaxing, forcing_map)
    groups = lax.axis_size("gx")
    length_x = extent_x * groups
    fresh_major, layered = stream_and_render(collided, velocities, extent_x, extent_y, length_x)
    fresh = jnp.transpose(fresh_major, (1, 2, 0, 3))
    depth_z = layered.shape[2]
    block_len = depth_z // groups
    blocked = layered.reshape(4, extent_y, groups, block_len)
    position = lax.axis_index("gx")
    current = blocked
    for level in range(groups.bit_length() - 1):
        parity = position // (1 << level) % 2
        halves = current.shape[2] // 2
        paired = current.reshape(4, extent_y, halves, 2, block_len)
        lower = paired[:, :, :, 0]
        upper = paired[:, :, :, 1]
        kept = jnp.where(parity == 1, upper, lower)
        handed = jnp.where(parity == 1, lower, upper)
        partner = from_partner(handed, "gx", level)
        nearer = jnp.where(parity == 0, kept, partner)
        farther = jnp.where(parity == 0, partner, kept)
        current = nearer + (1.0 - nearer[3:4]) * farther
    picture = current.reshape(4, extent_y, block_len)
    return (fresh, picture)


def solution(mesh):
    placed = (P("gx", "gy", None, None),)
    return jax.shard_map(
        body,
        mesh=mesh,
        in_specs=placed,
        out_specs=(P("gx", "gy", None, None), P(None, "gy", "gx")),
        check_vma=False,
    )
```

```python
import jax
import jax.numpy as jnp
import numpy as np
from jax import lax
from jax.sharding import PartitionSpec as P
from jax.experimental import pallas as pl
from jax.experimental.pallas import tpu as pltpu

cohesion = -6.0
optical = 2.0


def extended(cells, sides, width):
    for axis, dim in sides:
        count = lax.axis_size(axis)
        head = lax.slice_in_dim(cells, 0, width, axis=dim)
        tail = lax.slice_in_dim(cells, cells.shape[dim] - width, cells.shape[dim], axis=dim)
        cells = jnp.concatenate(
            [
                lax.ppermute(tail, axis, [(i, (i + 1) % count) for i in range(count)]),
                cells,
                lax.ppermute(head, axis, [((i + 1) % count, i) for i in range(count)]),
            ],
            axis=dim,
        )
    return cells


def from_partner(x, axis, distance):
    return lax.ppermute(x, axis, [(i, i ^ 1 << distance) for i in range(lax.axis_size(axis))])


def lattice_tables():
    velocities = np.array(
        [
            [0, 0, 0],
            [1, 0, 0],
            [-1, 0, 0],
            [0, 1, 0],
            [0, -1, 0],
            [0, 0, 1],
            [0, 0, -1],
            [1, 1, 0],
            [-1, -1, 0],
            [1, -1, 0],
            [-1, 1, 0],
            [1, 0, 1],
            [-1, 0, -1],
            [1, 0, -1],
            [-1, 0, 1],
            [0, 1, 1],
            [0, -1, -1],
            [0, 1, -1],
            [0, -1, 1],
        ]
    )
    weights = np.array([1.0 / 3.0] + [1.0 / 18.0] * 6 + [1.0 / 36.0] * 12)
    along_x = velocities[:, 0] * 1.0
    along_y = velocities[:, 1] * 1.0
    along_z = velocities[:, 2] * 1.0
    squared = along_x * along_x + along_y * along_y + along_z * along_z
    moment_rows = [
        np.ones(19),
        19.0 * squared - 30.0,
        (21.0 * squared * squared - 53.0 * squared + 24.0) / 2.0,
        along_x,
        (5.0 * squared - 9.0) * along_x,
        along_y,
        (5.0 * squared - 9.0) * along_y,
        along_z,
        (5.0 * squared - 9.0) * along_z,
        3.0 * along_x * along_x - squared,
        (3.0 * squared - 5.0) * (3.0 * along_x * along_x - squared),
        along_y * along_y - along_z * along_z,
        (3.0 * squared - 5.0) * (along_y * along_y - along_z * along_z),
        along_x * along_y,
        along_y * along_z,
        along_x * along_z,
        (along_y * along_y - along_z * along_z) * along_x,
        (along_z * along_z - along_x * along_x) * along_y,
        (along_x * along_x - along_y * along_y) * along_z,
    ]
    moments = np.stack(moment_rows)
    inverse = moments.T / np.sum(moments * moments, axis=1)
    relax_rates = np.array(
        [
            0.0,
            1.19,
            1.4,
            0.0,
            1.2,
            0.0,
            1.2,
            0.0,
            1.2,
            1.0,
            1.4,
            1.0,
            1.4,
            1.0,
            1.0,
            1.0,
            1.98,
            1.98,
            1.98,
        ]
    )
    relaxing = inverse @ (relax_rates[:, None] * moments)
    forcing_map = inverse @ ((1.0 - 0.5 * relax_rates)[:, None] * moments)
    return (velocities, weights, relaxing, forcing_map)


def collide(populations, density, forcing, velocities, weights, relaxing, forcing_map):
    lattice = jnp.asarray(velocities, dtype=jnp.float32)
    spread = jnp.asarray(weights, dtype=jnp.float32)[None, None, :, None]
    relax_table = jnp.asarray(relaxing, dtype=jnp.float32)
    source_table = jnp.asarray(forcing_map, dtype=jnp.float32)
    momentum = jnp.einsum("qd,xyqz->dxyz", lattice, populations, precision=lax.Precision.HIGHEST)
    drift = (momentum + 0.5 * forcing) / density[None]
    along = jnp.einsum("qd,dxyz->xyqz", lattice, drift, precision=lax.Precision.HIGHEST)
    pushed = jnp.einsum("qd,dxyz->xyqz", lattice, forcing, precision=lax.Precision.HIGHEST)
    speed_squared = jnp.sum(drift * drift, axis=0)[:, :, None, :]
    work_done = jnp.sum(drift * forcing, axis=0)[:, :, None, :]
    balance = (
        spread
        * density[:, :, None, :]
        * (1.0 + 3.0 * along + 4.5 * along * along - 1.5 * speed_squared)
    )
    guo_term = spread * (3.0 * (pushed - work_done) + 9.0 * along * pushed)
    relaxed = jnp.einsum(
        "pq,xyqz->xypz", relax_table, populations - balance, precision=lax.Precision.HIGHEST
    )
    sourced = jnp.einsum("pq,xyqz->xypz", source_table, guo_term, precision=lax.Precision.HIGHEST)
    return populations - relaxed + sourced


def attraction(padded, offset, extent_x, extent_y, velocities, weights):
    centre = padded[offset : offset + extent_x, offset : offset + extent_y]
    totals = [jnp.zeros_like(centre), jnp.zeros_like(centre), jnp.zeros_like(centre)]
    for q in range(1, 19):
        steps = [int(v) for v in velocities[q]]
        start_x = offset + steps[0]
        start_y = offset + steps[1]
        neighbour = padded[start_x : start_x + extent_x, start_y : start_y + extent_y]
        neighbour = jnp.roll(neighbour, -steps[2], axis=2)
        for d in range(3):
            if steps[d] != 0:
                totals[d] = totals[d] + weights[q] * steps[d] * neighbour
    return jnp.stack([-cohesion * centre * totals[d] for d in range(3)])


def palette(density):
    reds = density / (1.0 + density)
    greens = jnp.exp(-density)
    blues = 0.5 * (1.0 + jnp.tanh(2.0 * (density - 1.0)))
    return (reds, greens, blues)


def shift_ring(x, axis, step):
    count = lax.axis_size(axis)
    return lax.ppermute(x, axis, [(i, (i - step) % count) for i in range(count)])


def collide_major(f, rho, force, velocities, weights, relaxing, forcing_map):
    lattice = velocities.astype(np.float32)
    extra = (1,) * rho.ndim
    cx = jnp.asarray(lattice[:, 0]).reshape((19,) + extra)
    cy = jnp.asarray(lattice[:, 1]).reshape((19,) + extra)
    cz = jnp.asarray(lattice[:, 2]).reshape((19,) + extra)
    spread = jnp.asarray(weights.astype(np.float32)).reshape((19,) + extra)
    momentum = [
        sum(f[q] * float(velocities[q][d]) for q in range(19) if velocities[q][d] != 0)
        for d in range(3)
    ]
    drift = [(momentum[d] + 0.5 * force[d]) / rho for d in range(3)]
    along = cx * drift[0] + cy * drift[1] + cz * drift[2]
    pushed = cx * force[0] + cy * force[1] + cz * force[2]
    speed_squared = drift[0] * drift[0] + drift[1] * drift[1] + drift[2] * drift[2]
    work_done = drift[0] * force[0] + drift[1] * force[1] + drift[2] * force[2]
    balance = spread * rho * (1.0 + 3.0 * along + 4.5 * along * along - 1.5 * speed_squared)
    guo_term = spread * (3.0 * (pushed - work_done) + 9.0 * along * pushed)
    relax_table = jnp.asarray(relaxing, dtype=jnp.float32)
    source_table = jnp.asarray(forcing_map, dtype=jnp.float32)
    relaxed = jnp.einsum("pq,q...->p...", relax_table, f - balance, precision=lax.Precision.HIGHEST)
    sourced = jnp.einsum("pq,q...->p...", source_table, guo_term, precision=lax.Precision.HIGHEST)
    return f - relaxed + sourced


def stream_and_render(collided, velocities, extent_x, extent_y, length_x):
    depth_z = collided.shape[3]
    steps = [[int(v) for v in velocities[q]] for q in range(19)]

    def kernel(c_ref, o_ref, pic_ref):
        for q in range(19):
            cx, cy, cz = steps[q]

            def move(x, carry):
                v = c_ref[q, x + 1 - cx, pl.ds(1 - cy, extent_y), :]
                if cz != 0:
                    v = pltpu.roll(v, shift=cz % depth_z, axis=1)
                o_ref[q, x] = v
                return carry

            lax.fori_loop(0, extent_x, move, 0, unroll=True)

        def render(x, carry):
            depth, red, green, blue = carry
            fresh_density = o_ref[0, x]
            for q in range(1, 19):
                fresh_density = fresh_density + o_ref[q, x]
            extinction = optical * fresh_density / length_x
            weight = jnp.exp(-depth) * (1.0 - jnp.exp(-extinction))
            red = red + weight * (fresh_density / (1.0 + fresh_density))
            green = green + weight * jnp.exp(-fresh_density)
            blue = blue + weight * (0.5 * (1.0 + jnp.tanh(2.0 * (fresh_density - 1.0))))
            return (depth + extinction, red, green, blue)

        zero = jnp.zeros((extent_y, depth_z), jnp.float32)
        depth, red, green, blue = lax.fori_loop(0, extent_x, render, (zero, zero, zero, zero), unroll=True)
        pic_ref[0] = red
        pic_ref[1] = green
        pic_ref[2] = blue
        pic_ref[3] = 1.0 - jnp.exp(-depth)

    return pl.pallas_call(
        kernel,
        out_shape=(
            jax.ShapeDtypeStruct((19, extent_x, extent_y, depth_z), jnp.float32),
            jax.ShapeDtypeStruct((4, extent_y, depth_z), jnp.float32),
        ),
        in_specs=[pl.BlockSpec(memory_space=pltpu.VMEM)],
        out_specs=(pl.BlockSpec(memory_space=pltpu.VMEM), pl.BlockSpec(memory_space=pltpu.VMEM)),
    )(collided)


def body(populations):
    velocities, weights, relaxing, forcing_map = lattice_tables()
    extent_x = populations.shape[0]
    extent_y = populations.shape[1]
    f = jnp.transpose(populations, (2, 0, 1, 3))
    potential = 1.0 - jnp.exp(-jnp.sum(f, axis=0))
    to_next = jnp.concatenate([f[:, extent_x - 1], potential[extent_x - 1 : extent_x], potential[extent_x - 2 : extent_x - 1]])
    to_prev = jnp.concatenate([f[:, 0], potential[0:1], potential[1:2]])
    from_prev = shift_ring(to_next, "gx", -1)
    from_next = shift_ring(to_prev, "gx", 1)
    fx = jnp.concatenate([from_prev[None, :19].transpose(1, 0, 2, 3), f, from_next[None, :19].transpose(1, 0, 2, 3)], axis=1)
    px = jnp.concatenate([from_prev[20:21], from_prev[19:20], potential, from_next[19:20], from_next[20:21]], axis=0)
    zero_x = jnp.zeros((19, 1, fx.shape[3]), f.dtype)

    def y_message(row_pop, row_near, row_far):
        pops = jnp.concatenate([zero_x, fx[:, :, row_pop], zero_x], axis=1)
        return jnp.concatenate([pops, px[None, :, row_near], px[None, :, row_far]], axis=0)

    from_below = shift_ring(y_message(extent_y - 1, extent_y - 1, extent_y - 2), "gy", -1)
    from_above = shift_ring(y_message(0, 0, 1), "gy", 1)
    fxy = jnp.concatenate(
        [from_below[:19, 1:-1, None], fx, from_above[:19, 1:-1, None]], axis=2
    )
    pxy = jnp.concatenate(
        [from_below[20][:, None], from_below[19][:, None], px, from_above[19][:, None], from_above[20][:, None]],
        axis=1,
    )
    ext_x = extent_x + 2
    ext_y = extent_y + 2
    centre = pxy[1 : 1 + ext_x, 1 : 1 + ext_y]
    totals = [jnp.zeros_like(centre), jnp.zeros_like(centre), jnp.zeros_like(centre)]
    for q in range(1, 19):
        steps = [int(v) for v in velocities[q]]
        neighbour = pxy[1 + steps[0] : 1 + steps[0] + ext_x, 1 + steps[1] : 1 + steps[1] + ext_y]
        neighbour = jnp.roll(neighbour, -steps[2], axis=2)
        for d in range(3):
            if steps[d] != 0:
                totals[d] = totals[d] + weights[q] * steps[d] * neighbour
    force = [-cohesion * centre * totals[d] for d in range(3)]
    rho = jnp.sum(fxy, axis=0)
    collided = collide_major(fxy, rho, force, velocities, weights, relaxing, forcing_map)
    groups = lax.axis_size("gx")
    length_x = extent_x * groups
    fresh_major, layered = stream_and_render(collided, velocities, extent_x, extent_y, length_x)
    fresh = jnp.transpose(fresh_major, (1, 2, 0, 3))
    depth_z = layered.shape[2]
    block_len = depth_z // groups
    blocked = layered.reshape(4, extent_y, groups, block_len)
    position = lax.axis_index("gx")
    current = blocked
    for level in range(groups.bit_length() - 1):
        parity = position // (1 << level) % 2
        halves = current.shape[2] // 2
        paired = current.reshape(4, extent_y, halves, 2, block_len)
        lower = paired[:, :, :, 0]
        upper = paired[:, :, :, 1]
        kept = jnp.where(parity == 1, upper, lower)
        handed = jnp.where(parity == 1, lower, upper)
        partner = from_partner(handed, "gx", level)
        nearer = jnp.where(parity == 0, kept, partner)
        farther = jnp.where(parity == 0, partner, kept)
        current = nearer + (1.0 - nearer[3:4]) * farther
    picture = current.reshape(4, extent_y, block_len)
    return (fresh, picture)


def solution(mesh):
    placed = (P("gx", "gy", None, None),)
    return jax.shard_map(
        body,
        mesh=mesh,
        in_specs=placed,
        out_specs=(P("gx", "gy", None, None), P(None, "gy", "gx")),
        check_vma=False,
    )
```

```python
import jax
import jax.numpy as jnp
import numpy as np
from jax import lax
from jax.sharding import PartitionSpec as P
from jax.experimental import pallas as pl
from jax.experimental.pallas import tpu as pltpu

cohesion = -6.0
optical = 2.0


def extended(cells, sides, width):
    for axis, dim in sides:
        count = lax.axis_size(axis)
        head = lax.slice_in_dim(cells, 0, width, axis=dim)
        tail = lax.slice_in_dim(cells, cells.shape[dim] - width, cells.shape[dim], axis=dim)
        cells = jnp.concatenate(
            [
                lax.ppermute(tail, axis, [(i, (i + 1) % count) for i in range(count)]),
                cells,
                lax.ppermute(head, axis, [((i + 1) % count, i) for i in range(count)]),
            ],
            axis=dim,
        )
    return cells


def from_partner(x, axis, distance):
    return lax.ppermute(x, axis, [(i, i ^ 1 << distance) for i in range(lax.axis_size(axis))])


def lattice_tables():
    velocities = np.array(
        [
            [0, 0, 0],
            [1, 0, 0],
            [-1, 0, 0],
            [0, 1, 0],
            [0, -1, 0],
            [0, 0, 1],
            [0, 0, -1],
            [1, 1, 0],
            [-1, -1, 0],
            [1, -1, 0],
            [-1, 1, 0],
            [1, 0, 1],
            [-1, 0, -1],
            [1, 0, -1],
            [-1, 0, 1],
            [0, 1, 1],
            [0, -1, -1],
            [0, 1, -1],
            [0, -1, 1],
        ]
    )
    weights = np.array([1.0 / 3.0] + [1.0 / 18.0] * 6 + [1.0 / 36.0] * 12)
    along_x = velocities[:, 0] * 1.0
    along_y = velocities[:, 1] * 1.0
    along_z = velocities[:, 2] * 1.0
    squared = along_x * along_x + along_y * along_y + along_z * along_z
    moment_rows = [
        np.ones(19),
        19.0 * squared - 30.0,
        (21.0 * squared * squared - 53.0 * squared + 24.0) / 2.0,
        along_x,
        (5.0 * squared - 9.0) * along_x,
        along_y,
        (5.0 * squared - 9.0) * along_y,
        along_z,
        (5.0 * squared - 9.0) * along_z,
        3.0 * along_x * along_x - squared,
        (3.0 * squared - 5.0) * (3.0 * along_x * along_x - squared),
        along_y * along_y - along_z * along_z,
        (3.0 * squared - 5.0) * (along_y * along_y - along_z * along_z),
        along_x * along_y,
        along_y * along_z,
        along_x * along_z,
        (along_y * along_y - along_z * along_z) * along_x,
        (along_z * along_z - along_x * along_x) * along_y,
        (along_x * along_x - along_y * along_y) * along_z,
    ]
    moments = np.stack(moment_rows)
    inverse = moments.T / np.sum(moments * moments, axis=1)
    relax_rates = np.array(
        [
            0.0,
            1.19,
            1.4,
            0.0,
            1.2,
            0.0,
            1.2,
            0.0,
            1.2,
            1.0,
            1.4,
            1.0,
            1.4,
            1.0,
            1.0,
            1.0,
            1.98,
            1.98,
            1.98,
        ]
    )
    relaxing = inverse @ (relax_rates[:, None] * moments)
    forcing_map = inverse @ ((1.0 - 0.5 * relax_rates)[:, None] * moments)
    return (velocities, weights, relaxing, forcing_map)


def collide(populations, density, forcing, velocities, weights, relaxing, forcing_map):
    lattice = jnp.asarray(velocities, dtype=jnp.float32)
    spread = jnp.asarray(weights, dtype=jnp.float32)[None, None, :, None]
    relax_table = jnp.asarray(relaxing, dtype=jnp.float32)
    source_table = jnp.asarray(forcing_map, dtype=jnp.float32)
    momentum = jnp.einsum("qd,xyqz->dxyz", lattice, populations, precision=lax.Precision.HIGHEST)
    drift = (momentum + 0.5 * forcing) / density[None]
    along = jnp.einsum("qd,dxyz->xyqz", lattice, drift, precision=lax.Precision.HIGHEST)
    pushed = jnp.einsum("qd,dxyz->xyqz", lattice, forcing, precision=lax.Precision.HIGHEST)
    speed_squared = jnp.sum(drift * drift, axis=0)[:, :, None, :]
    work_done = jnp.sum(drift * forcing, axis=0)[:, :, None, :]
    balance = (
        spread
        * density[:, :, None, :]
        * (1.0 + 3.0 * along + 4.5 * along * along - 1.5 * speed_squared)
    )
    guo_term = spread * (3.0 * (pushed - work_done) + 9.0 * along * pushed)
    relaxed = jnp.einsum(
        "pq,xyqz->xypz", relax_table, populations - balance, precision=lax.Precision.HIGHEST
    )
    sourced = jnp.einsum("pq,xyqz->xypz", source_table, guo_term, precision=lax.Precision.HIGHEST)
    return populations - relaxed + sourced


def attraction(padded, offset, extent_x, extent_y, velocities, weights):
    centre = padded[offset : offset + extent_x, offset : offset + extent_y]
    totals = [jnp.zeros_like(centre), jnp.zeros_like(centre), jnp.zeros_like(centre)]
    for q in range(1, 19):
        steps = [int(v) for v in velocities[q]]
        start_x = offset + steps[0]
        start_y = offset + steps[1]
        neighbour = padded[start_x : start_x + extent_x, start_y : start_y + extent_y]
        neighbour = jnp.roll(neighbour, -steps[2], axis=2)
        for d in range(3):
            if steps[d] != 0:
                totals[d] = totals[d] + weights[q] * steps[d] * neighbour
    return jnp.stack([-cohesion * centre * totals[d] for d in range(3)])


def palette(density):
    reds = density / (1.0 + density)
    greens = jnp.exp(-density)
    blues = 0.5 * (1.0 + jnp.tanh(2.0 * (density - 1.0)))
    return (reds, greens, blues)


def shift_ring(x, axis, step):
    count = lax.axis_size(axis)
    return lax.ppermute(x, axis, [(i, (i - step) % count) for i in range(count)])


def collide_major(f, rho, force, velocities, weights, relaxing, forcing_map):
    lattice = velocities.astype(np.float32)
    extra = (1,) * rho.ndim
    cx = jnp.asarray(lattice[:, 0]).reshape((19,) + extra)
    cy = jnp.asarray(lattice[:, 1]).reshape((19,) + extra)
    cz = jnp.asarray(lattice[:, 2]).reshape((19,) + extra)
    spread = jnp.asarray(weights.astype(np.float32)).reshape((19,) + extra)
    momentum = [
        sum(f[q] * float(velocities[q][d]) for q in range(19) if velocities[q][d] != 0)
        for d in range(3)
    ]
    drift = [(momentum[d] + 0.5 * force[d]) / rho for d in range(3)]
    along = cx * drift[0] + cy * drift[1] + cz * drift[2]
    pushed = cx * force[0] + cy * force[1] + cz * force[2]
    speed_squared = drift[0] * drift[0] + drift[1] * drift[1] + drift[2] * drift[2]
    work_done = drift[0] * force[0] + drift[1] * force[1] + drift[2] * force[2]
    balance = spread * rho * (1.0 + 3.0 * along + 4.5 * along * along - 1.5 * speed_squared)
    guo_term = spread * (3.0 * (pushed - work_done) + 9.0 * along * pushed)
    relax_table = jnp.asarray(relaxing, dtype=jnp.float32)
    source_table = jnp.asarray(forcing_map, dtype=jnp.float32)
    table = jnp.concatenate([relax_table, -source_table], axis=1)
    stacked = jnp.concatenate([f - balance, guo_term], axis=0)
    return f - jnp.einsum("pq,q...->p...", table, stacked, precision=lax.Precision.HIGH)


def stream_and_render(collided, velocities, extent_x, extent_y, length_x):
    depth_z = collided.shape[3]
    steps = [[int(v) for v in velocities[q]] for q in range(19)]

    def kernel(c_ref, o_ref, pic_ref):
        for q in range(19):
            cx, cy, cz = steps[q]

            def move(x, carry):
                v = c_ref[q, x + 1 - cx, pl.ds(1 - cy, extent_y), :]
                if cz != 0:
                    v = pltpu.roll(v, shift=cz % depth_z, axis=1)
                o_ref[q, x] = v
                return carry

            lax.fori_loop(0, extent_x, move, 0, unroll=True)

        def render(x, carry):
            depth, red, green, blue = carry
            fresh_density = o_ref[0, x]
            for q in range(1, 19):
                fresh_density = fresh_density + o_ref[q, x]
            extinction = optical * fresh_density / length_x
            weight = jnp.exp(-depth) * (1.0 - jnp.exp(-extinction))
            red = red + weight * (fresh_density / (1.0 + fresh_density))
            green = green + weight * jnp.exp(-fresh_density)
            blue = blue + weight * (0.5 * (1.0 + jnp.tanh(2.0 * (fresh_density - 1.0))))
            return (depth + extinction, red, green, blue)

        zero = jnp.zeros((extent_y, depth_z), jnp.float32)
        depth, red, green, blue = lax.fori_loop(0, extent_x, render, (zero, zero, zero, zero), unroll=True)
        pic_ref[0] = red
        pic_ref[1] = green
        pic_ref[2] = blue
        pic_ref[3] = 1.0 - jnp.exp(-depth)

    return pl.pallas_call(
        kernel,
        out_shape=(
            jax.ShapeDtypeStruct((19, extent_x, extent_y, depth_z), jnp.float32),
            jax.ShapeDtypeStruct((4, extent_y, depth_z), jnp.float32),
        ),
        in_specs=[pl.BlockSpec(memory_space=pltpu.VMEM)],
        out_specs=(pl.BlockSpec(memory_space=pltpu.VMEM), pl.BlockSpec(memory_space=pltpu.VMEM)),
    )(collided)


def body(populations):
    velocities, weights, relaxing, forcing_map = lattice_tables()
    extent_x = populations.shape[0]
    extent_y = populations.shape[1]
    f = jnp.transpose(populations, (2, 0, 1, 3))
    potential = 1.0 - jnp.exp(-jnp.sum(f, axis=0))
    to_next = jnp.concatenate([f[:, extent_x - 1], potential[extent_x - 1 : extent_x], potential[extent_x - 2 : extent_x - 1]])
    to_prev = jnp.concatenate([f[:, 0], potential[0:1], potential[1:2]])
    from_prev = shift_ring(to_next, "gx", -1)
    from_next = shift_ring(to_prev, "gx", 1)
    fx = jnp.concatenate([from_prev[None, :19].transpose(1, 0, 2, 3), f, from_next[None, :19].transpose(1, 0, 2, 3)], axis=1)
    px = jnp.concatenate([from_prev[20:21], from_prev[19:20], potential, from_next[19:20], from_next[20:21]], axis=0)
    zero_x = jnp.zeros((19, 1, fx.shape[3]), f.dtype)

    def y_message(row_pop, row_near, row_far):
        pops = jnp.concatenate([zero_x, fx[:, :, row_pop], zero_x], axis=1)
        return jnp.concatenate([pops, px[None, :, row_near], px[None, :, row_far]], axis=0)

    from_below = shift_ring(y_message(extent_y - 1, extent_y - 1, extent_y - 2), "gy", -1)
    from_above = shift_ring(y_message(0, 0, 1), "gy", 1)
    fxy = jnp.concatenate(
        [from_below[:19, 1:-1, None], fx, from_above[:19, 1:-1, None]], axis=2
    )
    pxy = jnp.concatenate(
        [from_below[20][:, None], from_below[19][:, None], px, from_above[19][:, None], from_above[20][:, None]],
        axis=1,
    )
    ext_x = extent_x + 2
    ext_y = extent_y + 2
    centre = pxy[1 : 1 + ext_x, 1 : 1 + ext_y]
    totals = [jnp.zeros_like(centre), jnp.zeros_like(centre), jnp.zeros_like(centre)]
    for q in range(1, 19):
        steps = [int(v) for v in velocities[q]]
        neighbour = pxy[1 + steps[0] : 1 + steps[0] + ext_x, 1 + steps[1] : 1 + steps[1] + ext_y]
        neighbour = jnp.roll(neighbour, -steps[2], axis=2)
        for d in range(3):
            if steps[d] != 0:
                totals[d] = totals[d] + weights[q] * steps[d] * neighbour
    force = [-cohesion * centre * totals[d] for d in range(3)]
    rho = jnp.sum(fxy, axis=0)
    collided = collide_major(fxy, rho, force, velocities, weights, relaxing, forcing_map)
    groups = lax.axis_size("gx")
    length_x = extent_x * groups
    fresh_major, layered = stream_and_render(collided, velocities, extent_x, extent_y, length_x)
    fresh = jnp.transpose(fresh_major, (1, 2, 0, 3))
    depth_z = layered.shape[2]
    block_len = depth_z // groups
    blocked = layered.reshape(4, extent_y, groups, block_len)
    position = lax.axis_index("gx")
    current = blocked
    for level in range(groups.bit_length() - 1):
        parity = position // (1 << level) % 2
        halves = current.shape[2] // 2
        paired = current.reshape(4, extent_y, halves, 2, block_len)
        lower = paired[:, :, :, 0]
        upper = paired[:, :, :, 1]
        kept = jnp.where(parity == 1, upper, lower)
        handed = jnp.where(parity == 1, lower, upper)
        partner = from_partner(handed, "gx", level)
        nearer = jnp.where(parity == 0, kept, partner)
        farther = jnp.where(parity == 0, partner, kept)
        current = nearer + (1.0 - nearer[3:4]) * farther
    picture = current.reshape(4, extent_y, block_len)
    return (fresh, picture)


def solution(mesh):
    placed = (P("gx", "gy", None, None),)
    return jax.shard_map(
        body,
        mesh=mesh,
        in_specs=placed,
        out_specs=(P("gx", "gy", None, None), P(None, "gy", "gx")),
        check_vma=False,
    )
```

```python
import jax
import jax.numpy as jnp
import numpy as np
from jax import lax
from jax.sharding import PartitionSpec as P
from jax.experimental import pallas as pl
from jax.experimental.pallas import tpu as pltpu

cohesion = -6.0
optical = 2.0


def extended(cells, sides, width):
    for axis, dim in sides:
        count = lax.axis_size(axis)
        head = lax.slice_in_dim(cells, 0, width, axis=dim)
        tail = lax.slice_in_dim(cells, cells.shape[dim] - width, cells.shape[dim], axis=dim)
        cells = jnp.concatenate(
            [
                lax.ppermute(tail, axis, [(i, (i + 1) % count) for i in range(count)]),
                cells,
                lax.ppermute(head, axis, [((i + 1) % count, i) for i in range(count)]),
            ],
            axis=dim,
        )
    return cells


def from_partner(x, axis, distance):
    return lax.ppermute(x, axis, [(i, i ^ 1 << distance) for i in range(lax.axis_size(axis))])


def lattice_tables():
    velocities = np.array(
        [
            [0, 0, 0],
            [1, 0, 0],
            [-1, 0, 0],
            [0, 1, 0],
            [0, -1, 0],
            [0, 0, 1],
            [0, 0, -1],
            [1, 1, 0],
            [-1, -1, 0],
            [1, -1, 0],
            [-1, 1, 0],
            [1, 0, 1],
            [-1, 0, -1],
            [1, 0, -1],
            [-1, 0, 1],
            [0, 1, 1],
            [0, -1, -1],
            [0, 1, -1],
            [0, -1, 1],
        ]
    )
    weights = np.array([1.0 / 3.0] + [1.0 / 18.0] * 6 + [1.0 / 36.0] * 12)
    along_x = velocities[:, 0] * 1.0
    along_y = velocities[:, 1] * 1.0
    along_z = velocities[:, 2] * 1.0
    squared = along_x * along_x + along_y * along_y + along_z * along_z
    moment_rows = [
        np.ones(19),
        19.0 * squared - 30.0,
        (21.0 * squared * squared - 53.0 * squared + 24.0) / 2.0,
        along_x,
        (5.0 * squared - 9.0) * along_x,
        along_y,
        (5.0 * squared - 9.0) * along_y,
        along_z,
        (5.0 * squared - 9.0) * along_z,
        3.0 * along_x * along_x - squared,
        (3.0 * squared - 5.0) * (3.0 * along_x * along_x - squared),
        along_y * along_y - along_z * along_z,
        (3.0 * squared - 5.0) * (along_y * along_y - along_z * along_z),
        along_x * along_y,
        along_y * along_z,
        along_x * along_z,
        (along_y * along_y - along_z * along_z) * along_x,
        (along_z * along_z - along_x * along_x) * along_y,
        (along_x * along_x - along_y * along_y) * along_z,
    ]
    moments = np.stack(moment_rows)
    inverse = moments.T / np.sum(moments * moments, axis=1)
    relax_rates = np.array(
        [
            0.0,
            1.19,
            1.4,
            0.0,
            1.2,
            0.0,
            1.2,
            0.0,
            1.2,
            1.0,
            1.4,
            1.0,
            1.4,
            1.0,
            1.0,
            1.0,
            1.98,
            1.98,
            1.98,
        ]
    )
    relaxing = inverse @ (relax_rates[:, None] * moments)
    forcing_map = inverse @ ((1.0 - 0.5 * relax_rates)[:, None] * moments)
    return (velocities, weights, relaxing, forcing_map)


def collide(populations, density, forcing, velocities, weights, relaxing, forcing_map):
    lattice = jnp.asarray(velocities, dtype=jnp.float32)
    spread = jnp.asarray(weights, dtype=jnp.float32)[None, None, :, None]
    relax_table = jnp.asarray(relaxing, dtype=jnp.float32)
    source_table = jnp.asarray(forcing_map, dtype=jnp.float32)
    momentum = jnp.einsum("qd,xyqz->dxyz", lattice, populations, precision=lax.Precision.HIGHEST)
    drift = (momentum + 0.5 * forcing) / density[None]
    along = jnp.einsum("qd,dxyz->xyqz", lattice, drift, precision=lax.Precision.HIGHEST)
    pushed = jnp.einsum("qd,dxyz->xyqz", lattice, forcing, precision=lax.Precision.HIGHEST)
    speed_squared = jnp.sum(drift * drift, axis=0)[:, :, None, :]
    work_done = jnp.sum(drift * forcing, axis=0)[:, :, None, :]
    balance = (
        spread
        * density[:, :, None, :]
        * (1.0 + 3.0 * along + 4.5 * along * along - 1.5 * speed_squared)
    )
    guo_term = spread * (3.0 * (pushed - work_done) + 9.0 * along * pushed)
    relaxed = jnp.einsum(
        "pq,xyqz->xypz", relax_table, populations - balance, precision=lax.Precision.HIGHEST
    )
    sourced = jnp.einsum("pq,xyqz->xypz", source_table, guo_term, precision=lax.Precision.HIGHEST)
    return populations - relaxed + sourced


def attraction(padded, offset, extent_x, extent_y, velocities, weights):
    centre = padded[offset : offset + extent_x, offset : offset + extent_y]
    totals = [jnp.zeros_like(centre), jnp.zeros_like(centre), jnp.zeros_like(centre)]
    for q in range(1, 19):
        steps = [int(v) for v in velocities[q]]
        start_x = offset + steps[0]
        start_y = offset + steps[1]
        neighbour = padded[start_x : start_x + extent_x, start_y : start_y + extent_y]
        neighbour = jnp.roll(neighbour, -steps[2], axis=2)
        for d in range(3):
            if steps[d] != 0:
                totals[d] = totals[d] + weights[q] * steps[d] * neighbour
    return jnp.stack([-cohesion * centre * totals[d] for d in range(3)])


def palette(density):
    reds = density / (1.0 + density)
    greens = jnp.exp(-density)
    blues = 0.5 * (1.0 + jnp.tanh(2.0 * (density - 1.0)))
    return (reds, greens, blues)


def shift_ring(x, axis, step):
    count = lax.axis_size(axis)
    return lax.ppermute(x, axis, [(i, (i - step) % count) for i in range(count)])


def collide_major(f, rho, force, velocities, weights, relaxing, forcing_map):
    lattice = velocities.astype(np.float32)
    extra = (1,) * rho.ndim
    cx = jnp.asarray(lattice[:, 0]).reshape((19,) + extra)
    cy = jnp.asarray(lattice[:, 1]).reshape((19,) + extra)
    cz = jnp.asarray(lattice[:, 2]).reshape((19,) + extra)
    spread = jnp.asarray(weights.astype(np.float32)).reshape((19,) + extra)
    momentum = [
        sum(f[q] * float(velocities[q][d]) for q in range(19) if velocities[q][d] != 0)
        for d in range(3)
    ]
    drift = [(momentum[d] + 0.5 * force[d]) / rho for d in range(3)]
    along = cx * drift[0] + cy * drift[1] + cz * drift[2]
    pushed = cx * force[0] + cy * force[1] + cz * force[2]
    speed_squared = drift[0] * drift[0] + drift[1] * drift[1] + drift[2] * drift[2]
    work_done = drift[0] * force[0] + drift[1] * force[1] + drift[2] * force[2]
    balance = spread * rho * (1.0 + 3.0 * along + 4.5 * along * along - 1.5 * speed_squared)
    guo_term = spread * (3.0 * (pushed - work_done) + 9.0 * along * pushed)
    relax_table = jnp.asarray(relaxing, dtype=jnp.float32)
    source_table = jnp.asarray(forcing_map, dtype=jnp.float32)
    table = jnp.concatenate([relax_table, -source_table], axis=1)
    stacked = jnp.concatenate([f - balance, guo_term], axis=0)
    return f - jnp.einsum("pq,q...->p...", table, stacked, precision=lax.Precision.HIGH)


def stream_and_render(collided, velocities, extent_x, extent_y, length_x):
    near_y, band, far_y = collided
    depth_z = band.shape[3]
    edge = near_y.shape[2]
    steps = [[int(v) for v in velocities[q]] for q in range(19)]

    def kernel(near_ref, band_ref, far_ref, o_ref, pic_ref, c_ref):
        def gather(q, carry):
            c_ref[q, :, 0:edge] = near_ref[q]
            c_ref[q, :, edge : edge + extent_y - 2] = band_ref[q]
            c_ref[q, :, edge + extent_y - 2 :] = far_ref[q]
            return carry

        lax.fori_loop(0, 19, gather, 0)
        for q in range(19):
            cx, cy, cz = steps[q]

            def move(x, carry):
                v = c_ref[q, x + 1 - cx, pl.ds(1 - cy, extent_y), :]
                if cz != 0:
                    v = pltpu.roll(v, shift=cz % depth_z, axis=1)
                o_ref[q, x] = v
                return carry

            lax.fori_loop(0, extent_x, move, 0, unroll=True)

        def render(x, carry):
            depth, red, green, blue = carry
            fresh_density = o_ref[0, x]
            for q in range(1, 19):
                fresh_density = fresh_density + o_ref[q, x]
            extinction = optical * fresh_density / length_x
            weight = jnp.exp(-depth) * (1.0 - jnp.exp(-extinction))
            red = red + weight * (fresh_density / (1.0 + fresh_density))
            green = green + weight * jnp.exp(-fresh_density)
            blue = blue + weight * (0.5 * (1.0 + jnp.tanh(2.0 * (fresh_density - 1.0))))
            return (depth + extinction, red, green, blue)

        zero = jnp.zeros((extent_y, depth_z), jnp.float32)
        depth, red, green, blue = lax.fori_loop(0, extent_x, render, (zero, zero, zero, zero), unroll=True)
        pic_ref[0] = red
        pic_ref[1] = green
        pic_ref[2] = blue
        pic_ref[3] = 1.0 - jnp.exp(-depth)

    return pl.pallas_call(
        kernel,
        out_shape=(
            jax.ShapeDtypeStruct((19, extent_x, extent_y, depth_z), jnp.float32),
            jax.ShapeDtypeStruct((4, extent_y, depth_z), jnp.float32),
        ),
        in_specs=[pl.BlockSpec(memory_space=pltpu.VMEM)] * 3,
        out_specs=(pl.BlockSpec(memory_space=pltpu.VMEM), pl.BlockSpec(memory_space=pltpu.VMEM)),
        scratch_shapes=[pltpu.VMEM((19, extent_x + 2, extent_y + 2, depth_z), jnp.float32)],
    )(near_y, band, far_y)


def collide_region(cells, pot, tables):
    velocities, weights, relaxing, forcing_map = tables
    nx, ny = cells.shape[1], cells.shape[2]
    centre = pot[1 : 1 + nx, 1 : 1 + ny]
    totals = [jnp.zeros_like(centre), jnp.zeros_like(centre), jnp.zeros_like(centre)]
    for q in range(1, 19):
        steps = [int(v) for v in velocities[q]]
        neighbour = pot[1 + steps[0] : 1 + steps[0] + nx, 1 + steps[1] : 1 + steps[1] + ny]
        neighbour = jnp.roll(neighbour, -steps[2], axis=2)
        for d in range(3):
            if steps[d] != 0:
                totals[d] = totals[d] + weights[q] * steps[d] * neighbour
    force = [-cohesion * centre * totals[d] for d in range(3)]
    rho = jnp.sum(cells, axis=0)
    return collide_major(cells, rho, force, velocities, weights, relaxing, forcing_map)


def body(populations):
    velocities, weights, relaxing, forcing_map = lattice_tables()
    extent_x = populations.shape[0]
    extent_y = populations.shape[1]
    f = jnp.transpose(populations, (2, 0, 1, 3))
    potential = 1.0 - jnp.exp(-jnp.sum(f, axis=0))
    to_next = jnp.concatenate([f[:, extent_x - 1], potential[extent_x - 1 : extent_x], potential[extent_x - 2 : extent_x - 1]])
    to_prev = jnp.concatenate([f[:, 0], potential[0:1], potential[1:2]])
    from_prev = shift_ring(to_next, "gx", -1)
    from_next = shift_ring(to_prev, "gx", 1)
    fx = jnp.concatenate([from_prev[None, :19].transpose(1, 0, 2, 3), f, from_next[None, :19].transpose(1, 0, 2, 3)], axis=1)
    px = jnp.concatenate([from_prev[20:21], from_prev[19:20], potential, from_next[19:20], from_next[20:21]], axis=0)
    zero_x = jnp.zeros((19, 1, fx.shape[3]), f.dtype)

    def y_message(row_pop, row_near, row_far):
        pops = jnp.concatenate([zero_x, fx[:, :, row_pop], zero_x], axis=1)
        return jnp.concatenate([pops, px[None, :, row_near], px[None, :, row_far]], axis=0)

    from_below = shift_ring(y_message(extent_y - 1, extent_y - 1, extent_y - 2), "gy", -1)
    from_above = shift_ring(y_message(0, 0, 1), "gy", 1)
    fxy = jnp.concatenate(
        [from_below[:19, 1:-1, None], fx, from_above[:19, 1:-1, None]], axis=2
    )
    pxy = jnp.concatenate(
        [from_below[20][:, None], from_below[19][:, None], px, from_above[19][:, None], from_above[20][:, None]],
        axis=1,
    )
    tables = (velocities, weights, relaxing, forcing_map)
    inner = collide_region(f[:, 1 : extent_x - 1, 1 : extent_y - 1], potential, tables)
    near_x = collide_region(fx[:, 0:2, 1 : extent_y - 1], px[0:4], tables)
    far_x = collide_region(fx[:, extent_x : extent_x + 2, 1 : extent_y - 1], px[extent_x : extent_x + 4], tables)
    band = jnp.concatenate([near_x, inner, far_x], axis=1)
    near_y = collide_region(fxy[:, :, 0:2], pxy[:, 0:4], tables)
    far_y = collide_region(fxy[:, :, extent_y : extent_y + 2], pxy[:, extent_y : extent_y + 4], tables)
    collided = (near_y, band, far_y)
    groups = lax.axis_size("gx")
    length_x = extent_x * groups
    fresh_major, layered = stream_and_render(collided, velocities, extent_x, extent_y, length_x)
    fresh = jnp.transpose(fresh_major, (1, 2, 0, 3))
    depth_z = layered.shape[2]
    block_len = depth_z // groups
    blocked = layered.reshape(4, extent_y, groups, block_len)
    position = lax.axis_index("gx")
    current = blocked
    for level in range(groups.bit_length() - 1):
        parity = position // (1 << level) % 2
        halves = current.shape[2] // 2
        paired = current.reshape(4, extent_y, halves, 2, block_len)
        lower = paired[:, :, :, 0]
        upper = paired[:, :, :, 1]
        kept = jnp.where(parity == 1, upper, lower)
        handed = jnp.where(parity == 1, lower, upper)
        partner = from_partner(handed, "gx", level)
        nearer = jnp.where(parity == 0, kept, partner)
        farther = jnp.where(parity == 0, partner, kept)
        current = nearer + (1.0 - nearer[3:4]) * farther
    picture = current.reshape(4, extent_y, block_len)
    return (fresh, picture)


def solution(mesh):
    placed = (P("gx", "gy", None, None),)
    return jax.shard_map(
        body,
        mesh=mesh,
        in_specs=placed,
        out_specs=(P("gx", "gy", None, None), P(None, "gy", "gx")),
        check_vma=False,
    )
```

```python
import jax
import jax.numpy as jnp
import numpy as np
from jax import lax
from jax.sharding import PartitionSpec as P
from jax.experimental import pallas as pl
from jax.experimental.pallas import tpu as pltpu

cohesion = -6.0
optical = 2.0


def extended(cells, sides, width):
    for axis, dim in sides:
        count = lax.axis_size(axis)
        head = lax.slice_in_dim(cells, 0, width, axis=dim)
        tail = lax.slice_in_dim(cells, cells.shape[dim] - width, cells.shape[dim], axis=dim)
        cells = jnp.concatenate(
            [
                lax.ppermute(tail, axis, [(i, (i + 1) % count) for i in range(count)]),
                cells,
                lax.ppermute(head, axis, [((i + 1) % count, i) for i in range(count)]),
            ],
            axis=dim,
        )
    return cells


def from_partner(x, axis, distance):
    return lax.ppermute(x, axis, [(i, i ^ 1 << distance) for i in range(lax.axis_size(axis))])


def lattice_tables():
    velocities = np.array(
        [
            [0, 0, 0],
            [1, 0, 0],
            [-1, 0, 0],
            [0, 1, 0],
            [0, -1, 0],
            [0, 0, 1],
            [0, 0, -1],
            [1, 1, 0],
            [-1, -1, 0],
            [1, -1, 0],
            [-1, 1, 0],
            [1, 0, 1],
            [-1, 0, -1],
            [1, 0, -1],
            [-1, 0, 1],
            [0, 1, 1],
            [0, -1, -1],
            [0, 1, -1],
            [0, -1, 1],
        ]
    )
    weights = np.array([1.0 / 3.0] + [1.0 / 18.0] * 6 + [1.0 / 36.0] * 12)
    along_x = velocities[:, 0] * 1.0
    along_y = velocities[:, 1] * 1.0
    along_z = velocities[:, 2] * 1.0
    squared = along_x * along_x + along_y * along_y + along_z * along_z
    moment_rows = [
        np.ones(19),
        19.0 * squared - 30.0,
        (21.0 * squared * squared - 53.0 * squared + 24.0) / 2.0,
        along_x,
        (5.0 * squared - 9.0) * along_x,
        along_y,
        (5.0 * squared - 9.0) * along_y,
        along_z,
        (5.0 * squared - 9.0) * along_z,
        3.0 * along_x * along_x - squared,
        (3.0 * squared - 5.0) * (3.0 * along_x * along_x - squared),
        along_y * along_y - along_z * along_z,
        (3.0 * squared - 5.0) * (along_y * along_y - along_z * along_z),
        along_x * along_y,
        along_y * along_z,
        along_x * along_z,
        (along_y * along_y - along_z * along_z) * along_x,
        (along_z * along_z - along_x * along_x) * along_y,
        (along_x * along_x - along_y * along_y) * along_z,
    ]
    moments = np.stack(moment_rows)
    inverse = moments.T / np.sum(moments * moments, axis=1)
    relax_rates = np.array(
        [
            0.0,
            1.19,
            1.4,
            0.0,
            1.2,
            0.0,
            1.2,
            0.0,
            1.2,
            1.0,
            1.4,
            1.0,
            1.4,
            1.0,
            1.0,
            1.0,
            1.98,
            1.98,
            1.98,
        ]
    )
    relaxing = inverse @ (relax_rates[:, None] * moments)
    forcing_map = inverse @ ((1.0 - 0.5 * relax_rates)[:, None] * moments)
    return (velocities, weights, relaxing, forcing_map)


def collide(populations, density, forcing, velocities, weights, relaxing, forcing_map):
    lattice = jnp.asarray(velocities, dtype=jnp.float32)
    spread = jnp.asarray(weights, dtype=jnp.float32)[None, None, :, None]
    relax_table = jnp.asarray(relaxing, dtype=jnp.float32)
    source_table = jnp.asarray(forcing_map, dtype=jnp.float32)
    momentum = jnp.einsum("qd,xyqz->dxyz", lattice, populations, precision=lax.Precision.HIGHEST)
    drift = (momentum + 0.5 * forcing) / density[None]
    along = jnp.einsum("qd,dxyz->xyqz", lattice, drift, precision=lax.Precision.HIGHEST)
    pushed = jnp.einsum("qd,dxyz->xyqz", lattice, forcing, precision=lax.Precision.HIGHEST)
    speed_squared = jnp.sum(drift * drift, axis=0)[:, :, None, :]
    work_done = jnp.sum(drift * forcing, axis=0)[:, :, None, :]
    balance = (
        spread
        * density[:, :, None, :]
        * (1.0 + 3.0 * along + 4.5 * along * along - 1.5 * speed_squared)
    )
    guo_term = spread * (3.0 * (pushed - work_done) + 9.0 * along * pushed)
    relaxed = jnp.einsum(
        "pq,xyqz->xypz", relax_table, populations - balance, precision=lax.Precision.HIGHEST
    )
    sourced = jnp.einsum("pq,xyqz->xypz", source_table, guo_term, precision=lax.Precision.HIGHEST)
    return populations - relaxed + sourced


def attraction(padded, offset, extent_x, extent_y, velocities, weights):
    centre = padded[offset : offset + extent_x, offset : offset + extent_y]
    totals = [jnp.zeros_like(centre), jnp.zeros_like(centre), jnp.zeros_like(centre)]
    for q in range(1, 19):
        steps = [int(v) for v in velocities[q]]
        start_x = offset + steps[0]
        start_y = offset + steps[1]
        neighbour = padded[start_x : start_x + extent_x, start_y : start_y + extent_y]
        neighbour = jnp.roll(neighbour, -steps[2], axis=2)
        for d in range(3):
            if steps[d] != 0:
                totals[d] = totals[d] + weights[q] * steps[d] * neighbour
    return jnp.stack([-cohesion * centre * totals[d] for d in range(3)])


def palette(density):
    reds = density / (1.0 + density)
    greens = jnp.exp(-density)
    blues = 0.5 * (1.0 + jnp.tanh(2.0 * (density - 1.0)))
    return (reds, greens, blues)


def shift_ring(x, axis, step):
    count = lax.axis_size(axis)
    return lax.ppermute(x, axis, [(i, (i - step) % count) for i in range(count)])


def collide_major(f, rho, force, velocities, weights, relaxing, forcing_map):
    lattice = velocities.astype(np.float32)
    extra = (1,) * rho.ndim
    cx = jnp.asarray(lattice[:, 0]).reshape((19,) + extra)
    cy = jnp.asarray(lattice[:, 1]).reshape((19,) + extra)
    cz = jnp.asarray(lattice[:, 2]).reshape((19,) + extra)
    spread = jnp.asarray(weights.astype(np.float32)).reshape((19,) + extra)
    momentum = [
        sum(f[q] * float(velocities[q][d]) for q in range(19) if velocities[q][d] != 0)
        for d in range(3)
    ]
    drift = [(momentum[d] + 0.5 * force[d]) / rho for d in range(3)]
    along = cx * drift[0] + cy * drift[1] + cz * drift[2]
    pushed = cx * force[0] + cy * force[1] + cz * force[2]
    speed_squared = drift[0] * drift[0] + drift[1] * drift[1] + drift[2] * drift[2]
    work_done = drift[0] * force[0] + drift[1] * force[1] + drift[2] * force[2]
    balance = spread * rho * (1.0 + 3.0 * along + 4.5 * along * along - 1.5 * speed_squared)
    guo_term = spread * (3.0 * (pushed - work_done) + 9.0 * along * pushed)
    relax_table = jnp.asarray(relaxing, dtype=jnp.float32)
    source_table = jnp.asarray(forcing_map, dtype=jnp.float32)
    table = jnp.concatenate([relax_table, -source_table], axis=1)
    stacked = jnp.concatenate([f - balance, guo_term], axis=0)
    return f - jnp.einsum("pq,q...->p...", table, stacked, precision=lax.Precision.HIGH)


def stream_and_render(collided, velocities, extent_x, extent_y, length_x):
    near_y, band, far_y = collided
    depth_z = band.shape[3]
    edge = near_y.shape[2]
    steps = [[int(v) for v in velocities[q]] for q in range(19)]

    def kernel(near_ref, band_ref, far_ref, o_ref, pic_ref, c_ref):
        def gather(q, carry):
            c_ref[q, :, 0:edge] = near_ref[q]
            c_ref[q, :, edge : edge + extent_y - 2] = band_ref[q]
            c_ref[q, :, edge + extent_y - 2 :] = far_ref[q]
            return carry

        lax.fori_loop(0, 19, gather, 0)
        for q in range(19):
            cx, cy, cz = steps[q]

            def move(x, carry):
                v = c_ref[q, x + 1 - cx, pl.ds(1 - cy, extent_y), :]
                if cz != 0:
                    v = pltpu.roll(v, shift=cz % depth_z, axis=1)
                o_ref[q, x] = v
                return carry

            lax.fori_loop(0, extent_x, move, 0, unroll=True)

        def render(x, carry):
            depth, red, green, blue = carry
            fresh_density = o_ref[0, x]
            for q in range(1, 19):
                fresh_density = fresh_density + o_ref[q, x]
            extinction = optical * fresh_density / length_x
            weight = jnp.exp(-depth) * (1.0 - jnp.exp(-extinction))
            red = red + weight * (fresh_density / (1.0 + fresh_density))
            green = green + weight * jnp.exp(-fresh_density)
            blue = blue + weight * (0.5 * (1.0 + jnp.tanh(2.0 * (fresh_density - 1.0))))
            return (depth + extinction, red, green, blue)

        zero = jnp.zeros((extent_y, depth_z), jnp.float32)
        depth, red, green, blue = lax.fori_loop(0, extent_x, render, (zero, zero, zero, zero), unroll=True)
        pic_ref[0] = red
        pic_ref[1] = green
        pic_ref[2] = blue
        pic_ref[3] = 1.0 - jnp.exp(-depth)

    return pl.pallas_call(
        kernel,
        out_shape=(
            jax.ShapeDtypeStruct((19, extent_x, extent_y, depth_z), jnp.float32),
            jax.ShapeDtypeStruct((4, extent_y, depth_z), jnp.float32),
        ),
        in_specs=[pl.BlockSpec(memory_space=pltpu.VMEM)] * 3,
        out_specs=(pl.BlockSpec(memory_space=pltpu.VMEM), pl.BlockSpec(memory_space=pltpu.VMEM)),
        scratch_shapes=[pltpu.VMEM((19, extent_x + 2, extent_y + 2, depth_z), jnp.float32)],
    )(near_y, band, far_y)


def collide_region(cells, pot, tables):
    velocities, weights, relaxing, forcing_map = tables
    nx, ny = cells.shape[-3], cells.shape[-2]
    pot = pot.reshape((-1,) + pot.shape[-3:])
    centre = pot[:, 1 : 1 + nx, 1 : 1 + ny]
    totals = [jnp.zeros_like(centre), jnp.zeros_like(centre), jnp.zeros_like(centre)]
    for q in range(1, 19):
        steps = [int(v) for v in velocities[q]]
        neighbour = pot[:, 1 + steps[0] : 1 + steps[0] + nx, 1 + steps[1] : 1 + steps[1] + ny]
        neighbour = jnp.roll(neighbour, -steps[2], axis=3)
        for d in range(3):
            if steps[d] != 0:
                totals[d] = totals[d] + weights[q] * steps[d] * neighbour
    rho = jnp.sum(cells, axis=0)
    force = [(-cohesion * centre * totals[d]).reshape(rho.shape) for d in range(3)]
    return collide_major(cells, rho, force, velocities, weights, relaxing, forcing_map)


def body(populations):
    velocities, weights, relaxing, forcing_map = lattice_tables()
    extent_x = populations.shape[0]
    extent_y = populations.shape[1]
    f = jnp.transpose(populations, (2, 0, 1, 3))
    potential = 1.0 - jnp.exp(-jnp.sum(f, axis=0))
    to_next = jnp.concatenate([f[:, extent_x - 1], potential[extent_x - 1 : extent_x], potential[extent_x - 2 : extent_x - 1]])
    to_prev = jnp.concatenate([f[:, 0], potential[0:1], potential[1:2]])
    from_prev = shift_ring(to_next, "gx", -1)
    from_next = shift_ring(to_prev, "gx", 1)
    fx = jnp.concatenate([from_prev[None, :19].transpose(1, 0, 2, 3), f, from_next[None, :19].transpose(1, 0, 2, 3)], axis=1)
    px = jnp.concatenate([from_prev[20:21], from_prev[19:20], potential, from_next[19:20], from_next[20:21]], axis=0)
    zero_x = jnp.zeros((19, 1, fx.shape[3]), f.dtype)

    def y_message(row_pop, row_near, row_far):
        pops = jnp.concatenate([zero_x, fx[:, :, row_pop], zero_x], axis=1)
        return jnp.concatenate([pops, px[None, :, row_near], px[None, :, row_far]], axis=0)

    from_below = shift_ring(y_message(extent_y - 1, extent_y - 1, extent_y - 2), "gy", -1)
    from_above = shift_ring(y_message(0, 0, 1), "gy", 1)
    fxy = jnp.concatenate(
        [from_below[:19, 1:-1, None], fx, from_above[:19, 1:-1, None]], axis=2
    )
    pxy = jnp.concatenate(
        [from_below[20][:, None], from_below[19][:, None], px, from_above[19][:, None], from_above[20][:, None]],
        axis=1,
    )
    tables = (velocities, weights, relaxing, forcing_map)
    inner = collide_region(f[:, 1 : extent_x - 1, 1 : extent_y - 1], potential, tables)
    near_x = collide_region(fx[:, 0:2, 1 : extent_y - 1], px[0:4], tables)
    far_x = collide_region(fx[:, extent_x : extent_x + 2, 1 : extent_y - 1], px[extent_x : extent_x + 4], tables)
    band = jnp.concatenate([near_x, inner, far_x], axis=1)
    pair = collide_region(
        jnp.stack([fxy[:, :, 0:2], fxy[:, :, extent_y : extent_y + 2]], axis=1),
        jnp.stack([pxy[:, 0:4], pxy[:, extent_y : extent_y + 4]]),
        tables,
    )
    near_y = pair[:, 0]
    far_y = pair[:, 1]
    collided = (near_y, band, far_y)
    groups = lax.axis_size("gx")
    length_x = extent_x * groups
    fresh_major, layered = stream_and_render(collided, velocities, extent_x, extent_y, length_x)
    fresh = jnp.transpose(fresh_major, (1, 2, 0, 3))
    depth_z = layered.shape[2]
    block_len = depth_z // groups
    blocked = layered.reshape(4, extent_y, groups, block_len)
    position = lax.axis_index("gx")
    current = blocked
    for level in range(groups.bit_length() - 1):
        parity = position // (1 << level) % 2
        halves = current.shape[2] // 2
        paired = current.reshape(4, extent_y, halves, 2, block_len)
        lower = paired[:, :, :, 0]
        upper = paired[:, :, :, 1]
        kept = jnp.where(parity == 1, upper, lower)
        handed = jnp.where(parity == 1, lower, upper)
        partner = from_partner(handed, "gx", level)
        nearer = jnp.where(parity == 0, kept, partner)
        farther = jnp.where(parity == 0, partner, kept)
        current = nearer + (1.0 - nearer[3:4]) * farther
    picture = current.reshape(4, extent_y, block_len)
    return (fresh, picture)


def solution(mesh):
    placed = (P("gx", "gy", None, None),)
    return jax.shard_map(
        body,
        mesh=mesh,
        in_specs=placed,
        out_specs=(P("gx", "gy", None, None), P(None, "gy", "gx")),
        check_vma=False,
    )
```

```python
import jax
import jax.numpy as jnp
import numpy as np
from jax import lax
from jax.sharding import PartitionSpec as P
from jax.experimental import pallas as pl
from jax.experimental.pallas import tpu as pltpu

cohesion = -6.0
optical = 2.0


def extended(cells, sides, width):
    for axis, dim in sides:
        count = lax.axis_size(axis)
        head = lax.slice_in_dim(cells, 0, width, axis=dim)
        tail = lax.slice_in_dim(cells, cells.shape[dim] - width, cells.shape[dim], axis=dim)
        cells = jnp.concatenate(
            [
                lax.ppermute(tail, axis, [(i, (i + 1) % count) for i in range(count)]),
                cells,
                lax.ppermute(head, axis, [((i + 1) % count, i) for i in range(count)]),
            ],
            axis=dim,
        )
    return cells


def from_partner(x, axis, distance):
    return lax.ppermute(x, axis, [(i, i ^ 1 << distance) for i in range(lax.axis_size(axis))])


def lattice_tables():
    velocities = np.array(
        [
            [0, 0, 0],
            [1, 0, 0],
            [-1, 0, 0],
            [0, 1, 0],
            [0, -1, 0],
            [0, 0, 1],
            [0, 0, -1],
            [1, 1, 0],
            [-1, -1, 0],
            [1, -1, 0],
            [-1, 1, 0],
            [1, 0, 1],
            [-1, 0, -1],
            [1, 0, -1],
            [-1, 0, 1],
            [0, 1, 1],
            [0, -1, -1],
            [0, 1, -1],
            [0, -1, 1],
        ]
    )
    weights = np.array([1.0 / 3.0] + [1.0 / 18.0] * 6 + [1.0 / 36.0] * 12)
    along_x = velocities[:, 0] * 1.0
    along_y = velocities[:, 1] * 1.0
    along_z = velocities[:, 2] * 1.0
    squared = along_x * along_x + along_y * along_y + along_z * along_z
    moment_rows = [
        np.ones(19),
        19.0 * squared - 30.0,
        (21.0 * squared * squared - 53.0 * squared + 24.0) / 2.0,
        along_x,
        (5.0 * squared - 9.0) * along_x,
        along_y,
        (5.0 * squared - 9.0) * along_y,
        along_z,
        (5.0 * squared - 9.0) * along_z,
        3.0 * along_x * along_x - squared,
        (3.0 * squared - 5.0) * (3.0 * along_x * along_x - squared),
        along_y * along_y - along_z * along_z,
        (3.0 * squared - 5.0) * (along_y * along_y - along_z * along_z),
        along_x * along_y,
        along_y * along_z,
        along_x * along_z,
        (along_y * along_y - along_z * along_z) * along_x,
        (along_z * along_z - along_x * along_x) * along_y,
        (along_x * along_x - along_y * along_y) * along_z,
    ]
    moments = np.stack(moment_rows)
    inverse = moments.T / np.sum(moments * moments, axis=1)
    relax_rates = np.array(
        [
            0.0,
            1.19,
            1.4,
            0.0,
            1.2,
            0.0,
            1.2,
            0.0,
            1.2,
            1.0,
            1.4,
            1.0,
            1.4,
            1.0,
            1.0,
            1.0,
            1.98,
            1.98,
            1.98,
        ]
    )
    relaxing = inverse @ (relax_rates[:, None] * moments)
    forcing_map = inverse @ ((1.0 - 0.5 * relax_rates)[:, None] * moments)
    return (velocities, weights, relaxing, forcing_map)


def collide(populations, density, forcing, velocities, weights, relaxing, forcing_map):
    lattice = jnp.asarray(velocities, dtype=jnp.float32)
    spread = jnp.asarray(weights, dtype=jnp.float32)[None, None, :, None]
    relax_table = jnp.asarray(relaxing, dtype=jnp.float32)
    source_table = jnp.asarray(forcing_map, dtype=jnp.float32)
    momentum = jnp.einsum("qd,xyqz->dxyz", lattice, populations, precision=lax.Precision.HIGHEST)
    drift = (momentum + 0.5 * forcing) / density[None]
    along = jnp.einsum("qd,dxyz->xyqz", lattice, drift, precision=lax.Precision.HIGHEST)
    pushed = jnp.einsum("qd,dxyz->xyqz", lattice, forcing, precision=lax.Precision.HIGHEST)
    speed_squared = jnp.sum(drift * drift, axis=0)[:, :, None, :]
    work_done = jnp.sum(drift * forcing, axis=0)[:, :, None, :]
    balance = (
        spread
        * density[:, :, None, :]
        * (1.0 + 3.0 * along + 4.5 * along * along - 1.5 * speed_squared)
    )
    guo_term = spread * (3.0 * (pushed - work_done) + 9.0 * along * pushed)
    relaxed = jnp.einsum(
        "pq,xyqz->xypz", relax_table, populations - balance, precision=lax.Precision.HIGHEST
    )
    sourced = jnp.einsum("pq,xyqz->xypz", source_table, guo_term, precision=lax.Precision.HIGHEST)
    return populations - relaxed + sourced


def attraction(padded, offset, extent_x, extent_y, velocities, weights):
    centre = padded[offset : offset + extent_x, offset : offset + extent_y]
    totals = [jnp.zeros_like(centre), jnp.zeros_like(centre), jnp.zeros_like(centre)]
    for q in range(1, 19):
        steps = [int(v) for v in velocities[q]]
        start_x = offset + steps[0]
        start_y = offset + steps[1]
        neighbour = padded[start_x : start_x + extent_x, start_y : start_y + extent_y]
        neighbour = jnp.roll(neighbour, -steps[2], axis=2)
        for d in range(3):
            if steps[d] != 0:
                totals[d] = totals[d] + weights[q] * steps[d] * neighbour
    return jnp.stack([-cohesion * centre * totals[d] for d in range(3)])


def palette(density):
    reds = density / (1.0 + density)
    greens = jnp.exp(-density)
    blues = 0.5 * (1.0 + jnp.tanh(2.0 * (density - 1.0)))
    return (reds, greens, blues)


def shift_ring(x, axis, step):
    count = lax.axis_size(axis)
    return lax.ppermute(x, axis, [(i, (i - step) % count) for i in range(count)])


def collide_major(f, rho, force, velocities, weights, relaxing, forcing_map):
    lattice = velocities.astype(np.float32)
    extra = (1,) * rho.ndim
    cx = jnp.asarray(lattice[:, 0]).reshape((19,) + extra)
    cy = jnp.asarray(lattice[:, 1]).reshape((19,) + extra)
    cz = jnp.asarray(lattice[:, 2]).reshape((19,) + extra)
    spread = jnp.asarray(weights.astype(np.float32)).reshape((19,) + extra)
    momentum = [
        sum(f[q] * float(velocities[q][d]) for q in range(19) if velocities[q][d] != 0)
        for d in range(3)
    ]
    drift = [(momentum[d] + 0.5 * force[d]) / rho for d in range(3)]
    along = cx * drift[0] + cy * drift[1] + cz * drift[2]
    pushed = cx * force[0] + cy * force[1] + cz * force[2]
    speed_squared = drift[0] * drift[0] + drift[1] * drift[1] + drift[2] * drift[2]
    work_done = drift[0] * force[0] + drift[1] * force[1] + drift[2] * force[2]
    balance = spread * rho * (1.0 + 3.0 * along + 4.5 * along * along - 1.5 * speed_squared)
    guo_term = spread * (3.0 * (pushed - work_done) + 9.0 * along * pushed)
    relax_table = jnp.asarray(relaxing, dtype=jnp.float32)
    source_table = jnp.asarray(forcing_map, dtype=jnp.float32)
    table = jnp.concatenate([relax_table, -source_table], axis=1)
    stacked = jnp.concatenate([f - balance, guo_term], axis=0)
    return f - jnp.einsum("pq,q...->p...", table, stacked, precision=lax.Precision.HIGH)


def stream_and_render(collided, velocities, extent_x, extent_y, length_x):
    near_y, band, far_y = collided
    depth_z = band.shape[3]
    edge = near_y.shape[2]
    steps = [[int(v) for v in velocities[q]] for q in range(19)]

    def kernel(near_ref, band_ref, far_ref, o_ref, pic_ref, c_ref):
        def gather(q, carry):
            c_ref[q, :, 0:edge] = near_ref[q]
            c_ref[q, :, edge : edge + extent_y - 2] = band_ref[q]
            c_ref[q, :, edge + extent_y - 2 :] = far_ref[q]
            return carry

        lax.fori_loop(0, 19, gather, 0)
        for q in range(19):
            cx, cy, cz = steps[q]

            def move(x, carry):
                v = c_ref[q, x + 1 - cx, pl.ds(1 - cy, extent_y), :]
                if cz != 0:
                    v = pltpu.roll(v, shift=cz % depth_z, axis=1)
                o_ref[q, x] = v
                return carry

            lax.fori_loop(0, extent_x, move, 0, unroll=True)

        def render(x, carry):
            depth, red, green, blue = carry
            fresh_density = o_ref[0, x]
            for q in range(1, 19):
                fresh_density = fresh_density + o_ref[q, x]
            extinction = optical * fresh_density / length_x
            weight = jnp.exp(-depth) * (1.0 - jnp.exp(-extinction))
            red = red + weight * (fresh_density / (1.0 + fresh_density))
            green = green + weight * jnp.exp(-fresh_density)
            blue = blue + weight * (0.5 * (1.0 + jnp.tanh(2.0 * (fresh_density - 1.0))))
            return (depth + extinction, red, green, blue)

        zero = jnp.zeros((extent_y, depth_z), jnp.float32)
        depth, red, green, blue = lax.fori_loop(0, extent_x, render, (zero, zero, zero, zero), unroll=True)
        pic_ref[0] = red
        pic_ref[1] = green
        pic_ref[2] = blue
        pic_ref[3] = 1.0 - jnp.exp(-depth)

    return pl.pallas_call(
        kernel,
        out_shape=(
            jax.ShapeDtypeStruct((19, extent_x, extent_y, depth_z), jnp.float32),
            jax.ShapeDtypeStruct((4, extent_y, depth_z), jnp.float32),
        ),
        in_specs=[pl.BlockSpec(memory_space=pltpu.VMEM)] * 3,
        out_specs=(pl.BlockSpec(memory_space=pltpu.VMEM), pl.BlockSpec(memory_space=pltpu.VMEM)),
        scratch_shapes=[pltpu.VMEM((19, extent_x + 2, extent_y + 2, depth_z), jnp.float32)],
    )(near_y, band, far_y)


def collide_region(cells, pot, tables):
    velocities, weights, relaxing, forcing_map = tables
    nx, ny = cells.shape[1], cells.shape[2]
    centre = pot[1 : 1 + nx, 1 : 1 + ny]
    totals = [jnp.zeros_like(centre), jnp.zeros_like(centre), jnp.zeros_like(centre)]
    for q in range(1, 19):
        steps = [int(v) for v in velocities[q]]
        neighbour = pot[1 + steps[0] : 1 + steps[0] + nx, 1 + steps[1] : 1 + steps[1] + ny]
        neighbour = jnp.roll(neighbour, -steps[2], axis=2)
        for d in range(3):
            if steps[d] != 0:
                totals[d] = totals[d] + weights[q] * steps[d] * neighbour
    force = [-cohesion * centre * totals[d] for d in range(3)]
    rho = jnp.sum(cells, axis=0)
    return collide_major(cells, rho, force, velocities, weights, relaxing, forcing_map)


def body(populations):
    velocities, weights, relaxing, forcing_map = lattice_tables()
    extent_x = populations.shape[0]
    extent_y = populations.shape[1]
    f = jnp.transpose(populations, (2, 0, 1, 3))
    potential = 1.0 - jnp.exp(-jnp.sum(f, axis=0))

    def edge(row):
        cells = jnp.transpose(populations[row], (1, 0, 2))
        return cells, 1.0 - jnp.exp(-jnp.sum(cells, axis=0, keepdims=True))

    last, last_pot = edge(extent_x - 1)
    first, first_pot = edge(0)
    to_next = jnp.concatenate([last, last_pot, edge(extent_x - 2)[1]])
    to_prev = jnp.concatenate([first, first_pot, edge(1)[1]])
    from_prev = shift_ring(to_next, "gx", -1)
    from_next = shift_ring(to_prev, "gx", 1)
    fx = jnp.concatenate([from_prev[None, :19].transpose(1, 0, 2, 3), f, from_next[None, :19].transpose(1, 0, 2, 3)], axis=1)
    px = jnp.concatenate([from_prev[20:21], from_prev[19:20], potential, from_next[19:20], from_next[20:21]], axis=0)
    zero_x = jnp.zeros((19, 1, fx.shape[3]), f.dtype)

    def y_message(row_pop, row_near, row_far):
        pops = jnp.concatenate([zero_x, fx[:, :, row_pop], zero_x], axis=1)
        return jnp.concatenate([pops, px[None, :, row_near], px[None, :, row_far]], axis=0)

    from_below = shift_ring(y_message(extent_y - 1, extent_y - 1, extent_y - 2), "gy", -1)
    from_above = shift_ring(y_message(0, 0, 1), "gy", 1)
    fxy = jnp.concatenate(
        [from_below[:19, 1:-1, None], fx, from_above[:19, 1:-1, None]], axis=2
    )
    pxy = jnp.concatenate(
        [from_below[20][:, None], from_below[19][:, None], px, from_above[19][:, None], from_above[20][:, None]],
        axis=1,
    )
    tables = (velocities, weights, relaxing, forcing_map)
    inner = collide_region(f[:, 1 : extent_x - 1, 1 : extent_y - 1], potential, tables)
    near_x = collide_region(fx[:, 0:2, 1 : extent_y - 1], px[0:4], tables)
    far_x = collide_region(fx[:, extent_x : extent_x + 2, 1 : extent_y - 1], px[extent_x : extent_x + 4], tables)
    band = jnp.concatenate([near_x, inner, far_x], axis=1)
    near_y = collide_region(fxy[:, :, 0:2], pxy[:, 0:4], tables)
    far_y = collide_region(fxy[:, :, extent_y : extent_y + 2], pxy[:, extent_y : extent_y + 4], tables)
    collided = (near_y, band, far_y)
    groups = lax.axis_size("gx")
    length_x = extent_x * groups
    fresh_major, layered = stream_and_render(collided, velocities, extent_x, extent_y, length_x)
    fresh = jnp.transpose(fresh_major, (1, 2, 0, 3))
    depth_z = layered.shape[2]
    block_len = depth_z // groups
    blocked = layered.reshape(4, extent_y, groups, block_len)
    position = lax.axis_index("gx")
    current = blocked
    for level in range(groups.bit_length() - 1):
        parity = position // (1 << level) % 2
        halves = current.shape[2] // 2
        paired = current.reshape(4, extent_y, halves, 2, block_len)
        lower = paired[:, :, :, 0]
        upper = paired[:, :, :, 1]
        kept = jnp.where(parity == 1, upper, lower)
        handed = jnp.where(parity == 1, lower, upper)
        partner = from_partner(handed, "gx", level)
        nearer = jnp.where(parity == 0, kept, partner)
        farther = jnp.where(parity == 0, partner, kept)
        current = nearer + (1.0 - nearer[3:4]) * farther
    picture = current.reshape(4, extent_y, block_len)
    return (fresh, picture)


def solution(mesh):
    placed = (P("gx", "gy", None, None),)
    return jax.shard_map(
        body,
        mesh=mesh,
        in_specs=placed,
        out_specs=(P("gx", "gy", None, None), P(None, "gy", "gx")),
        check_vma=False,
    )
```

```python
import jax
import jax.numpy as jnp
import numpy as np
from jax import lax
from jax.sharding import PartitionSpec as P
from jax.experimental import pallas as pl
from jax.experimental.pallas import tpu as pltpu

cohesion = -6.0
optical = 2.0


def extended(cells, sides, width):
    for axis, dim in sides:
        count = lax.axis_size(axis)
        head = lax.slice_in_dim(cells, 0, width, axis=dim)
        tail = lax.slice_in_dim(cells, cells.shape[dim] - width, cells.shape[dim], axis=dim)
        cells = jnp.concatenate(
            [
                lax.ppermute(tail, axis, [(i, (i + 1) % count) for i in range(count)]),
                cells,
                lax.ppermute(head, axis, [((i + 1) % count, i) for i in range(count)]),
            ],
            axis=dim,
        )
    return cells


def from_partner(x, axis, distance):
    return lax.ppermute(x, axis, [(i, i ^ 1 << distance) for i in range(lax.axis_size(axis))])


def lattice_tables():
    velocities = np.array(
        [
            [0, 0, 0],
            [1, 0, 0],
            [-1, 0, 0],
            [0, 1, 0],
            [0, -1, 0],
            [0, 0, 1],
            [0, 0, -1],
            [1, 1, 0],
            [-1, -1, 0],
            [1, -1, 0],
            [-1, 1, 0],
            [1, 0, 1],
            [-1, 0, -1],
            [1, 0, -1],
            [-1, 0, 1],
            [0, 1, 1],
            [0, -1, -1],
            [0, 1, -1],
            [0, -1, 1],
        ]
    )
    weights = np.array([1.0 / 3.0] + [1.0 / 18.0] * 6 + [1.0 / 36.0] * 12)
    along_x = velocities[:, 0] * 1.0
    along_y = velocities[:, 1] * 1.0
    along_z = velocities[:, 2] * 1.0
    squared = along_x * along_x + along_y * along_y + along_z * along_z
    moment_rows = [
        np.ones(19),
        19.0 * squared - 30.0,
        (21.0 * squared * squared - 53.0 * squared + 24.0) / 2.0,
        along_x,
        (5.0 * squared - 9.0) * along_x,
        along_y,
        (5.0 * squared - 9.0) * along_y,
        along_z,
        (5.0 * squared - 9.0) * along_z,
        3.0 * along_x * along_x - squared,
        (3.0 * squared - 5.0) * (3.0 * along_x * along_x - squared),
        along_y * along_y - along_z * along_z,
        (3.0 * squared - 5.0) * (along_y * along_y - along_z * along_z),
        along_x * along_y,
        along_y * along_z,
        along_x * along_z,
        (along_y * along_y - along_z * along_z) * along_x,
        (along_z * along_z - along_x * along_x) * along_y,
        (along_x * along_x - along_y * along_y) * along_z,
    ]
    moments = np.stack(moment_rows)
    inverse = moments.T / np.sum(moments * moments, axis=1)
    relax_rates = np.array(
        [
            0.0,
            1.19,
            1.4,
            0.0,
            1.2,
            0.0,
            1.2,
            0.0,
            1.2,
            1.0,
            1.4,
            1.0,
            1.4,
            1.0,
            1.0,
            1.0,
            1.98,
            1.98,
            1.98,
        ]
    )
    relaxing = inverse @ (relax_rates[:, None] * moments)
    forcing_map = inverse @ ((1.0 - 0.5 * relax_rates)[:, None] * moments)
    return (velocities, weights, relaxing, forcing_map)


def collide(populations, density, forcing, velocities, weights, relaxing, forcing_map):
    lattice = jnp.asarray(velocities, dtype=jnp.float32)
    spread = jnp.asarray(weights, dtype=jnp.float32)[None, None, :, None]
    relax_table = jnp.asarray(relaxing, dtype=jnp.float32)
    source_table = jnp.asarray(forcing_map, dtype=jnp.float32)
    momentum = jnp.einsum("qd,xyqz->dxyz", lattice, populations, precision=lax.Precision.HIGHEST)
    drift = (momentum + 0.5 * forcing) / density[None]
    along = jnp.einsum("qd,dxyz->xyqz", lattice, drift, precision=lax.Precision.HIGHEST)
    pushed = jnp.einsum("qd,dxyz->xyqz", lattice, forcing, precision=lax.Precision.HIGHEST)
    speed_squared = jnp.sum(drift * drift, axis=0)[:, :, None, :]
    work_done = jnp.sum(drift * forcing, axis=0)[:, :, None, :]
    balance = (
        spread
        * density[:, :, None, :]
        * (1.0 + 3.0 * along + 4.5 * along * along - 1.5 * speed_squared)
    )
    guo_term = spread * (3.0 * (pushed - work_done) + 9.0 * along * pushed)
    relaxed = jnp.einsum(
        "pq,xyqz->xypz", relax_table, populations - balance, precision=lax.Precision.HIGHEST
    )
    sourced = jnp.einsum("pq,xyqz->xypz", source_table, guo_term, precision=lax.Precision.HIGHEST)
    return populations - relaxed + sourced


def attraction(padded, offset, extent_x, extent_y, velocities, weights):
    centre = padded[offset : offset + extent_x, offset : offset + extent_y]
    totals = [jnp.zeros_like(centre), jnp.zeros_like(centre), jnp.zeros_like(centre)]
    for q in range(1, 19):
        steps = [int(v) for v in velocities[q]]
        start_x = offset + steps[0]
        start_y = offset + steps[1]
        neighbour = padded[start_x : start_x + extent_x, start_y : start_y + extent_y]
        neighbour = jnp.roll(neighbour, -steps[2], axis=2)
        for d in range(3):
            if steps[d] != 0:
                totals[d] = totals[d] + weights[q] * steps[d] * neighbour
    return jnp.stack([-cohesion * centre * totals[d] for d in range(3)])


def palette(density):
    reds = density / (1.0 + density)
    greens = jnp.exp(-density)
    blues = 0.5 * (1.0 + jnp.tanh(2.0 * (density - 1.0)))
    return (reds, greens, blues)


def shift_ring(x, axis, step):
    count = lax.axis_size(axis)
    return lax.ppermute(x, axis, [(i, (i - step) % count) for i in range(count)])


def collide_major(f, rho, force, velocities, weights, relaxing, forcing_map):
    lattice = velocities.astype(np.float32)
    extra = (1,) * rho.ndim
    cx = jnp.asarray(lattice[:, 0]).reshape((19,) + extra)
    cy = jnp.asarray(lattice[:, 1]).reshape((19,) + extra)
    cz = jnp.asarray(lattice[:, 2]).reshape((19,) + extra)
    spread = jnp.asarray(weights.astype(np.float32)).reshape((19,) + extra)
    momentum = [
        sum(f[q] * float(velocities[q][d]) for q in range(19) if velocities[q][d] != 0)
        for d in range(3)
    ]
    drift = [(momentum[d] + 0.5 * force[d]) / rho for d in range(3)]
    along = cx * drift[0] + cy * drift[1] + cz * drift[2]
    pushed = cx * force[0] + cy * force[1] + cz * force[2]
    speed_squared = drift[0] * drift[0] + drift[1] * drift[1] + drift[2] * drift[2]
    work_done = drift[0] * force[0] + drift[1] * force[1] + drift[2] * force[2]
    balance = spread * rho * (1.0 + 3.0 * along + 4.5 * along * along - 1.5 * speed_squared)
    guo_term = spread * (3.0 * (pushed - work_done) + 9.0 * along * pushed)
    relax_table = jnp.asarray(relaxing, dtype=jnp.float32)
    source_table = jnp.asarray(forcing_map, dtype=jnp.float32)
    table = jnp.concatenate([relax_table, -source_table], axis=1)
    stacked = jnp.concatenate([f - balance, guo_term], axis=0)
    return f - jnp.einsum("pq,q...->p...", table, stacked, precision=lax.Precision.HIGH)


def stream_and_render(collided, velocities, extent_x, extent_y, length_x):
    near_y, band, far_y = collided
    depth_z = band.shape[3]
    edge = near_y.shape[2]
    steps = [[int(v) for v in velocities[q]] for q in range(19)]

    def kernel(near_ref, band_ref, far_ref, o_ref, pic_ref, c_ref):
        def gather(q, carry):
            c_ref[q, :, 0:edge] = near_ref[q]
            c_ref[q, :, edge : edge + extent_y - 2] = band_ref[q]
            c_ref[q, :, edge + extent_y - 2 :] = far_ref[q]
            return carry

        lax.fori_loop(0, 19, gather, 0)
        for q in range(19):
            cx, cy, cz = steps[q]

            def move(x, carry):
                v = c_ref[q, x + 1 - cx, pl.ds(1 - cy, extent_y), :]
                if cz != 0:
                    v = pltpu.roll(v, shift=cz % depth_z, axis=1)
                o_ref[q, x] = v
                return carry

            lax.fori_loop(0, extent_x, move, 0, unroll=True)

        def render(x, carry):
            depth, red, green, blue = carry
            fresh_density = o_ref[0, x]
            for q in range(1, 19):
                fresh_density = fresh_density + o_ref[q, x]
            extinction = optical * fresh_density / length_x
            weight = jnp.exp(-depth) * (1.0 - jnp.exp(-extinction))
            red = red + weight * (fresh_density / (1.0 + fresh_density))
            green = green + weight * jnp.exp(-fresh_density)
            blue = blue + weight * (0.5 * (1.0 + jnp.tanh(2.0 * (fresh_density - 1.0))))
            return (depth + extinction, red, green, blue)

        zero = jnp.zeros((extent_y, depth_z), jnp.float32)
        depth, red, green, blue = lax.fori_loop(0, extent_x, render, (zero, zero, zero, zero), unroll=True)
        pic_ref[0] = red
        pic_ref[1] = green
        pic_ref[2] = blue
        pic_ref[3] = 1.0 - jnp.exp(-depth)

    return pl.pallas_call(
        kernel,
        out_shape=(
            jax.ShapeDtypeStruct((19, extent_x, extent_y, depth_z), jnp.float32),
            jax.ShapeDtypeStruct((4, extent_y, depth_z), jnp.float32),
        ),
        in_specs=[pl.BlockSpec(memory_space=pltpu.VMEM)] * 3,
        out_specs=(pl.BlockSpec(memory_space=pltpu.VMEM), pl.BlockSpec(memory_space=pltpu.VMEM)),
        scratch_shapes=[pltpu.VMEM((19, extent_x + 2, extent_y + 2, depth_z), jnp.float32)],
    )(near_y, band, far_y)


def collide_region(cells, pot, tables, swapped=False):
    velocities, weights, relaxing, forcing_map = tables
    nx, ny = cells.shape[1], cells.shape[2]
    centre = pot[1 : 1 + nx, 1 : 1 + ny]
    totals = [jnp.zeros_like(centre), jnp.zeros_like(centre), jnp.zeros_like(centre)]
    for q in range(1, 19):
        steps = [int(v) for v in velocities[q]]
        first, second = (steps[1], steps[0]) if swapped else (steps[0], steps[1])
        neighbour = pot[1 + first : 1 + first + nx, 1 + second : 1 + second + ny]
        neighbour = jnp.roll(neighbour, -steps[2], axis=2)
        for d in range(3):
            if steps[d] != 0:
                totals[d] = totals[d] + weights[q] * steps[d] * neighbour
    force = [-cohesion * centre * totals[d] for d in range(3)]
    rho = jnp.sum(cells, axis=0)
    return collide_major(cells, rho, force, velocities, weights, relaxing, forcing_map)


def body(populations):
    velocities, weights, relaxing, forcing_map = lattice_tables()
    extent_x = populations.shape[0]
    extent_y = populations.shape[1]
    f = jnp.transpose(populations, (2, 0, 1, 3))
    potential = 1.0 - jnp.exp(-jnp.sum(f, axis=0))
    to_next = jnp.concatenate([f[:, extent_x - 1], potential[extent_x - 1 : extent_x], potential[extent_x - 2 : extent_x - 1]])
    to_prev = jnp.concatenate([f[:, 0], potential[0:1], potential[1:2]])
    from_prev = shift_ring(to_next, "gx", -1)
    from_next = shift_ring(to_prev, "gx", 1)
    fx = jnp.concatenate([from_prev[None, :19].transpose(1, 0, 2, 3), f, from_next[None, :19].transpose(1, 0, 2, 3)], axis=1)
    px = jnp.concatenate([from_prev[20:21], from_prev[19:20], potential, from_next[19:20], from_next[20:21]], axis=0)
    zero_x = jnp.zeros((19, 1, fx.shape[3]), f.dtype)

    def y_message(row_pop, row_near, row_far):
        pops = jnp.concatenate([zero_x, fx[:, :, row_pop], zero_x], axis=1)
        return jnp.concatenate([pops, px[None, :, row_near], px[None, :, row_far]], axis=0)

    from_below = shift_ring(y_message(extent_y - 1, extent_y - 1, extent_y - 2), "gy", -1)
    from_above = shift_ring(y_message(0, 0, 1), "gy", 1)
    fxy = jnp.concatenate(
        [from_below[:19, 1:-1, None], fx, from_above[:19, 1:-1, None]], axis=2
    )
    pxy = jnp.concatenate(
        [from_below[20][:, None], from_below[19][:, None], px, from_above[19][:, None], from_above[20][:, None]],
        axis=1,
    )
    tables = (velocities, weights, relaxing, forcing_map)
    inner = collide_region(f[:, 1 : extent_x - 1, 1 : extent_y - 1], potential, tables)
    near_x = collide_region(fx[:, 0:2, 1 : extent_y - 1], px[0:4], tables)
    far_x = collide_region(fx[:, extent_x : extent_x + 2, 1 : extent_y - 1], px[extent_x : extent_x + 4], tables)
    band = jnp.concatenate([near_x, inner, far_x], axis=1)

    def strip(lo, hi):
        cells = jnp.swapaxes(fxy[:, :, lo:hi], 1, 2)
        pot = jnp.swapaxes(pxy[:, lo : hi + 2], 0, 1)
        return jnp.swapaxes(collide_region(cells, pot, tables, swapped=True), 1, 2)

    near_y = strip(0, 2)
    far_y = strip(extent_y, extent_y + 2)
    collided = (near_y, band, far_y)
    groups = lax.axis_size("gx")
    length_x = extent_x * groups
    fresh_major, layered = stream_and_render(collided, velocities, extent_x, extent_y, length_x)
    fresh = jnp.transpose(fresh_major, (1, 2, 0, 3))
    depth_z = layered.shape[2]
    block_len = depth_z // groups
    blocked = layered.reshape(4, extent_y, groups, block_len)
    position = lax.axis_index("gx")
    current = blocked
    for level in range(groups.bit_length() - 1):
        parity = position // (1 << level) % 2
        halves = current.shape[2] // 2
        paired = current.reshape(4, extent_y, halves, 2, block_len)
        lower = paired[:, :, :, 0]
        upper = paired[:, :, :, 1]
        kept = jnp.where(parity == 1, upper, lower)
        handed = jnp.where(parity == 1, lower, upper)
        partner = from_partner(handed, "gx", level)
        nearer = jnp.where(parity == 0, kept, partner)
        farther = jnp.where(parity == 0, partner, kept)
        current = nearer + (1.0 - nearer[3:4]) * farther
    picture = current.reshape(4, extent_y, block_len)
    return (fresh, picture)


def solution(mesh):
    placed = (P("gx", "gy", None, None),)
    return jax.shard_map(
        body,
        mesh=mesh,
        in_specs=placed,
        out_specs=(P("gx", "gy", None, None), P(None, "gy", "gx")),
        check_vma=False,
    )
```

```python
import jax
import jax.numpy as jnp
import numpy as np
from jax import lax
from jax.sharding import PartitionSpec as P
from jax.experimental import pallas as pl
from jax.experimental.pallas import tpu as pltpu

cohesion = -6.0
optical = 2.0


def extended(cells, sides, width):
    for axis, dim in sides:
        count = lax.axis_size(axis)
        head = lax.slice_in_dim(cells, 0, width, axis=dim)
        tail = lax.slice_in_dim(cells, cells.shape[dim] - width, cells.shape[dim], axis=dim)
        cells = jnp.concatenate(
            [
                lax.ppermute(tail, axis, [(i, (i + 1) % count) for i in range(count)]),
                cells,
                lax.ppermute(head, axis, [((i + 1) % count, i) for i in range(count)]),
            ],
            axis=dim,
        )
    return cells


def from_partner(x, axis, distance):
    return lax.ppermute(x, axis, [(i, i ^ 1 << distance) for i in range(lax.axis_size(axis))])


def lattice_tables():
    velocities = np.array(
        [
            [0, 0, 0],
            [1, 0, 0],
            [-1, 0, 0],
            [0, 1, 0],
            [0, -1, 0],
            [0, 0, 1],
            [0, 0, -1],
            [1, 1, 0],
            [-1, -1, 0],
            [1, -1, 0],
            [-1, 1, 0],
            [1, 0, 1],
            [-1, 0, -1],
            [1, 0, -1],
            [-1, 0, 1],
            [0, 1, 1],
            [0, -1, -1],
            [0, 1, -1],
            [0, -1, 1],
        ]
    )
    weights = np.array([1.0 / 3.0] + [1.0 / 18.0] * 6 + [1.0 / 36.0] * 12)
    along_x = velocities[:, 0] * 1.0
    along_y = velocities[:, 1] * 1.0
    along_z = velocities[:, 2] * 1.0
    squared = along_x * along_x + along_y * along_y + along_z * along_z
    moment_rows = [
        np.ones(19),
        19.0 * squared - 30.0,
        (21.0 * squared * squared - 53.0 * squared + 24.0) / 2.0,
        along_x,
        (5.0 * squared - 9.0) * along_x,
        along_y,
        (5.0 * squared - 9.0) * along_y,
        along_z,
        (5.0 * squared - 9.0) * along_z,
        3.0 * along_x * along_x - squared,
        (3.0 * squared - 5.0) * (3.0 * along_x * along_x - squared),
        along_y * along_y - along_z * along_z,
        (3.0 * squared - 5.0) * (along_y * along_y - along_z * along_z),
        along_x * along_y,
        along_y * along_z,
        along_x * along_z,
        (along_y * along_y - along_z * along_z) * along_x,
        (along_z * along_z - along_x * along_x) * along_y,
        (along_x * along_x - along_y * along_y) * along_z,
    ]
    moments = np.stack(moment_rows)
    inverse = moments.T / np.sum(moments * moments, axis=1)
    relax_rates = np.array(
        [
            0.0,
            1.19,
            1.4,
            0.0,
            1.2,
            0.0,
            1.2,
            0.0,
            1.2,
            1.0,
            1.4,
            1.0,
            1.4,
            1.0,
            1.0,
            1.0,
            1.98,
            1.98,
            1.98,
        ]
    )
    relaxing = inverse @ (relax_rates[:, None] * moments)
    forcing_map = inverse @ ((1.0 - 0.5 * relax_rates)[:, None] * moments)
    return (velocities, weights, relaxing, forcing_map)


def collide(populations, density, forcing, velocities, weights, relaxing, forcing_map):
    lattice = jnp.asarray(velocities, dtype=jnp.float32)
    spread = jnp.asarray(weights, dtype=jnp.float32)[None, None, :, None]
    relax_table = jnp.asarray(relaxing, dtype=jnp.float32)
    source_table = jnp.asarray(forcing_map, dtype=jnp.float32)
    momentum = jnp.einsum("qd,xyqz->dxyz", lattice, populations, precision=lax.Precision.HIGHEST)
    drift = (momentum + 0.5 * forcing) / density[None]
    along = jnp.einsum("qd,dxyz->xyqz", lattice, drift, precision=lax.Precision.HIGHEST)
    pushed = jnp.einsum("qd,dxyz->xyqz", lattice, forcing, precision=lax.Precision.HIGHEST)
    speed_squared = jnp.sum(drift * drift, axis=0)[:, :, None, :]
    work_done = jnp.sum(drift * forcing, axis=0)[:, :, None, :]
    balance = (
        spread
        * density[:, :, None, :]
        * (1.0 + 3.0 * along + 4.5 * along * along - 1.5 * speed_squared)
    )
    guo_term = spread * (3.0 * (pushed - work_done) + 9.0 * along * pushed)
    relaxed = jnp.einsum(
        "pq,xyqz->xypz", relax_table, populations - balance, precision=lax.Precision.HIGHEST
    )
    sourced = jnp.einsum("pq,xyqz->xypz", source_table, guo_term, precision=lax.Precision.HIGHEST)
    return populations - relaxed + sourced


def attraction(padded, offset, extent_x, extent_y, velocities, weights):
    centre = padded[offset : offset + extent_x, offset : offset + extent_y]
    totals = [jnp.zeros_like(centre), jnp.zeros_like(centre), jnp.zeros_like(centre)]
    for q in range(1, 19):
        steps = [int(v) for v in velocities[q]]
        start_x = offset + steps[0]
        start_y = offset + steps[1]
        neighbour = padded[start_x : start_x + extent_x, start_y : start_y + extent_y]
        neighbour = jnp.roll(neighbour, -steps[2], axis=2)
        for d in range(3):
            if steps[d] != 0:
                totals[d] = totals[d] + weights[q] * steps[d] * neighbour
    return jnp.stack([-cohesion * centre * totals[d] for d in range(3)])


def palette(density):
    reds = density / (1.0 + density)
    greens = jnp.exp(-density)
    blues = 0.5 * (1.0 + jnp.tanh(2.0 * (density - 1.0)))
    return (reds, greens, blues)


def shift_ring(x, axis, step):
    count = lax.axis_size(axis)
    return lax.ppermute(x, axis, [(i, (i - step) % count) for i in range(count)])


def collide_major(f, rho, force, velocities, weights, relaxing, forcing_map):
    lattice = velocities.astype(np.float32)
    extra = (1,) * rho.ndim
    cx = jnp.asarray(lattice[:, 0]).reshape((19,) + extra)
    cy = jnp.asarray(lattice[:, 1]).reshape((19,) + extra)
    cz = jnp.asarray(lattice[:, 2]).reshape((19,) + extra)
    spread = jnp.asarray(weights.astype(np.float32)).reshape((19,) + extra)
    momentum = [
        sum(f[q] * float(velocities[q][d]) for q in range(19) if velocities[q][d] != 0)
        for d in range(3)
    ]
    drift = [(momentum[d] + 0.5 * force[d]) / rho for d in range(3)]
    along = cx * drift[0] + cy * drift[1] + cz * drift[2]
    pushed = cx * force[0] + cy * force[1] + cz * force[2]
    speed_squared = drift[0] * drift[0] + drift[1] * drift[1] + drift[2] * drift[2]
    work_done = drift[0] * force[0] + drift[1] * force[1] + drift[2] * force[2]
    balance = spread * rho * (1.0 + 3.0 * along + 4.5 * along * along - 1.5 * speed_squared)
    guo_term = spread * (3.0 * (pushed - work_done) + 9.0 * along * pushed)
    relax_table = jnp.asarray(relaxing, dtype=jnp.float32)
    source_table = jnp.asarray(forcing_map, dtype=jnp.float32)
    table = jnp.concatenate([relax_table, -source_table], axis=1)
    stacked = jnp.concatenate([f - balance, guo_term], axis=0)
    return f - jnp.einsum("pq,q...->p...", table, stacked, precision=lax.Precision.HIGH)


def stream_and_render(collided, velocities, extent_x, extent_y, length_x):
    near_y, band, far_y = collided
    depth_z = band.shape[3]
    edge = near_y.shape[2]
    steps = [[int(v) for v in velocities[q]] for q in range(19)]

    def kernel(near_ref, band_ref, far_ref, o_ref, pic_ref, c_ref):
        def gather(q, carry):
            c_ref[q, :, 0:edge] = near_ref[q]
            c_ref[q, :, edge : edge + extent_y - 2] = band_ref[q]
            c_ref[q, :, edge + extent_y - 2 :] = far_ref[q]
            return carry

        lax.fori_loop(0, 19, gather, 0)
        for q in range(19):
            cx, cy, cz = steps[q]

            def move(x, carry):
                v = c_ref[q, x + 1 - cx, pl.ds(1 - cy, extent_y), :]
                if cz != 0:
                    v = pltpu.roll(v, shift=cz % depth_z, axis=1)
                o_ref[q, x] = v
                return carry

            lax.fori_loop(0, extent_x, move, 0, unroll=True)

        def render(x, carry):
            depth, red, green, blue = carry
            fresh_density = o_ref[0, x]
            for q in range(1, 19):
                fresh_density = fresh_density + o_ref[q, x]
            extinction = optical * fresh_density / length_x
            weight = jnp.exp(-depth) * (1.0 - jnp.exp(-extinction))
            red = red + weight * (fresh_density / (1.0 + fresh_density))
            green = green + weight * jnp.exp(-fresh_density)
            blue = blue + weight * (0.5 * (1.0 + jnp.tanh(2.0 * (fresh_density - 1.0))))
            return (depth + extinction, red, green, blue)

        zero = jnp.zeros((extent_y, depth_z), jnp.float32)
        depth, red, green, blue = lax.fori_loop(0, extent_x, render, (zero, zero, zero, zero), unroll=True)
        pic_ref[0] = red
        pic_ref[1] = green
        pic_ref[2] = blue
        pic_ref[3] = 1.0 - jnp.exp(-depth)

    return pl.pallas_call(
        kernel,
        out_shape=(
            jax.ShapeDtypeStruct((19, extent_x, extent_y, depth_z), jnp.float32),
            jax.ShapeDtypeStruct((4, extent_y, depth_z), jnp.float32),
        ),
        in_specs=[pl.BlockSpec(memory_space=pltpu.VMEM)] * 3,
        out_specs=(pl.BlockSpec(memory_space=pltpu.VMEM), pl.BlockSpec(memory_space=pltpu.VMEM)),
        scratch_shapes=[pltpu.VMEM((19, extent_x + 2, extent_y + 2, depth_z), jnp.float32)],
    )(near_y, band, far_y)


def collide_region(cells, pot, tables):
    velocities, weights, relaxing, forcing_map = tables
    nx, ny = cells.shape[1], cells.shape[2]
    centre = pot[1 : 1 + nx, 1 : 1 + ny]
    totals = [jnp.zeros_like(centre), jnp.zeros_like(centre), jnp.zeros_like(centre)]
    for q in range(1, 19):
        steps = [int(v) for v in velocities[q]]
        neighbour = pot[1 + steps[0] : 1 + steps[0] + nx, 1 + steps[1] : 1 + steps[1] + ny]
        neighbour = jnp.roll(neighbour, -steps[2], axis=2)
        for d in range(3):
            if steps[d] != 0:
                totals[d] = totals[d] + weights[q] * steps[d] * neighbour
    force = [-cohesion * centre * totals[d] for d in range(3)]
    rho = jnp.sum(cells, axis=0)
    return collide_major(cells, rho, force, velocities, weights, relaxing, forcing_map)


def body(populations):
    velocities, weights, relaxing, forcing_map = lattice_tables()
    extent_x = populations.shape[0]
    extent_y = populations.shape[1]
    f = jnp.transpose(populations, (2, 0, 1, 3))
    potential = 1.0 - jnp.exp(-jnp.sum(f, axis=0))
    to_next = jnp.concatenate([f[:, extent_x - 1], potential[extent_x - 1 : extent_x], potential[extent_x - 2 : extent_x - 1]])
    to_prev = jnp.concatenate([f[:, 0], potential[0:1], potential[1:2]])
    from_prev = shift_ring(to_next, "gx", -1)
    from_next = shift_ring(to_prev, "gx", 1)
    fx = jnp.concatenate([from_prev[None, :19].transpose(1, 0, 2, 3), f, from_next[None, :19].transpose(1, 0, 2, 3)], axis=1)
    px = jnp.concatenate([from_prev[20:21], from_prev[19:20], potential, from_next[19:20], from_next[20:21]], axis=0)
    zero_x = jnp.zeros((19, 1, fx.shape[3]), f.dtype)

    def y_message(row_pop, row_near, row_far):
        pops = jnp.concatenate([zero_x, fx[:, :, row_pop], zero_x], axis=1)
        return jnp.concatenate([pops, px[None, :, row_near], px[None, :, row_far]], axis=0)

    from_below = shift_ring(y_message(extent_y - 1, extent_y - 1, extent_y - 2), "gy", -1)
    from_above = shift_ring(y_message(0, 0, 1), "gy", 1)
    fxy = jnp.concatenate(
        [from_below[:19, 1:-1, None], fx, from_above[:19, 1:-1, None]], axis=2
    )
    pxy = jnp.concatenate(
        [from_below[20][:, None], from_below[19][:, None], px, from_above[19][:, None], from_above[20][:, None]],
        axis=1,
    )
    tables = (velocities, weights, relaxing, forcing_map)
    inner = collide_region(f[:, 1 : extent_x - 1, 1 : extent_y - 1], potential, tables)
    near_x = collide_region(fx[:, 0:2, 1 : extent_y - 1], px[0:4], tables)
    far_x = collide_region(fx[:, extent_x : extent_x + 2, 1 : extent_y - 1], px[extent_x : extent_x + 4], tables)
    band = jnp.concatenate([near_x, inner, far_x], axis=1)
    near_y = collide_region(fxy[:, :, 0:2], pxy[:, 0:4], tables)
    far_y = collide_region(fxy[:, :, extent_y : extent_y + 2], pxy[:, extent_y : extent_y + 4], tables)
    collided = (near_y, band, far_y)
    groups = lax.axis_size("gx")
    length_x = extent_x * groups
    fresh_major, layered = stream_and_render(collided, velocities, extent_x, extent_y, length_x)
    fresh = jnp.transpose(fresh_major, (1, 2, 0, 3))
    depth_z = layered.shape[2]
    block_len = depth_z // groups
    blocked = layered.reshape(4, extent_y, groups, block_len)
    gathered = lax.all_to_all(blocked, "gx", 2, 2, tiled=True)
    current = gathered[:, :, 0]
    for source in range(1, groups):
        current = current + (1.0 - current[3:4]) * gathered[:, :, source]
    picture = current
    return (fresh, picture)


def solution(mesh):
    placed = (P("gx", "gy", None, None),)
    return jax.shard_map(
        body,
        mesh=mesh,
        in_specs=placed,
        out_specs=(P("gx", "gy", None, None), P(None, "gy", "gx")),
        check_vma=False,
    )
```

```python
import jax
import jax.numpy as jnp
import numpy as np
from jax import lax
from jax.sharding import PartitionSpec as P
from jax.experimental import pallas as pl
from jax.experimental.pallas import tpu as pltpu

cohesion = -6.0
optical = 2.0


def extended(cells, sides, width):
    for axis, dim in sides:
        count = lax.axis_size(axis)
        head = lax.slice_in_dim(cells, 0, width, axis=dim)
        tail = lax.slice_in_dim(cells, cells.shape[dim] - width, cells.shape[dim], axis=dim)
        cells = jnp.concatenate(
            [
                lax.ppermute(tail, axis, [(i, (i + 1) % count) for i in range(count)]),
                cells,
                lax.ppermute(head, axis, [((i + 1) % count, i) for i in range(count)]),
            ],
            axis=dim,
        )
    return cells


def from_partner(x, axis, distance):
    return lax.ppermute(x, axis, [(i, i ^ 1 << distance) for i in range(lax.axis_size(axis))])


def lattice_tables():
    velocities = np.array(
        [
            [0, 0, 0],
            [1, 0, 0],
            [-1, 0, 0],
            [0, 1, 0],
            [0, -1, 0],
            [0, 0, 1],
            [0, 0, -1],
            [1, 1, 0],
            [-1, -1, 0],
            [1, -1, 0],
            [-1, 1, 0],
            [1, 0, 1],
            [-1, 0, -1],
            [1, 0, -1],
            [-1, 0, 1],
            [0, 1, 1],
            [0, -1, -1],
            [0, 1, -1],
            [0, -1, 1],
        ]
    )
    weights = np.array([1.0 / 3.0] + [1.0 / 18.0] * 6 + [1.0 / 36.0] * 12)
    along_x = velocities[:, 0] * 1.0
    along_y = velocities[:, 1] * 1.0
    along_z = velocities[:, 2] * 1.0
    squared = along_x * along_x + along_y * along_y + along_z * along_z
    moment_rows = [
        np.ones(19),
        19.0 * squared - 30.0,
        (21.0 * squared * squared - 53.0 * squared + 24.0) / 2.0,
        along_x,
        (5.0 * squared - 9.0) * along_x,
        along_y,
        (5.0 * squared - 9.0) * along_y,
        along_z,
        (5.0 * squared - 9.0) * along_z,
        3.0 * along_x * along_x - squared,
        (3.0 * squared - 5.0) * (3.0 * along_x * along_x - squared),
        along_y * along_y - along_z * along_z,
        (3.0 * squared - 5.0) * (along_y * along_y - along_z * along_z),
        along_x * along_y,
        along_y * along_z,
        along_x * along_z,
        (along_y * along_y - along_z * along_z) * along_x,
        (along_z * along_z - along_x * along_x) * along_y,
        (along_x * along_x - along_y * along_y) * along_z,
    ]
    moments = np.stack(moment_rows)
    inverse = moments.T / np.sum(moments * moments, axis=1)
    relax_rates = np.array(
        [
            0.0,
            1.19,
            1.4,
            0.0,
            1.2,
            0.0,
            1.2,
            0.0,
            1.2,
            1.0,
            1.4,
            1.0,
            1.4,
            1.0,
            1.0,
            1.0,
            1.98,
            1.98,
            1.98,
        ]
    )
    relaxing = inverse @ (relax_rates[:, None] * moments)
    forcing_map = inverse @ ((1.0 - 0.5 * relax_rates)[:, None] * moments)
    return (velocities, weights, relaxing, forcing_map)


def collide(populations, density, forcing, velocities, weights, relaxing, forcing_map):
    lattice = jnp.asarray(velocities, dtype=jnp.float32)
    spread = jnp.asarray(weights, dtype=jnp.float32)[None, None, :, None]
    relax_table = jnp.asarray(relaxing, dtype=jnp.float32)
    source_table = jnp.asarray(forcing_map, dtype=jnp.float32)
    momentum = jnp.einsum("qd,xyqz->dxyz", lattice, populations, precision=lax.Precision.HIGHEST)
    drift = (momentum + 0.5 * forcing) / density[None]
    along = jnp.einsum("qd,dxyz->xyqz", lattice, drift, precision=lax.Precision.HIGHEST)
    pushed = jnp.einsum("qd,dxyz->xyqz", lattice, forcing, precision=lax.Precision.HIGHEST)
    speed_squared = jnp.sum(drift * drift, axis=0)[:, :, None, :]
    work_done = jnp.sum(drift * forcing, axis=0)[:, :, None, :]
    balance = (
        spread
        * density[:, :, None, :]
        * (1.0 + 3.0 * along + 4.5 * along * along - 1.5 * speed_squared)
    )
    guo_term = spread * (3.0 * (pushed - work_done) + 9.0 * along * pushed)
    relaxed = jnp.einsum(
        "pq,xyqz->xypz", relax_table, populations - balance, precision=lax.Precision.HIGHEST
    )
    sourced = jnp.einsum("pq,xyqz->xypz", source_table, guo_term, precision=lax.Precision.HIGHEST)
    return populations - relaxed + sourced


def attraction(padded, offset, extent_x, extent_y, velocities, weights):
    centre = padded[offset : offset + extent_x, offset : offset + extent_y]
    totals = [jnp.zeros_like(centre), jnp.zeros_like(centre), jnp.zeros_like(centre)]
    for q in range(1, 19):
        steps = [int(v) for v in velocities[q]]
        start_x = offset + steps[0]
        start_y = offset + steps[1]
        neighbour = padded[start_x : start_x + extent_x, start_y : start_y + extent_y]
        neighbour = jnp.roll(neighbour, -steps[2], axis=2)
        for d in range(3):
            if steps[d] != 0:
                totals[d] = totals[d] + weights[q] * steps[d] * neighbour
    return jnp.stack([-cohesion * centre * totals[d] for d in range(3)])


def palette(density):
    reds = density / (1.0 + density)
    greens = jnp.exp(-density)
    blues = 0.5 * (1.0 + jnp.tanh(2.0 * (density - 1.0)))
    return (reds, greens, blues)


def shift_ring(x, axis, step):
    count = lax.axis_size(axis)
    return lax.ppermute(x, axis, [(i, (i - step) % count) for i in range(count)])


def collide_major(f, rho, force, velocities, weights, relaxing, forcing_map):
    lattice = velocities.astype(np.float32)
    extra = (1,) * rho.ndim
    cx = jnp.asarray(lattice[:, 0]).reshape((19,) + extra)
    cy = jnp.asarray(lattice[:, 1]).reshape((19,) + extra)
    cz = jnp.asarray(lattice[:, 2]).reshape((19,) + extra)
    spread = jnp.asarray(weights.astype(np.float32)).reshape((19,) + extra)
    momentum = [
        sum(f[q] * float(velocities[q][d]) for q in range(19) if velocities[q][d] != 0)
        for d in range(3)
    ]
    drift = [(momentum[d] + 0.5 * force[d]) / rho for d in range(3)]
    along = cx * drift[0] + cy * drift[1] + cz * drift[2]
    pushed = cx * force[0] + cy * force[1] + cz * force[2]
    speed_squared = drift[0] * drift[0] + drift[1] * drift[1] + drift[2] * drift[2]
    work_done = drift[0] * force[0] + drift[1] * force[1] + drift[2] * force[2]
    balance = spread * rho * (1.0 + 3.0 * along + 4.5 * along * along - 1.5 * speed_squared)
    guo_term = spread * (3.0 * (pushed - work_done) + 9.0 * along * pushed)
    relax_table = jnp.asarray(relaxing, dtype=jnp.float32)
    source_table = jnp.asarray(forcing_map, dtype=jnp.float32)
    table = jnp.concatenate([relax_table, -source_table], axis=1)
    stacked = jnp.concatenate([f - balance, guo_term], axis=0)
    return f - jnp.einsum("pq,q...->p...", table, stacked, precision=lax.Precision.HIGH)


def stream_and_render(collided, velocities, extent_x, extent_y, length_x, groups):
    near_y, band, far_y = collided
    depth_z = band.shape[3]
    edge = near_y.shape[2]
    steps = [[int(v) for v in velocities[q]] for q in range(19)]

    def kernel(near_ref, band_ref, far_ref, o_ref, pic_ref, c_ref):
        def gather(q, carry):
            c_ref[q, :, 0:edge] = near_ref[q]
            c_ref[q, :, edge : edge + extent_y - 2] = band_ref[q]
            c_ref[q, :, edge + extent_y - 2 :] = far_ref[q]
            return carry

        lax.fori_loop(0, 19, gather, 0)
        for q in range(19):
            cx, cy, cz = steps[q]

            def move(x, carry):
                v = c_ref[q, x + 1 - cx, pl.ds(1 - cy, extent_y), :]
                if cz != 0:
                    v = pltpu.roll(v, shift=cz % depth_z, axis=1)
                o_ref[q, x] = v
                return carry

            lax.fori_loop(0, extent_x, move, 0, unroll=True)

        def render(x, carry):
            depth, red, green, blue = carry
            fresh_density = o_ref[0, x]
            for q in range(1, 19):
                fresh_density = fresh_density + o_ref[q, x]
            extinction = optical * fresh_density / length_x
            weight = jnp.exp(-depth) * (1.0 - jnp.exp(-extinction))
            red = red + weight * (fresh_density / (1.0 + fresh_density))
            green = green + weight * jnp.exp(-fresh_density)
            blue = blue + weight * (0.5 * (1.0 + jnp.tanh(2.0 * (fresh_density - 1.0))))
            return (depth + extinction, red, green, blue)

        zero = jnp.zeros((extent_y, depth_z), jnp.float32)
        depth, red, green, blue = lax.fori_loop(0, extent_x, render, (zero, zero, zero, zero), unroll=True)
        block_len = depth_z // groups
        for channel, value in enumerate((red, green, blue, 1.0 - jnp.exp(-depth))):
            for block in range(groups):
                pic_ref[block, channel] = value[:, block * block_len : (block + 1) * block_len]

    return pl.pallas_call(
        kernel,
        out_shape=(
            jax.ShapeDtypeStruct((19, extent_x, extent_y, depth_z), jnp.float32),
            jax.ShapeDtypeStruct((groups, 4, extent_y, depth_z // groups), jnp.float32),
        ),
        in_specs=[pl.BlockSpec(memory_space=pltpu.VMEM)] * 3,
        out_specs=(pl.BlockSpec(memory_space=pltpu.VMEM), pl.BlockSpec(memory_space=pltpu.VMEM)),
        scratch_shapes=[pltpu.VMEM((19, extent_x + 2, extent_y + 2, depth_z), jnp.float32)],
    )(near_y, band, far_y)


def collide_region(cells, pot, tables):
    velocities, weights, relaxing, forcing_map = tables
    nx, ny = cells.shape[1], cells.shape[2]
    centre = pot[1 : 1 + nx, 1 : 1 + ny]
    totals = [jnp.zeros_like(centre), jnp.zeros_like(centre), jnp.zeros_like(centre)]
    for q in range(1, 19):
        steps = [int(v) for v in velocities[q]]
        neighbour = pot[1 + steps[0] : 1 + steps[0] + nx, 1 + steps[1] : 1 + steps[1] + ny]
        neighbour = jnp.roll(neighbour, -steps[2], axis=2)
        for d in range(3):
            if steps[d] != 0:
                totals[d] = totals[d] + weights[q] * steps[d] * neighbour
    force = [-cohesion * centre * totals[d] for d in range(3)]
    rho = jnp.sum(cells, axis=0)
    return collide_major(cells, rho, force, velocities, weights, relaxing, forcing_map)


def body(populations):
    velocities, weights, relaxing, forcing_map = lattice_tables()
    extent_x = populations.shape[0]
    extent_y = populations.shape[1]
    f = jnp.transpose(populations, (2, 0, 1, 3))
    potential = 1.0 - jnp.exp(-jnp.sum(f, axis=0))
    to_next = jnp.concatenate([f[:, extent_x - 1], potential[extent_x - 1 : extent_x], potential[extent_x - 2 : extent_x - 1]])
    to_prev = jnp.concatenate([f[:, 0], potential[0:1], potential[1:2]])
    from_prev = shift_ring(to_next, "gx", -1)
    from_next = shift_ring(to_prev, "gx", 1)
    fx = jnp.concatenate([from_prev[None, :19].transpose(1, 0, 2, 3), f, from_next[None, :19].transpose(1, 0, 2, 3)], axis=1)
    px = jnp.concatenate([from_prev[20:21], from_prev[19:20], potential, from_next[19:20], from_next[20:21]], axis=0)
    zero_x = jnp.zeros((19, 1, fx.shape[3]), f.dtype)

    def y_message(row_pop, row_near, row_far):
        pops = jnp.concatenate([zero_x, fx[:, :, row_pop], zero_x], axis=1)
        return jnp.concatenate([pops, px[None, :, row_near], px[None, :, row_far]], axis=0)

    from_below = shift_ring(y_message(extent_y - 1, extent_y - 1, extent_y - 2), "gy", -1)
    from_above = shift_ring(y_message(0, 0, 1), "gy", 1)
    fxy = jnp.concatenate(
        [from_below[:19, 1:-1, None], fx, from_above[:19, 1:-1, None]], axis=2
    )
    pxy = jnp.concatenate(
        [from_below[20][:, None], from_below[19][:, None], px, from_above[19][:, None], from_above[20][:, None]],
        axis=1,
    )
    tables = (velocities, weights, relaxing, forcing_map)
    inner = collide_region(f[:, 1 : extent_x - 1, 1 : extent_y - 1], potential, tables)
    near_x = collide_region(fx[:, 0:2, 1 : extent_y - 1], px[0:4], tables)
    far_x = collide_region(fx[:, extent_x : extent_x + 2, 1 : extent_y - 1], px[extent_x : extent_x + 4], tables)
    band = jnp.concatenate([near_x, inner, far_x], axis=1)
    near_y = collide_region(fxy[:, :, 0:2], pxy[:, 0:4], tables)
    far_y = collide_region(fxy[:, :, extent_y : extent_y + 2], pxy[:, extent_y : extent_y + 4], tables)
    collided = (near_y, band, far_y)
    groups = lax.axis_size("gx")
    length_x = extent_x * groups
    fresh_major, blocked = stream_and_render(collided, velocities, extent_x, extent_y, length_x, groups)
    fresh = jnp.transpose(fresh_major, (1, 2, 0, 3))
    gathered = lax.all_to_all(blocked, "gx", 0, 0, tiled=True)
    current = gathered[0]
    for source in range(1, groups):
        current = current + (1.0 - current[3:4]) * gathered[source]
    picture = current
    return (fresh, picture)


def solution(mesh):
    placed = (P("gx", "gy", None, None),)
    return jax.shard_map(
        body,
        mesh=mesh,
        in_specs=placed,
        out_specs=(P("gx", "gy", None, None), P(None, "gy", "gx")),
        check_vma=False,
    )
```

```python
import jax
import jax.numpy as jnp
import numpy as np
from jax import lax
from jax.sharding import PartitionSpec as P
from jax.experimental import pallas as pl
from jax.experimental.pallas import tpu as pltpu

cohesion = -6.0
optical = 2.0


def extended(cells, sides, width):
    for axis, dim in sides:
        count = lax.axis_size(axis)
        head = lax.slice_in_dim(cells, 0, width, axis=dim)
        tail = lax.slice_in_dim(cells, cells.shape[dim] - width, cells.shape[dim], axis=dim)
        cells = jnp.concatenate(
            [
                lax.ppermute(tail, axis, [(i, (i + 1) % count) for i in range(count)]),
                cells,
                lax.ppermute(head, axis, [((i + 1) % count, i) for i in range(count)]),
            ],
            axis=dim,
        )
    return cells


def from_partner(x, axis, distance):
    return lax.ppermute(x, axis, [(i, i ^ 1 << distance) for i in range(lax.axis_size(axis))])


def lattice_tables():
    velocities = np.array(
        [
            [0, 0, 0],
            [1, 0, 0],
            [-1, 0, 0],
            [0, 1, 0],
            [0, -1, 0],
            [0, 0, 1],
            [0, 0, -1],
            [1, 1, 0],
            [-1, -1, 0],
            [1, -1, 0],
            [-1, 1, 0],
            [1, 0, 1],
            [-1, 0, -1],
            [1, 0, -1],
            [-1, 0, 1],
            [0, 1, 1],
            [0, -1, -1],
            [0, 1, -1],
            [0, -1, 1],
        ]
    )
    weights = np.array([1.0 / 3.0] + [1.0 / 18.0] * 6 + [1.0 / 36.0] * 12)
    along_x = velocities[:, 0] * 1.0
    along_y = velocities[:, 1] * 1.0
    along_z = velocities[:, 2] * 1.0
    squared = along_x * along_x + along_y * along_y + along_z * along_z
    moment_rows = [
        np.ones(19),
        19.0 * squared - 30.0,
        (21.0 * squared * squared - 53.0 * squared + 24.0) / 2.0,
        along_x,
        (5.0 * squared - 9.0) * along_x,
        along_y,
        (5.0 * squared - 9.0) * along_y,
        along_z,
        (5.0 * squared - 9.0) * along_z,
        3.0 * along_x * along_x - squared,
        (3.0 * squared - 5.0) * (3.0 * along_x * along_x - squared),
        along_y * along_y - along_z * along_z,
        (3.0 * squared - 5.0) * (along_y * along_y - along_z * along_z),
        along_x * along_y,
        along_y * along_z,
        along_x * along_z,
        (along_y * along_y - along_z * along_z) * along_x,
        (along_z * along_z - along_x * along_x) * along_y,
        (along_x * along_x - along_y * along_y) * along_z,
    ]
    moments = np.stack(moment_rows)
    inverse = moments.T / np.sum(moments * moments, axis=1)
    relax_rates = np.array(
        [
            0.0,
            1.19,
            1.4,
            0.0,
            1.2,
            0.0,
            1.2,
            0.0,
            1.2,
            1.0,
            1.4,
            1.0,
            1.4,
            1.0,
            1.0,
            1.0,
            1.98,
            1.98,
            1.98,
        ]
    )
    relaxing = inverse @ (relax_rates[:, None] * moments)
    forcing_map = inverse @ ((1.0 - 0.5 * relax_rates)[:, None] * moments)
    return (velocities, weights, relaxing, forcing_map)


def collide(populations, density, forcing, velocities, weights, relaxing, forcing_map):
    lattice = jnp.asarray(velocities, dtype=jnp.float32)
    spread = jnp.asarray(weights, dtype=jnp.float32)[None, None, :, None]
    relax_table = jnp.asarray(relaxing, dtype=jnp.float32)
    source_table = jnp.asarray(forcing_map, dtype=jnp.float32)
    momentum = jnp.einsum("qd,xyqz->dxyz", lattice, populations, precision=lax.Precision.HIGHEST)
    drift = (momentum + 0.5 * forcing) / density[None]
    along = jnp.einsum("qd,dxyz->xyqz", lattice, drift, precision=lax.Precision.HIGHEST)
    pushed = jnp.einsum("qd,dxyz->xyqz", lattice, forcing, precision=lax.Precision.HIGHEST)
    speed_squared = jnp.sum(drift * drift, axis=0)[:, :, None, :]
    work_done = jnp.sum(drift * forcing, axis=0)[:, :, None, :]
    balance = (
        spread
        * density[:, :, None, :]
        * (1.0 + 3.0 * along + 4.5 * along * along - 1.5 * speed_squared)
    )
    guo_term = spread * (3.0 * (pushed - work_done) + 9.0 * along * pushed)
    relaxed = jnp.einsum(
        "pq,xyqz->xypz", relax_table, populations - balance, precision=lax.Precision.HIGHEST
    )
    sourced = jnp.einsum("pq,xyqz->xypz", source_table, guo_term, precision=lax.Precision.HIGHEST)
    return populations - relaxed + sourced


def attraction(padded, offset, extent_x, extent_y, velocities, weights):
    centre = padded[offset : offset + extent_x, offset : offset + extent_y]
    totals = [jnp.zeros_like(centre), jnp.zeros_like(centre), jnp.zeros_like(centre)]
    for q in range(1, 19):
        steps = [int(v) for v in velocities[q]]
        start_x = offset + steps[0]
        start_y = offset + steps[1]
        neighbour = padded[start_x : start_x + extent_x, start_y : start_y + extent_y]
        neighbour = jnp.roll(neighbour, -steps[2], axis=2)
        for d in range(3):
            if steps[d] != 0:
                totals[d] = totals[d] + weights[q] * steps[d] * neighbour
    return jnp.stack([-cohesion * centre * totals[d] for d in range(3)])


def palette(density):
    reds = density / (1.0 + density)
    greens = jnp.exp(-density)
    blues = 0.5 * (1.0 + jnp.tanh(2.0 * (density - 1.0)))
    return (reds, greens, blues)


def shift_ring(x, axis, step):
    count = lax.axis_size(axis)
    return lax.ppermute(x, axis, [(i, (i - step) % count) for i in range(count)])


def collide_major(f, rho, force, velocities, weights, relaxing, forcing_map):
    lattice = velocities.astype(np.float32)
    extra = (1,) * rho.ndim
    cx = jnp.asarray(lattice[:, 0]).reshape((19,) + extra)
    cy = jnp.asarray(lattice[:, 1]).reshape((19,) + extra)
    cz = jnp.asarray(lattice[:, 2]).reshape((19,) + extra)
    spread = jnp.asarray(weights.astype(np.float32)).reshape((19,) + extra)
    momentum = [
        sum(f[q] * float(velocities[q][d]) for q in range(19) if velocities[q][d] != 0)
        for d in range(3)
    ]
    drift = [(momentum[d] + 0.5 * force[d]) / rho for d in range(3)]
    along = cx * drift[0] + cy * drift[1] + cz * drift[2]
    pushed = cx * force[0] + cy * force[1] + cz * force[2]
    speed_squared = drift[0] * drift[0] + drift[1] * drift[1] + drift[2] * drift[2]
    work_done = drift[0] * force[0] + drift[1] * force[1] + drift[2] * force[2]
    balance = spread * rho * (1.0 + 3.0 * along + 4.5 * along * along - 1.5 * speed_squared)
    guo_term = spread * (3.0 * (pushed - work_done) + 9.0 * along * pushed)
    relax_table = jnp.asarray(relaxing, dtype=jnp.float32)
    source_table = jnp.asarray(forcing_map, dtype=jnp.float32)
    table = jnp.concatenate([relax_table, -source_table], axis=1)
    stacked = jnp.concatenate([f - balance, guo_term], axis=0)
    return f - jnp.einsum("pq,q...->p...", table, stacked, precision=lax.Precision.HIGH)


def stream_and_render(collided, velocities, extent_x, extent_y, length_x):
    near_y, band, far_y = collided
    depth_z = band.shape[3]
    edge = near_y.shape[2]
    inner_rows = extent_y - 2 * edge
    steps = [[int(v) for v in velocities[q]] for q in range(19)]
    fresh_shape = jax.ShapeDtypeStruct((19, extent_x, extent_y, depth_z), jnp.float32)

    def shifted(v, cz):
        return pltpu.roll(v, shift=cz % depth_z, axis=1) if cz != 0 else v

    def band_kernel(band_ref, o_ref):
        for q in range(19):
            cx, cy, cz = steps[q]
            for x in range(extent_x):
                v = band_ref[q, x + 1 - cx, pl.ds(1 - cy, inner_rows), :]
                o_ref[q, x, pl.ds(edge, inner_rows), :] = shifted(v, cz)

    partial = pl.pallas_call(
        band_kernel,
        out_shape=fresh_shape,
        in_specs=[pl.BlockSpec(memory_space=pltpu.VMEM)],
        out_specs=pl.BlockSpec(memory_space=pltpu.VMEM),
        cost_estimate=pl.CostEstimate(flops=0, transcendentals=0, bytes_accessed=2 * band.size * 4),
    )(band)

    def edge_kernel(near_ref, band_ref, far_ref, fresh_ref, o_ref, pic_ref, low_ref, high_ref):
        def gather(q, carry):
            o_ref[q] = fresh_ref[q]
            low_ref[q, :, 0:edge] = near_ref[q]
            low_ref[q, :, edge : 2 * edge] = band_ref[q, :, 0:edge]
            high_ref[q, :, 0:edge] = band_ref[q, :, inner_rows : inner_rows + edge]
            high_ref[q, :, edge : 2 * edge] = far_ref[q]
            return carry

        lax.fori_loop(0, 19, gather, 0)
        for q in range(19):
            cx, cy, cz = steps[q]
            for x in range(extent_x):
                v = low_ref[q, x + 1 - cx, pl.ds(1 - cy, edge), :]
                o_ref[q, x, pl.ds(0, edge), :] = shifted(v, cz)
                v = high_ref[q, x + 1 - cx, pl.ds(1 - cy, edge), :]
                o_ref[q, x, pl.ds(extent_y - edge, edge), :] = shifted(v, cz)

        def render(x, carry):
            depth, red, green, blue = carry
            fresh_density = o_ref[0, x]
            for q in range(1, 19):
                fresh_density = fresh_density + o_ref[q, x]
            extinction = optical * fresh_density / length_x
            weight = jnp.exp(-depth) * (1.0 - jnp.exp(-extinction))
            red = red + weight * (fresh_density / (1.0 + fresh_density))
            green = green + weight * jnp.exp(-fresh_density)
            blue = blue + weight * (0.5 * (1.0 + jnp.tanh(2.0 * (fresh_density - 1.0))))
            return (depth + extinction, red, green, blue)

        zero = jnp.zeros((extent_y, depth_z), jnp.float32)
        depth, red, green, blue = lax.fori_loop(0, extent_x, render, (zero, zero, zero, zero), unroll=True)
        pic_ref[0] = red
        pic_ref[1] = green
        pic_ref[2] = blue
        pic_ref[3] = 1.0 - jnp.exp(-depth)

    return pl.pallas_call(
        edge_kernel,
        out_shape=(fresh_shape, jax.ShapeDtypeStruct((4, extent_y, depth_z), jnp.float32)),
        in_specs=[pl.BlockSpec(memory_space=pltpu.VMEM)] * 4,
        out_specs=(pl.BlockSpec(memory_space=pltpu.VMEM), pl.BlockSpec(memory_space=pltpu.VMEM)),
        scratch_shapes=[
            pltpu.VMEM((19, extent_x + 2, 2 * edge, depth_z), jnp.float32),
            pltpu.VMEM((19, extent_x + 2, 2 * edge, depth_z), jnp.float32),
        ],
        input_output_aliases={3: 0},
    )(near_y, band, far_y, partial)


def collide_region(cells, pot, tables):
    velocities, weights, relaxing, forcing_map = tables
    nx, ny = cells.shape[1], cells.shape[2]
    centre = pot[1 : 1 + nx, 1 : 1 + ny]
    totals = [jnp.zeros_like(centre), jnp.zeros_like(centre), jnp.zeros_like(centre)]
    for q in range(1, 19):
        steps = [int(v) for v in velocities[q]]
        neighbour = pot[1 + steps[0] : 1 + steps[0] + nx, 1 + steps[1] : 1 + steps[1] + ny]
        neighbour = jnp.roll(neighbour, -steps[2], axis=2)
        for d in range(3):
            if steps[d] != 0:
                totals[d] = totals[d] + weights[q] * steps[d] * neighbour
    force = [-cohesion * centre * totals[d] for d in range(3)]
    rho = jnp.sum(cells, axis=0)
    return collide_major(cells, rho, force, velocities, weights, relaxing, forcing_map)


def body(populations):
    velocities, weights, relaxing, forcing_map = lattice_tables()
    extent_x = populations.shape[0]
    extent_y = populations.shape[1]
    f = jnp.transpose(populations, (2, 0, 1, 3))
    potential = 1.0 - jnp.exp(-jnp.sum(f, axis=0))
    to_next = jnp.concatenate([f[:, extent_x - 1], potential[extent_x - 1 : extent_x], potential[extent_x - 2 : extent_x - 1]])
    to_prev = jnp.concatenate([f[:, 0], potential[0:1], potential[1:2]])
    from_prev = shift_ring(to_next, "gx", -1)
    from_next = shift_ring(to_prev, "gx", 1)
    fx = jnp.concatenate([from_prev[None, :19].transpose(1, 0, 2, 3), f, from_next[None, :19].transpose(1, 0, 2, 3)], axis=1)
    px = jnp.concatenate([from_prev[20:21], from_prev[19:20], potential, from_next[19:20], from_next[20:21]], axis=0)
    zero_x = jnp.zeros((19, 1, fx.shape[3]), f.dtype)

    def y_message(row_pop, row_near, row_far):
        pops = jnp.concatenate([zero_x, fx[:, :, row_pop], zero_x], axis=1)
        return jnp.concatenate([pops, px[None, :, row_near], px[None, :, row_far]], axis=0)

    from_below = shift_ring(y_message(extent_y - 1, extent_y - 1, extent_y - 2), "gy", -1)
    from_above = shift_ring(y_message(0, 0, 1), "gy", 1)
    fxy = jnp.concatenate(
        [from_below[:19, 1:-1, None], fx, from_above[:19, 1:-1, None]], axis=2
    )
    pxy = jnp.concatenate(
        [from_below[20][:, None], from_below[19][:, None], px, from_above[19][:, None], from_above[20][:, None]],
        axis=1,
    )
    tables = (velocities, weights, relaxing, forcing_map)
    inner = collide_region(f[:, 1 : extent_x - 1, 1 : extent_y - 1], potential, tables)
    near_x = collide_region(fx[:, 0:2, 1 : extent_y - 1], px[0:4], tables)
    far_x = collide_region(fx[:, extent_x : extent_x + 2, 1 : extent_y - 1], px[extent_x : extent_x + 4], tables)
    band = jnp.concatenate([near_x, inner, far_x], axis=1)
    near_y = collide_region(fxy[:, :, 0:2], pxy[:, 0:4], tables)
    far_y = collide_region(fxy[:, :, extent_y : extent_y + 2], pxy[:, extent_y : extent_y + 4], tables)
    collided = (near_y, band, far_y)
    groups = lax.axis_size("gx")
    length_x = extent_x * groups
    fresh_major, layered = stream_and_render(collided, velocities, extent_x, extent_y, length_x)
    fresh = jnp.transpose(fresh_major, (1, 2, 0, 3))
    depth_z = layered.shape[2]
    block_len = depth_z // groups
    blocked = layered.reshape(4, extent_y, groups, block_len)
    position = lax.axis_index("gx")
    current = blocked
    for level in range(groups.bit_length() - 1):
        parity = position // (1 << level) % 2
        halves = current.shape[2] // 2
        paired = current.reshape(4, extent_y, halves, 2, block_len)
        lower = paired[:, :, :, 0]
        upper = paired[:, :, :, 1]
        kept = jnp.where(parity == 1, upper, lower)
        handed = jnp.where(parity == 1, lower, upper)
        partner = from_partner(handed, "gx", level)
        nearer = jnp.where(parity == 0, kept, partner)
        farther = jnp.where(parity == 0, partner, kept)
        current = nearer + (1.0 - nearer[3:4]) * farther
    picture = current.reshape(4, extent_y, block_len)
    return (fresh, picture)


def solution(mesh):
    placed = (P("gx", "gy", None, None),)
    return jax.shard_map(
        body,
        mesh=mesh,
        in_specs=placed,
        out_specs=(P("gx", "gy", None, None), P(None, "gy", "gx")),
        check_vma=False,
    )
```

```python
import jax
import jax.numpy as jnp
import numpy as np
from jax import lax
from jax.sharding import PartitionSpec as P
from jax.experimental import pallas as pl
from jax.experimental.pallas import tpu as pltpu

cohesion = -6.0
optical = 2.0


def extended(cells, sides, width):
    for axis, dim in sides:
        count = lax.axis_size(axis)
        head = lax.slice_in_dim(cells, 0, width, axis=dim)
        tail = lax.slice_in_dim(cells, cells.shape[dim] - width, cells.shape[dim], axis=dim)
        cells = jnp.concatenate(
            [
                lax.ppermute(tail, axis, [(i, (i + 1) % count) for i in range(count)]),
                cells,
                lax.ppermute(head, axis, [((i + 1) % count, i) for i in range(count)]),
            ],
            axis=dim,
        )
    return cells


def from_partner(x, axis, distance):
    return lax.ppermute(x, axis, [(i, i ^ 1 << distance) for i in range(lax.axis_size(axis))])


def lattice_tables():
    velocities = np.array(
        [
            [0, 0, 0],
            [1, 0, 0],
            [-1, 0, 0],
            [0, 1, 0],
            [0, -1, 0],
            [0, 0, 1],
            [0, 0, -1],
            [1, 1, 0],
            [-1, -1, 0],
            [1, -1, 0],
            [-1, 1, 0],
            [1, 0, 1],
            [-1, 0, -1],
            [1, 0, -1],
            [-1, 0, 1],
            [0, 1, 1],
            [0, -1, -1],
            [0, 1, -1],
            [0, -1, 1],
        ]
    )
    weights = np.array([1.0 / 3.0] + [1.0 / 18.0] * 6 + [1.0 / 36.0] * 12)
    along_x = velocities[:, 0] * 1.0
    along_y = velocities[:, 1] * 1.0
    along_z = velocities[:, 2] * 1.0
    squared = along_x * along_x + along_y * along_y + along_z * along_z
    moment_rows = [
        np.ones(19),
        19.0 * squared - 30.0,
        (21.0 * squared * squared - 53.0 * squared + 24.0) / 2.0,
        along_x,
        (5.0 * squared - 9.0) * along_x,
        along_y,
        (5.0 * squared - 9.0) * along_y,
        along_z,
        (5.0 * squared - 9.0) * along_z,
        3.0 * along_x * along_x - squared,
        (3.0 * squared - 5.0) * (3.0 * along_x * along_x - squared),
        along_y * along_y - along_z * along_z,
        (3.0 * squared - 5.0) * (along_y * along_y - along_z * along_z),
        along_x * along_y,
        along_y * along_z,
        along_x * along_z,
        (along_y * along_y - along_z * along_z) * along_x,
        (along_z * along_z - along_x * along_x) * along_y,
        (along_x * along_x - along_y * along_y) * along_z,
    ]
    moments = np.stack(moment_rows)
    inverse = moments.T / np.sum(moments * moments, axis=1)
    relax_rates = np.array(
        [
            0.0,
            1.19,
            1.4,
            0.0,
            1.2,
            0.0,
            1.2,
            0.0,
            1.2,
            1.0,
            1.4,
            1.0,
            1.4,
            1.0,
            1.0,
            1.0,
            1.98,
            1.98,
            1.98,
        ]
    )
    relaxing = inverse @ (relax_rates[:, None] * moments)
    forcing_map = inverse @ ((1.0 - 0.5 * relax_rates)[:, None] * moments)
    return (velocities, weights, relaxing, forcing_map)


def collide(populations, density, forcing, velocities, weights, relaxing, forcing_map):
    lattice = jnp.asarray(velocities, dtype=jnp.float32)
    spread = jnp.asarray(weights, dtype=jnp.float32)[None, None, :, None]
    relax_table = jnp.asarray(relaxing, dtype=jnp.float32)
    source_table = jnp.asarray(forcing_map, dtype=jnp.float32)
    momentum = jnp.einsum("qd,xyqz->dxyz", lattice, populations, precision=lax.Precision.HIGHEST)
    drift = (momentum + 0.5 * forcing) / density[None]
    along = jnp.einsum("qd,dxyz->xyqz", lattice, drift, precision=lax.Precision.HIGHEST)
    pushed = jnp.einsum("qd,dxyz->xyqz", lattice, forcing, precision=lax.Precision.HIGHEST)
    speed_squared = jnp.sum(drift * drift, axis=0)[:, :, None, :]
    work_done = jnp.sum(drift * forcing, axis=0)[:, :, None, :]
    balance = (
        spread
        * density[:, :, None, :]
        * (1.0 + 3.0 * along + 4.5 * along * along - 1.5 * speed_squared)
    )
    guo_term = spread * (3.0 * (pushed - work_done) + 9.0 * along * pushed)
    relaxed = jnp.einsum(
        "pq,xyqz->xypz", relax_table, populations - balance, precision=lax.Precision.HIGHEST
    )
    sourced = jnp.einsum("pq,xyqz->xypz", source_table, guo_term, precision=lax.Precision.HIGHEST)
    return populations - relaxed + sourced


def attraction(padded, offset, extent_x, extent_y, velocities, weights):
    centre = padded[offset : offset + extent_x, offset : offset + extent_y]
    totals = [jnp.zeros_like(centre), jnp.zeros_like(centre), jnp.zeros_like(centre)]
    for q in range(1, 19):
        steps = [int(v) for v in velocities[q]]
        start_x = offset + steps[0]
        start_y = offset + steps[1]
        neighbour = padded[start_x : start_x + extent_x, start_y : start_y + extent_y]
        neighbour = jnp.roll(neighbour, -steps[2], axis=2)
        for d in range(3):
            if steps[d] != 0:
                totals[d] = totals[d] + weights[q] * steps[d] * neighbour
    return jnp.stack([-cohesion * centre * totals[d] for d in range(3)])


def palette(density):
    reds = density / (1.0 + density)
    greens = jnp.exp(-density)
    blues = 0.5 * (1.0 + jnp.tanh(2.0 * (density - 1.0)))
    return (reds, greens, blues)


def shift_ring(x, axis, step):
    count = lax.axis_size(axis)
    return lax.ppermute(x, axis, [(i, (i - step) % count) for i in range(count)])


def collide_major(f, rho, force, velocities, weights, relaxing, forcing_map):
    lattice = velocities.astype(np.float32)
    extra = (1,) * rho.ndim
    cx = jnp.asarray(lattice[:, 0]).reshape((19,) + extra)
    cy = jnp.asarray(lattice[:, 1]).reshape((19,) + extra)
    cz = jnp.asarray(lattice[:, 2]).reshape((19,) + extra)
    spread = jnp.asarray(weights.astype(np.float32)).reshape((19,) + extra)
    momentum = [
        sum(f[q] * float(velocities[q][d]) for q in range(19) if velocities[q][d] != 0)
        for d in range(3)
    ]
    drift = [(momentum[d] + 0.5 * force[d]) / rho for d in range(3)]
    along = cx * drift[0] + cy * drift[1] + cz * drift[2]
    pushed = cx * force[0] + cy * force[1] + cz * force[2]
    speed_squared = drift[0] * drift[0] + drift[1] * drift[1] + drift[2] * drift[2]
    work_done = drift[0] * force[0] + drift[1] * force[1] + drift[2] * force[2]
    balance = spread * rho * (1.0 + 3.0 * along + 4.5 * along * along - 1.5 * speed_squared)
    guo_term = spread * (3.0 * (pushed - work_done) + 9.0 * along * pushed)
    relax_table = jnp.asarray(relaxing, dtype=jnp.float32)
    source_table = jnp.asarray(forcing_map, dtype=jnp.float32)
    table = jnp.concatenate([relax_table, -source_table], axis=1)
    stacked = jnp.concatenate([f - balance, guo_term], axis=0)
    return f - jnp.einsum("pq,q...->p...", table, stacked, precision=lax.Precision.HIGH)


def stream_and_render(collided, velocities, extent_x, extent_y, length_x):
    near_y, band, far_y = collided
    depth_z = band.shape[3]
    edge = near_y.shape[2]
    steps = [[int(v) for v in velocities[q]] for q in range(19)]

    def kernel(near_ref, band_ref, far_ref, o_ref, pic_ref, c_ref):
        def gather(q, carry):
            c_ref[q, :, 0:edge] = near_ref[q]
            c_ref[q, :, edge : edge + extent_y - 2] = band_ref[q]
            c_ref[q, :, edge + extent_y - 2 :] = far_ref[q]
            return carry

        lax.fori_loop(0, 19, gather, 0)
        for q in range(19):
            cx, cy, cz = steps[q]

            def move(x, carry):
                v = c_ref[q, x + 1 - cx, pl.ds(1 - cy, extent_y), :]
                if cz != 0:
                    v = pltpu.roll(v, shift=cz % depth_z, axis=1)
                o_ref[q, x] = v
                return carry

            lax.fori_loop(0, extent_x, move, 0, unroll=True)

        def render(x, carry):
            depth, red, green, blue = carry
            fresh_density = o_ref[0, x]
            for q in range(1, 19):
                fresh_density = fresh_density + o_ref[q, x]
            extinction = optical * fresh_density / length_x
            weight = jnp.exp(-depth) * (1.0 - jnp.exp(-extinction))
            red = red + weight * (fresh_density / (1.0 + fresh_density))
            green = green + weight * jnp.exp(-fresh_density)
            blue = blue + weight * (0.5 * (1.0 + jnp.tanh(2.0 * (fresh_density - 1.0))))
            return (depth + extinction, red, green, blue)

        zero = jnp.zeros((extent_y, depth_z), jnp.float32)
        depth, red, green, blue = lax.fori_loop(0, extent_x, render, (zero, zero, zero, zero), unroll=True)
        pic_ref[0] = red
        pic_ref[1] = green
        pic_ref[2] = blue
        pic_ref[3] = 1.0 - jnp.exp(-depth)

    return pl.pallas_call(
        kernel,
        out_shape=(
            jax.ShapeDtypeStruct((19, extent_x, extent_y, depth_z), jnp.float32),
            jax.ShapeDtypeStruct((4, extent_y, depth_z), jnp.float32),
        ),
        in_specs=[pl.BlockSpec(memory_space=pltpu.VMEM)] * 3,
        out_specs=(pl.BlockSpec(memory_space=pltpu.VMEM), pl.BlockSpec(memory_space=pltpu.VMEM)),
        scratch_shapes=[pltpu.VMEM((19, extent_x + 2, extent_y + 2, depth_z), jnp.float32)],
    )(near_y, band, far_y)


def collide_region(cells, pot, tables, force_only=False):
    velocities, weights, relaxing, forcing_map = tables
    nx, ny = cells.shape[1], cells.shape[2]
    centre = pot[1 : 1 + nx, 1 : 1 + ny]
    totals = [jnp.zeros_like(centre), jnp.zeros_like(centre), jnp.zeros_like(centre)]
    for q in range(1, 19):
        steps = [int(v) for v in velocities[q]]
        neighbour = pot[1 + steps[0] : 1 + steps[0] + nx, 1 + steps[1] : 1 + steps[1] + ny]
        neighbour = jnp.roll(neighbour, -steps[2], axis=2)
        for d in range(3):
            if steps[d] != 0:
                totals[d] = totals[d] + weights[q] * steps[d] * neighbour
    force = [-cohesion * centre * totals[d] for d in range(3)]
    if force_only:
        return force
    rho = jnp.sum(cells, axis=0)
    return collide_major(cells, rho, force, velocities, weights, relaxing, forcing_map)


def body(populations):
    velocities, weights, relaxing, forcing_map = lattice_tables()
    extent_x = populations.shape[0]
    extent_y = populations.shape[1]
    f = jnp.transpose(populations, (2, 0, 1, 3))
    potential = 1.0 - jnp.exp(-jnp.sum(f, axis=0))
    to_next = jnp.concatenate([f[:, extent_x - 1], potential[extent_x - 1 : extent_x], potential[extent_x - 2 : extent_x - 1]])
    to_prev = jnp.concatenate([f[:, 0], potential[0:1], potential[1:2]])
    from_prev = shift_ring(to_next, "gx", -1)
    from_next = shift_ring(to_prev, "gx", 1)
    fx = jnp.concatenate([from_prev[None, :19].transpose(1, 0, 2, 3), f, from_next[None, :19].transpose(1, 0, 2, 3)], axis=1)
    px = jnp.concatenate([from_prev[20:21], from_prev[19:20], potential, from_next[19:20], from_next[20:21]], axis=0)
    zero_x = jnp.zeros((19, 1, fx.shape[3]), f.dtype)

    def y_message(row_pop, row_near, row_far):
        pops = jnp.concatenate([zero_x, fx[:, :, row_pop], zero_x], axis=1)
        return jnp.concatenate([pops, px[None, :, row_near], px[None, :, row_far]], axis=0)

    from_below = shift_ring(y_message(extent_y - 1, extent_y - 1, extent_y - 2), "gy", -1)
    from_above = shift_ring(y_message(0, 0, 1), "gy", 1)
    fxy = jnp.concatenate(
        [from_below[:19, 1:-1, None], fx, from_above[:19, 1:-1, None]], axis=2
    )
    pxy = jnp.concatenate(
        [from_below[20][:, None], from_below[19][:, None], px, from_above[19][:, None], from_above[20][:, None]],
        axis=1,
    )
    tables = (velocities, weights, relaxing, forcing_map)
    inner = collide_region(f[:, 1 : extent_x - 1, 1 : extent_y - 1], potential, tables)
    near_x = collide_region(fx[:, 0:2, 1 : extent_y - 1], px[0:4], tables)
    far_x = collide_region(fx[:, extent_x : extent_x + 2, 1 : extent_y - 1], px[extent_x : extent_x + 4], tables)
    band = jnp.concatenate([near_x, inner, far_x], axis=1)
    low_cells = fxy[:, :, 0:2]
    high_cells = fxy[:, :, extent_y : extent_y + 2]
    low_force = collide_region(low_cells, pxy[:, 0:4], tables, force_only=True)
    high_force = collide_region(high_cells, pxy[:, extent_y : extent_y + 4], tables, force_only=True)
    strips = jnp.concatenate([low_cells, high_cells], axis=1)
    strip_force = [jnp.concatenate([low_force[d], high_force[d]], axis=0) for d in range(3)]
    both = collide_major(strips, jnp.sum(strips, axis=0), strip_force, velocities, weights, relaxing, forcing_map)
    near_y = both[:, : extent_x + 2]
    far_y = both[:, extent_x + 2 :]
    collided = (near_y, band, far_y)
    groups = lax.axis_size("gx")
    length_x = extent_x * groups
    fresh_major, layered = stream_and_render(collided, velocities, extent_x, extent_y, length_x)
    fresh = jnp.transpose(fresh_major, (1, 2, 0, 3))
    depth_z = layered.shape[2]
    block_len = depth_z // groups
    blocked = layered.reshape(4, extent_y, groups, block_len)
    position = lax.axis_index("gx")
    current = blocked
    for level in range(groups.bit_length() - 1):
        parity = position // (1 << level) % 2
        halves = current.shape[2] // 2
        paired = current.reshape(4, extent_y, halves, 2, block_len)
        lower = paired[:, :, :, 0]
        upper = paired[:, :, :, 1]
        kept = jnp.where(parity == 1, upper, lower)
        handed = jnp.where(parity == 1, lower, upper)
        partner = from_partner(handed, "gx", level)
        nearer = jnp.where(parity == 0, kept, partner)
        farther = jnp.where(parity == 0, partner, kept)
        current = nearer + (1.0 - nearer[3:4]) * farther
    picture = current.reshape(4, extent_y, block_len)
    return (fresh, picture)


def solution(mesh):
    placed = (P("gx", "gy", None, None),)
    return jax.shard_map(
        body,
        mesh=mesh,
        in_specs=placed,
        out_specs=(P("gx", "gy", None, None), P(None, "gy", "gx")),
        check_vma=False,
    )
```

```python
import jax
import jax.numpy as jnp
import numpy as np
from jax import lax
from jax.sharding import PartitionSpec as P
from jax.experimental import pallas as pl
from jax.experimental.pallas import tpu as pltpu

cohesion = -6.0
optical = 2.0


def extended(cells, sides, width):
    for axis, dim in sides:
        count = lax.axis_size(axis)
        head = lax.slice_in_dim(cells, 0, width, axis=dim)
        tail = lax.slice_in_dim(cells, cells.shape[dim] - width, cells.shape[dim], axis=dim)
        cells = jnp.concatenate(
            [
                lax.ppermute(tail, axis, [(i, (i + 1) % count) for i in range(count)]),
                cells,
                lax.ppermute(head, axis, [((i + 1) % count, i) for i in range(count)]),
            ],
            axis=dim,
        )
    return cells


def from_partner(x, axis, distance):
    return lax.ppermute(x, axis, [(i, i ^ 1 << distance) for i in range(lax.axis_size(axis))])


def lattice_tables():
    velocities = np.array(
        [
            [0, 0, 0],
            [1, 0, 0],
            [-1, 0, 0],
            [0, 1, 0],
            [0, -1, 0],
            [0, 0, 1],
            [0, 0, -1],
            [1, 1, 0],
            [-1, -1, 0],
            [1, -1, 0],
            [-1, 1, 0],
            [1, 0, 1],
            [-1, 0, -1],
            [1, 0, -1],
            [-1, 0, 1],
            [0, 1, 1],
            [0, -1, -1],
            [0, 1, -1],
            [0, -1, 1],
        ]
    )
    weights = np.array([1.0 / 3.0] + [1.0 / 18.0] * 6 + [1.0 / 36.0] * 12)
    along_x = velocities[:, 0] * 1.0
    along_y = velocities[:, 1] * 1.0
    along_z = velocities[:, 2] * 1.0
    squared = along_x * along_x + along_y * along_y + along_z * along_z
    moment_rows = [
        np.ones(19),
        19.0 * squared - 30.0,
        (21.0 * squared * squared - 53.0 * squared + 24.0) / 2.0,
        along_x,
        (5.0 * squared - 9.0) * along_x,
        along_y,
        (5.0 * squared - 9.0) * along_y,
        along_z,
        (5.0 * squared - 9.0) * along_z,
        3.0 * along_x * along_x - squared,
        (3.0 * squared - 5.0) * (3.0 * along_x * along_x - squared),
        along_y * along_y - along_z * along_z,
        (3.0 * squared - 5.0) * (along_y * along_y - along_z * along_z),
        along_x * along_y,
        along_y * along_z,
        along_x * along_z,
        (along_y * along_y - along_z * along_z) * along_x,
        (along_z * along_z - along_x * along_x) * along_y,
        (along_x * along_x - along_y * along_y) * along_z,
    ]
    moments = np.stack(moment_rows)
    inverse = moments.T / np.sum(moments * moments, axis=1)
    relax_rates = np.array(
        [
            0.0,
            1.19,
            1.4,
            0.0,
            1.2,
            0.0,
            1.2,
            0.0,
            1.2,
            1.0,
            1.4,
            1.0,
            1.4,
            1.0,
            1.0,
            1.0,
            1.98,
            1.98,
            1.98,
        ]
    )
    relaxing = inverse @ (relax_rates[:, None] * moments)
    forcing_map = inverse @ ((1.0 - 0.5 * relax_rates)[:, None] * moments)
    return (velocities, weights, relaxing, forcing_map)


def collide(populations, density, forcing, velocities, weights, relaxing, forcing_map):
    lattice = jnp.asarray(velocities, dtype=jnp.float32)
    spread = jnp.asarray(weights, dtype=jnp.float32)[None, None, :, None]
    relax_table = jnp.asarray(relaxing, dtype=jnp.float32)
    source_table = jnp.asarray(forcing_map, dtype=jnp.float32)
    momentum = jnp.einsum("qd,xyqz->dxyz", lattice, populations, precision=lax.Precision.HIGHEST)
    drift = (momentum + 0.5 * forcing) / density[None]
    along = jnp.einsum("qd,dxyz->xyqz", lattice, drift, precision=lax.Precision.HIGHEST)
    pushed = jnp.einsum("qd,dxyz->xyqz", lattice, forcing, precision=lax.Precision.HIGHEST)
    speed_squared = jnp.sum(drift * drift, axis=0)[:, :, None, :]
    work_done = jnp.sum(drift * forcing, axis=0)[:, :, None, :]
    balance = (
        spread
        * density[:, :, None, :]
        * (1.0 + 3.0 * along + 4.5 * along * along - 1.5 * speed_squared)
    )
    guo_term = spread * (3.0 * (pushed - work_done) + 9.0 * along * pushed)
    relaxed = jnp.einsum(
        "pq,xyqz->xypz", relax_table, populations - balance, precision=lax.Precision.HIGHEST
    )
    sourced = jnp.einsum("pq,xyqz->xypz", source_table, guo_term, precision=lax.Precision.HIGHEST)
    return populations - relaxed + sourced


def attraction(padded, offset, extent_x, extent_y, velocities, weights):
    centre = padded[offset : offset + extent_x, offset : offset + extent_y]
    totals = [jnp.zeros_like(centre), jnp.zeros_like(centre), jnp.zeros_like(centre)]
    for q in range(1, 19):
        steps = [int(v) for v in velocities[q]]
        start_x = offset + steps[0]
        start_y = offset + steps[1]
        neighbour = padded[start_x : start_x + extent_x, start_y : start_y + extent_y]
        neighbour = jnp.roll(neighbour, -steps[2], axis=2)
        for d in range(3):
            if steps[d] != 0:
                totals[d] = totals[d] + weights[q] * steps[d] * neighbour
    return jnp.stack([-cohesion * centre * totals[d] for d in range(3)])


def palette(density):
    reds = density / (1.0 + density)
    greens = jnp.exp(-density)
    blues = 0.5 * (1.0 + jnp.tanh(2.0 * (density - 1.0)))
    return (reds, greens, blues)


def shift_ring(x, axis, step):
    count = lax.axis_size(axis)
    return lax.ppermute(x, axis, [(i, (i - step) % count) for i in range(count)])


def collide_major(f, rho, force, velocities, weights, relaxing, forcing_map):
    lattice = velocities.astype(np.float32)
    extra = (1,) * rho.ndim
    cx = jnp.asarray(lattice[:, 0]).reshape((19,) + extra)
    cy = jnp.asarray(lattice[:, 1]).reshape((19,) + extra)
    cz = jnp.asarray(lattice[:, 2]).reshape((19,) + extra)
    spread = jnp.asarray(weights.astype(np.float32)).reshape((19,) + extra)
    momentum = [
        sum(f[q] * float(velocities[q][d]) for q in range(19) if velocities[q][d] != 0)
        for d in range(3)
    ]
    drift = [(momentum[d] + 0.5 * force[d]) / rho for d in range(3)]
    along = cx * drift[0] + cy * drift[1] + cz * drift[2]
    pushed = cx * force[0] + cy * force[1] + cz * force[2]
    speed_squared = drift[0] * drift[0] + drift[1] * drift[1] + drift[2] * drift[2]
    work_done = drift[0] * force[0] + drift[1] * force[1] + drift[2] * force[2]
    balance = spread * rho * (1.0 + 3.0 * along + 4.5 * along * along - 1.5 * speed_squared)
    guo_term = spread * (3.0 * (pushed - work_done) + 9.0 * along * pushed)
    relax_table = jnp.asarray(relaxing, dtype=jnp.float32)
    source_table = jnp.asarray(forcing_map, dtype=jnp.float32)
    table = jnp.concatenate([relax_table, -source_table], axis=1)
    stacked = jnp.concatenate([f - balance, guo_term], axis=0)
    return f - jnp.einsum("pq,q...->p...", table, stacked, precision=lax.Precision.HIGH)


def stream_and_render(collided, velocities, extent_x, extent_y, length_x):
    near_y, band, far_y = collided
    depth_z = band.shape[3]
    edge = near_y.shape[2]
    steps = [[int(v) for v in velocities[q]] for q in range(19)]

    pieces = ((0, 0, edge), (1, edge, extent_y - 2), (2, edge + extent_y - 2, edge))

    def kernel(near_ref, band_ref, far_ref, o_ref, pic_ref):
        refs = (near_ref, band_ref, far_ref)
        for q in range(19):
            cx, cy, cz = steps[q]
            first = 1 - cy

            def move(x, carry):
                for which, start, count in pieces:
                    lo = max(first, start)
                    hi = min(first + extent_y, start + count)
                    if hi <= lo:
                        continue
                    v = refs[which][q, x + 1 - cx, lo - start : hi - start, :]
                    if cz != 0:
                        v = pltpu.roll(v, shift=cz % depth_z, axis=1)
                    o_ref[q, x, lo - first : hi - first, :] = v
                return carry

            lax.fori_loop(0, extent_x, move, 0, unroll=True)

        def render(x, carry):
            depth, red, green, blue = carry
            fresh_density = o_ref[0, x]
            for q in range(1, 19):
                fresh_density = fresh_density + o_ref[q, x]
            extinction = optical * fresh_density / length_x
            weight = jnp.exp(-depth) * (1.0 - jnp.exp(-extinction))
            red = red + weight * (fresh_density / (1.0 + fresh_density))
            green = green + weight * jnp.exp(-fresh_density)
            blue = blue + weight * (0.5 * (1.0 + jnp.tanh(2.0 * (fresh_density - 1.0))))
            return (depth + extinction, red, green, blue)

        zero = jnp.zeros((extent_y, depth_z), jnp.float32)
        depth, red, green, blue = lax.fori_loop(0, extent_x, render, (zero, zero, zero, zero), unroll=True)
        pic_ref[0] = red
        pic_ref[1] = green
        pic_ref[2] = blue
        pic_ref[3] = 1.0 - jnp.exp(-depth)

    return pl.pallas_call(
        kernel,
        out_shape=(
            jax.ShapeDtypeStruct((19, extent_x, extent_y, depth_z), jnp.float32),
            jax.ShapeDtypeStruct((4, extent_y, depth_z), jnp.float32),
        ),
        in_specs=[pl.BlockSpec(memory_space=pltpu.VMEM)] * 3,
        out_specs=(pl.BlockSpec(memory_space=pltpu.VMEM), pl.BlockSpec(memory_space=pltpu.VMEM)),
    )(near_y, band, far_y)


def collide_region(cells, pot, tables):
    velocities, weights, relaxing, forcing_map = tables
    nx, ny = cells.shape[1], cells.shape[2]
    centre = pot[1 : 1 + nx, 1 : 1 + ny]
    totals = [jnp.zeros_like(centre), jnp.zeros_like(centre), jnp.zeros_like(centre)]
    for q in range(1, 19):
        steps = [int(v) for v in velocities[q]]
        neighbour = pot[1 + steps[0] : 1 + steps[0] + nx, 1 + steps[1] : 1 + steps[1] + ny]
        neighbour = jnp.roll(neighbour, -steps[2], axis=2)
        for d in range(3):
            if steps[d] != 0:
                totals[d] = totals[d] + weights[q] * steps[d] * neighbour
    force = [-cohesion * centre * totals[d] for d in range(3)]
    rho = jnp.sum(cells, axis=0)
    return collide_major(cells, rho, force, velocities, weights, relaxing, forcing_map)


def body(populations):
    velocities, weights, relaxing, forcing_map = lattice_tables()
    extent_x = populations.shape[0]
    extent_y = populations.shape[1]
    f = jnp.transpose(populations, (2, 0, 1, 3))
    potential = 1.0 - jnp.exp(-jnp.sum(f, axis=0))
    to_next = jnp.concatenate([f[:, extent_x - 1], potential[extent_x - 1 : extent_x], potential[extent_x - 2 : extent_x - 1]])
    to_prev = jnp.concatenate([f[:, 0], potential[0:1], potential[1:2]])
    from_prev = shift_ring(to_next, "gx", -1)
    from_next = shift_ring(to_prev, "gx", 1)
    fx = jnp.concatenate([from_prev[None, :19].transpose(1, 0, 2, 3), f, from_next[None, :19].transpose(1, 0, 2, 3)], axis=1)
    px = jnp.concatenate([from_prev[20:21], from_prev[19:20], potential, from_next[19:20], from_next[20:21]], axis=0)
    zero_x = jnp.zeros((19, 1, fx.shape[3]), f.dtype)

    def y_message(row_pop, row_near, row_far):
        pops = jnp.concatenate([zero_x, fx[:, :, row_pop], zero_x], axis=1)
        return jnp.concatenate([pops, px[None, :, row_near], px[None, :, row_far]], axis=0)

    from_below = shift_ring(y_message(extent_y - 1, extent_y - 1, extent_y - 2), "gy", -1)
    from_above = shift_ring(y_message(0, 0, 1), "gy", 1)
    fxy = jnp.concatenate(
        [from_below[:19, 1:-1, None], fx, from_above[:19, 1:-1, None]], axis=2
    )
    pxy = jnp.concatenate(
        [from_below[20][:, None], from_below[19][:, None], px, from_above[19][:, None], from_above[20][:, None]],
        axis=1,
    )
    tables = (velocities, weights, relaxing, forcing_map)
    inner = collide_region(f[:, 1 : extent_x - 1, 1 : extent_y - 1], potential, tables)
    near_x = collide_region(fx[:, 0:2, 1 : extent_y - 1], px[0:4], tables)
    far_x = collide_region(fx[:, extent_x : extent_x + 2, 1 : extent_y - 1], px[extent_x : extent_x + 4], tables)
    band = jnp.concatenate([near_x, inner, far_x], axis=1)
    near_y = collide_region(fxy[:, :, 0:2], pxy[:, 0:4], tables)
    far_y = collide_region(fxy[:, :, extent_y : extent_y + 2], pxy[:, extent_y : extent_y + 4], tables)
    collided = (near_y, band, far_y)
    groups = lax.axis_size("gx")
    length_x = extent_x * groups
    fresh_major, layered = stream_and_render(collided, velocities, extent_x, extent_y, length_x)
    fresh = jnp.transpose(fresh_major, (1, 2, 0, 3))
    depth_z = layered.shape[2]
    block_len = depth_z // groups
    blocked = layered.reshape(4, extent_y, groups, block_len)
    position = lax.axis_index("gx")
    current = blocked
    for level in range(groups.bit_length() - 1):
        parity = position // (1 << level) % 2
        halves = current.shape[2] // 2
        paired = current.reshape(4, extent_y, halves, 2, block_len)
        lower = paired[:, :, :, 0]
        upper = paired[:, :, :, 1]
        kept = jnp.where(parity == 1, upper, lower)
        handed = jnp.where(parity == 1, lower, upper)
        partner = from_partner(handed, "gx", level)
        nearer = jnp.where(parity == 0, kept, partner)
        farther = jnp.where(parity == 0, partner, kept)
        current = nearer + (1.0 - nearer[3:4]) * farther
    picture = current.reshape(4, extent_y, block_len)
    return (fresh, picture)


def solution(mesh):
    placed = (P("gx", "gy", None, None),)
    return jax.shard_map(
        body,
        mesh=mesh,
        in_specs=placed,
        out_specs=(P("gx", "gy", None, None), P(None, "gy", "gx")),
        check_vma=False,
    )
```

```python
import jax
import jax.numpy as jnp
import numpy as np
from jax import lax
from jax.sharding import PartitionSpec as P
from jax.experimental import pallas as pl
from jax.experimental.pallas import tpu as pltpu

cohesion = -6.0
optical = 2.0


def extended(cells, sides, width):
    for axis, dim in sides:
        count = lax.axis_size(axis)
        head = lax.slice_in_dim(cells, 0, width, axis=dim)
        tail = lax.slice_in_dim(cells, cells.shape[dim] - width, cells.shape[dim], axis=dim)
        cells = jnp.concatenate(
            [
                lax.ppermute(tail, axis, [(i, (i + 1) % count) for i in range(count)]),
                cells,
                lax.ppermute(head, axis, [((i + 1) % count, i) for i in range(count)]),
            ],
            axis=dim,
        )
    return cells


def from_partner(x, axis, distance):
    return lax.ppermute(x, axis, [(i, i ^ 1 << distance) for i in range(lax.axis_size(axis))])


def lattice_tables():
    velocities = np.array(
        [
            [0, 0, 0],
            [1, 0, 0],
            [-1, 0, 0],
            [0, 1, 0],
            [0, -1, 0],
            [0, 0, 1],
            [0, 0, -1],
            [1, 1, 0],
            [-1, -1, 0],
            [1, -1, 0],
            [-1, 1, 0],
            [1, 0, 1],
            [-1, 0, -1],
            [1, 0, -1],
            [-1, 0, 1],
            [0, 1, 1],
            [0, -1, -1],
            [0, 1, -1],
            [0, -1, 1],
        ]
    )
    weights = np.array([1.0 / 3.0] + [1.0 / 18.0] * 6 + [1.0 / 36.0] * 12)
    along_x = velocities[:, 0] * 1.0
    along_y = velocities[:, 1] * 1.0
    along_z = velocities[:, 2] * 1.0
    squared = along_x * along_x + along_y * along_y + along_z * along_z
    moment_rows = [
        np.ones(19),
        19.0 * squared - 30.0,
        (21.0 * squared * squared - 53.0 * squared + 24.0) / 2.0,
        along_x,
        (5.0 * squared - 9.0) * along_x,
        along_y,
        (5.0 * squared - 9.0) * along_y,
        along_z,
        (5.0 * squared - 9.0) * along_z,
        3.0 * along_x * along_x - squared,
        (3.0 * squared - 5.0) * (3.0 * along_x * along_x - squared),
        along_y * along_y - along_z * along_z,
        (3.0 * squared - 5.0) * (along_y * along_y - along_z * along_z),
        along_x * along_y,
        along_y * along_z,
        along_x * along_z,
        (along_y * along_y - along_z * along_z) * along_x,
        (along_z * along_z - along_x * along_x) * along_y,
        (along_x * along_x - along_y * along_y) * along_z,
    ]
    moments = np.stack(moment_rows)
    inverse = moments.T / np.sum(moments * moments, axis=1)
    relax_rates = np.array(
        [
            0.0,
            1.19,
            1.4,
            0.0,
            1.2,
            0.0,
            1.2,
            0.0,
            1.2,
            1.0,
            1.4,
            1.0,
            1.4,
            1.0,
            1.0,
            1.0,
            1.98,
            1.98,
            1.98,
        ]
    )
    relaxing = inverse @ (relax_rates[:, None] * moments)
    forcing_map = inverse @ ((1.0 - 0.5 * relax_rates)[:, None] * moments)
    return (velocities, weights, relaxing, forcing_map)


def collide(populations, density, forcing, velocities, weights, relaxing, forcing_map):
    lattice = jnp.asarray(velocities, dtype=jnp.float32)
    spread = jnp.asarray(weights, dtype=jnp.float32)[None, None, :, None]
    relax_table = jnp.asarray(relaxing, dtype=jnp.float32)
    source_table = jnp.asarray(forcing_map, dtype=jnp.float32)
    momentum = jnp.einsum("qd,xyqz->dxyz", lattice, populations, precision=lax.Precision.HIGHEST)
    drift = (momentum + 0.5 * forcing) / density[None]
    along = jnp.einsum("qd,dxyz->xyqz", lattice, drift, precision=lax.Precision.HIGHEST)
    pushed = jnp.einsum("qd,dxyz->xyqz", lattice, forcing, precision=lax.Precision.HIGHEST)
    speed_squared = jnp.sum(drift * drift, axis=0)[:, :, None, :]
    work_done = jnp.sum(drift * forcing, axis=0)[:, :, None, :]
    balance = (
        spread
        * density[:, :, None, :]
        * (1.0 + 3.0 * along + 4.5 * along * along - 1.5 * speed_squared)
    )
    guo_term = spread * (3.0 * (pushed - work_done) + 9.0 * along * pushed)
    relaxed = jnp.einsum(
        "pq,xyqz->xypz", relax_table, populations - balance, precision=lax.Precision.HIGHEST
    )
    sourced = jnp.einsum("pq,xyqz->xypz", source_table, guo_term, precision=lax.Precision.HIGHEST)
    return populations - relaxed + sourced


def attraction(padded, offset, extent_x, extent_y, velocities, weights):
    centre = padded[offset : offset + extent_x, offset : offset + extent_y]
    totals = [jnp.zeros_like(centre), jnp.zeros_like(centre), jnp.zeros_like(centre)]
    for q in range(1, 19):
        steps = [int(v) for v in velocities[q]]
        start_x = offset + steps[0]
        start_y = offset + steps[1]
        neighbour = padded[start_x : start_x + extent_x, start_y : start_y + extent_y]
        neighbour = jnp.roll(neighbour, -steps[2], axis=2)
        for d in range(3):
            if steps[d] != 0:
                totals[d] = totals[d] + weights[q] * steps[d] * neighbour
    return jnp.stack([-cohesion * centre * totals[d] for d in range(3)])


def palette(density):
    reds = density / (1.0 + density)
    greens = jnp.exp(-density)
    blues = 0.5 * (1.0 + jnp.tanh(2.0 * (density - 1.0)))
    return (reds, greens, blues)


def shift_ring(x, axis, step):
    count = lax.axis_size(axis)
    return lax.ppermute(x, axis, [(i, (i - step) % count) for i in range(count)])


def collide_major(f, rho, force, velocities, weights, relaxing, forcing_map):
    lattice = velocities.astype(np.float32)
    extra = (1,) * rho.ndim
    cx = jnp.asarray(lattice[:, 0]).reshape((19,) + extra)
    cy = jnp.asarray(lattice[:, 1]).reshape((19,) + extra)
    cz = jnp.asarray(lattice[:, 2]).reshape((19,) + extra)
    spread = jnp.asarray(weights.astype(np.float32)).reshape((19,) + extra)
    momentum = [
        sum(f[q] * float(velocities[q][d]) for q in range(19) if velocities[q][d] != 0)
        for d in range(3)
    ]
    drift = [(momentum[d] + 0.5 * force[d]) / rho for d in range(3)]
    along = cx * drift[0] + cy * drift[1] + cz * drift[2]
    pushed = cx * force[0] + cy * force[1] + cz * force[2]
    speed_squared = drift[0] * drift[0] + drift[1] * drift[1] + drift[2] * drift[2]
    work_done = drift[0] * force[0] + drift[1] * force[1] + drift[2] * force[2]
    balance = spread * rho * (1.0 + 3.0 * along + 4.5 * along * along - 1.5 * speed_squared)
    guo_term = spread * (3.0 * (pushed - work_done) + 9.0 * along * pushed)
    relax_table = jnp.asarray(relaxing, dtype=jnp.float32)
    source_table = jnp.asarray(forcing_map, dtype=jnp.float32)
    table = jnp.concatenate([relax_table, -source_table], axis=1)
    stacked = jnp.concatenate([f - balance, guo_term], axis=0)
    return f - jnp.einsum("pq,q...->p...", table, stacked, precision=lax.Precision.HIGH)


def stream_and_render(collided, velocities, extent_x, extent_y, length_x):
    near_y, band, far_y = collided
    depth_z = band.shape[3]
    edge = near_y.shape[2]
    steps = [[int(v) for v in velocities[q]] for q in range(19)]

    pieces = ((0, 0, edge), (1, edge, extent_y - 2), (2, edge + extent_y - 2, edge))

    def kernel(near_ref, band_ref, far_ref, o_ref, pic_ref):
        refs = (near_ref, band_ref, far_ref)
        for q in range(19):
            cx, cy, cz = steps[q]
            first = 1 - cy

            def move(x, carry):
                for which, start, count in pieces:
                    lo = max(first, start)
                    hi = min(first + extent_y, start + count)
                    if hi <= lo:
                        continue
                    v = refs[which][q, x + 1 - cx, lo - start : hi - start, :]
                    if cz != 0:
                        v = pltpu.roll(v, shift=cz % depth_z, axis=1)
                    o_ref[q, x, lo - first : hi - first, :] = v
                return carry

            lax.fori_loop(0, extent_x, move, 0, unroll=True)

        def render(x, carry):
            depth, red, green, blue = carry
            fresh_density = o_ref[0, x]
            for q in range(1, 19):
                fresh_density = fresh_density + o_ref[q, x]
            extinction = optical * fresh_density / length_x
            weight = jnp.exp(-depth) * (1.0 - jnp.exp(-extinction))
            red = red + weight * (fresh_density / (1.0 + fresh_density))
            green = green + weight * jnp.exp(-fresh_density)
            blue = blue + weight * (0.5 * (1.0 + jnp.tanh(2.0 * (fresh_density - 1.0))))
            return (depth + extinction, red, green, blue)

        zero = jnp.zeros((extent_y, depth_z), jnp.float32)
        depth, red, green, blue = lax.fori_loop(0, extent_x, render, (zero, zero, zero, zero), unroll=True)
        pic_ref[0] = red
        pic_ref[1] = green
        pic_ref[2] = blue
        pic_ref[3] = 1.0 - jnp.exp(-depth)

    return pl.pallas_call(
        kernel,
        out_shape=(
            jax.ShapeDtypeStruct((19, extent_x, extent_y, depth_z), jnp.float32),
            jax.ShapeDtypeStruct((4, extent_y, depth_z), jnp.float32),
        ),
        in_specs=[pl.BlockSpec(memory_space=pltpu.VMEM)] * 3,
        out_specs=(pl.BlockSpec(memory_space=pltpu.VMEM), pl.BlockSpec(memory_space=pltpu.VMEM)),
    )(near_y, band, far_y)


def collide_region(cells, pot, tables):
    velocities, weights, relaxing, forcing_map = tables
    nx, ny = cells.shape[1], cells.shape[2]
    centre = pot[1 : 1 + nx, 1 : 1 + ny]
    totals = [jnp.zeros_like(centre), jnp.zeros_like(centre), jnp.zeros_like(centre)]
    for q in range(1, 19):
        steps = [int(v) for v in velocities[q]]
        neighbour = pot[1 + steps[0] : 1 + steps[0] + nx, 1 + steps[1] : 1 + steps[1] + ny]
        neighbour = jnp.roll(neighbour, -steps[2], axis=2)
        for d in range(3):
            if steps[d] != 0:
                totals[d] = totals[d] + weights[q] * steps[d] * neighbour
    force = [-cohesion * centre * totals[d] for d in range(3)]
    rho = jnp.sum(cells, axis=0)
    return collide_major(cells, rho, force, velocities, weights, relaxing, forcing_map)


def body(populations):
    velocities, weights, relaxing, forcing_map = lattice_tables()
    extent_x = populations.shape[0]
    extent_y = populations.shape[1]
    f = jnp.transpose(populations, (2, 0, 1, 3))
    potential = 1.0 - jnp.exp(-jnp.sum(f, axis=0))
    to_next = jnp.concatenate([f[:, extent_x - 1], potential[extent_x - 1 : extent_x], potential[extent_x - 2 : extent_x - 1]])
    to_prev = jnp.concatenate([f[:, 0], potential[0:1], potential[1:2]])
    from_prev = shift_ring(to_next, "gx", -1)
    from_next = shift_ring(to_prev, "gx", 1)
    fx = jnp.concatenate([from_prev[None, :19].transpose(1, 0, 2, 3), f, from_next[None, :19].transpose(1, 0, 2, 3)], axis=1)
    px = jnp.concatenate([from_prev[20:21], from_prev[19:20], potential, from_next[19:20], from_next[20:21]], axis=0)
    zero_x = jnp.zeros((19, 1, fx.shape[3]), f.dtype)

    def y_message(row_pop, row_near, row_far):
        pops = jnp.concatenate([zero_x, fx[:, :, row_pop], zero_x], axis=1)
        return jnp.concatenate([pops, px[None, :, row_near], px[None, :, row_far]], axis=0)

    from_below = shift_ring(y_message(extent_y - 1, extent_y - 1, extent_y - 2), "gy", -1)
    from_above = shift_ring(y_message(0, 0, 1), "gy", 1)
    fxy = jnp.concatenate(
        [from_below[:19, 1:-1, None], fx, from_above[:19, 1:-1, None]], axis=2
    )
    pxy = jnp.concatenate(
        [from_below[20][:, None], from_below[19][:, None], px, from_above[19][:, None], from_above[20][:, None]],
        axis=1,
    )
    tables = (velocities, weights, relaxing, forcing_map)
    inner = collide_region(f[:, 1 : extent_x - 1, 1 : extent_y - 1], potential, tables)
    near_x = collide_region(fx[:, 0:2, 1 : extent_y - 1], px[0:4], tables)
    far_x = collide_region(fx[:, extent_x : extent_x + 2, 1 : extent_y - 1], px[extent_x : extent_x + 4], tables)
    band = jnp.concatenate([near_x, inner, far_x], axis=1)
    near_y = collide_region(fxy[:, :, 0:2], pxy[:, 0:4], tables)
    far_y = collide_region(fxy[:, :, extent_y : extent_y + 2], pxy[:, extent_y : extent_y + 4], tables)
    collided = (near_y, band, far_y)
    groups = lax.axis_size("gx")
    length_x = extent_x * groups
    fresh_major, layered = stream_and_render(collided, velocities, extent_x, extent_y, length_x)
    fresh = jnp.transpose(fresh_major, (1, 2, 0, 3))
    depth_z = layered.shape[2]
    block_len = depth_z // groups
    blocked = layered.reshape(4, extent_y, groups, block_len)
    gathered = lax.all_to_all(blocked, "gx", 2, 2, tiled=True)
    current = gathered[:, :, 0]
    for source in range(1, groups):
        current = current + (1.0 - current[3:4]) * gathered[:, :, source]
    picture = current
    return (fresh, picture)


def solution(mesh):
    placed = (P("gx", "gy", None, None),)
    return jax.shard_map(
        body,
        mesh=mesh,
        in_specs=placed,
        out_specs=(P("gx", "gy", None, None), P(None, "gy", "gx")),
        check_vma=False,
    )
```
